128 devices in a mesh: req: 32 (over y, z_lo, x), exp: 4 (over z_hi, core).
Axes of the slice: x: 4, y: 4, z: 4 (z_hi: 2, z_lo: 2; z = z_hi * 2 + z_lo), core: 2. Of those that a mesh axis runs over, the one named last changes fastest.
Arguments:
- activations: bfloat16 [16384, 1536], P('req'), may hold values from -6 to 6
- attn_gain: float32 [1536], replicated, may hold values from 0.1 to 1.9
- w_query: bfloat16 [1536, 1536], P(None, 'exp'), may hold values from -0.15625 to 0.15625
- key_value_weight: bfloat16 [1536, 2, 256], replicated, may hold values from -0.15625 to 0.15625
- w_output: bfloat16 [1536, 1536], P('exp'), may hold values from -0.15625 to 0.15625
- group_prefix_cache: bfloat16 [8192, 2, 2, 128], P('req')
- lengths: int32 [64], replicated, may hold values from 64 to 448, as said below
- groups: int32 [64], replicated, may hold values from 0 to 3
- owners: int32 [32], replicated, may hold values from 0 to 31, each once
- moe_gain: float32 [1536], replicated, may hold values from 0.1 to 1.9
- w_gate: bfloat16 [32, 1536, 768], P('req', None, 'exp'), may hold values from -0.15625 to 0.15625
- w_up: bfloat16 [32, 1536, 768], P('req', None, 'exp'), may hold values from -0.15625 to 0.15625
- w_down: bfloat16 [32, 768, 1536], P('req', 'exp'), may hold values from -0.21875 to 0.21875
- picks: int32 [16384, 4], P('req'), may hold values from 0 to 31, all different within a row; in each aligned block of 512 rows (0 to 511, 512 to 1023, ...) at most 128 rows name the same one
- pick_weight: float32 [16384, 4], P('req'), may hold values from 0.05 to 0.6
Outputs:
- out: bfloat16 [16384, 1536], P('req')
The draws below stay inside these ranges and needn't reach their ends.
Inputs may be any that keep to these rules, and one draw needn't show every extreme that they name: `lengths`: entries 2r and 2r+1 sum to 512; every entry is a multiple of 64. `owners`: each value appears once. `picks`: a row names 4 different experts; in the rows of one index of req no expert is named by more than 128 rows.
All inputs are finite; a program needn't handle non-finite values.
Results may differ from the reference program's by a relative error of at most 0.0073.
Values may be sent and summed in bfloat16 or wider, within the bound.
No kernel may reach another device: no remote copies, remote signals or barrier semaphores. Data moves between devices by JAX's collectives and lax.ppermute only.
A program may use at most 128 MiB of HBM per device.

```python
import math
from functools import partial
import jax
import jax.numpy as jnp
import numpy as np
from jax import lax

MODEL_WIDTH = 1536
QUERY_HEADS = 12
KEY_VALUE_HEADS = 2
HEAD_SIZE = 128
FF = 768
TOP = 4
GROUPS = 4
REQ_DEV = 2
LMIN = 64
TOKENS_PER_SHARD = 512
PREFIX_SEGMENT = 256
EXPERTS = 32
OWNERS_G = 8
GROUP_PREFIX_LEN = 2048
ALL_PREFIX_ROWS = 8192
REQUESTS = 64
TOKENS = 16384
CAP = 128
N_REQ = 32


def draw_lengths(key, part):
    first_key, second_key, swap_key, pick_key = jax.random.split(key, 4)
    count = REQUESTS // REQ_DEV
    units = TOKENS_PER_SHARD // LMIN
    one = jax.random.randint(first_key, (count,), 1, units)
    two = jax.random.randint(second_key, (count,), 1, units)
    short = jnp.minimum(one, two)
    chosen = jax.random.randint(pick_key, (), 0, count)
    short = jnp.where(jnp.arange(count) == chosen, 1, short) * LMIN
    swap = jax.random.randint(swap_key, (count,), 0, 2)
    first = jnp.where(swap == 1, TOKENS_PER_SHARD - short, short)
    second = TOKENS_PER_SHARD - first
    return jnp.stack([first, second], axis=1).reshape(REQUESTS).astype(jnp.int32)


def draw_group_prefix_cache(key, part):
    random_key_alpha = jax.random.fold_in(key, 0)
    layer_cache = jax.random.normal(random_key_alpha, (ALL_PREFIX_ROWS, 2, KEY_VALUE_HEADS, HEAD_SIZE), jnp.float32)
    return layer_cache.astype(jnp.bfloat16)


def place_ends(array, rng, low, largest):
    longest = array.shape.index(max(array.shape))
    spots = []
    for shift in (0, 1):
        where = [jax.random.randint(jax.random.fold_in(rng, axis), (), 0, length) for axis, length in enumerate(array.shape)]
        where[longest] = (where[longest] + shift) % array.shape[longest]
        spots.append(tuple(where))
    return array.at[spots[0]].set(low).at[spots[1]].set(largest)


def level_of(key, shape, pieces, least, high):
    factor_of = 1.0
    for dim, shards_of in pieces:
        steps = jax.random.uniform(jax.random.fold_in(jax.random.fold_in(key, 6), dim), (shards_of,), jnp.float32, least / len(pieces), high / len(pieces))
        factor_of = factor_of * jnp.repeat(jnp.exp(steps), shape[dim] // shards_of).reshape((-1,) + (1,) * (len(shape) - 1 - dim))
    return factor_of


def deal_out(rng, own, number, rows, count, top, most, skew):
    sequence = jax.random.permutation(rng, count)
    packed, usual = load_shares(count, rows * top, most, skew, True), load_shares(count, rows * top, most, skew, False)
    places = jnp.arange(count)

    def named(sizes, turn):
        used = int((sizes > 0).sum())
        fixed = max(1, used // 4)
        shifted = fixed + (places - fixed + turn * (used - fixed)) % max(1, count - fixed)
        return jnp.zeros((count,), jnp.int32).at[sequence[jnp.where(places < fixed, places, shifted)]].set(jnp.asarray(sizes, jnp.int32))

    sizes = jnp.where(number % 4 == 0, named(packed, number // 4), named(usual, number - number // 4 - 1))
    mixed = jax.random.permutation(jax.random.fold_in(own, 3), count)
    source_of, taker = mixed[0:count // 2 * 2:2], mixed[1:count // 2 * 2:2]
    slack = jnp.minimum(sizes[source_of] - 1, most - sizes[taker]) // 2
    slack = jnp.where((source_of == sequence[0]) | (taker == sequence[0]) | (sizes[taker] == 0), 0, jnp.maximum(slack, 0))
    shifted = jax.random.randint(jax.random.fold_in(own, 4), (count // 2,), 0, 1 << 20) % (slack + 1)
    sizes = sizes.at[source_of].add(-shifted).at[taker].add(shifted)
    items = jnp.searchsorted(jnp.cumsum(sizes), jnp.arange(rows * top), side="right").astype(jnp.int32)
    listing = items.reshape(top, rows).T
    listing = listing[jax.random.permutation(jax.random.fold_in(own, 1), rows)]
    turn = jax.random.randint(jax.random.fold_in(own, 2), (rows, 1), 0, top)
    return jnp.take_along_axis(listing, (jnp.arange(top)[None, :] + turn) % top, axis=1)


def load_shares(number_of, total, most, skew, full):
    loads = [(1 << 20) // math.isqrt(grade ** skew) + 1 for grade in range(1, number_of + 1)]
    largest = most if full else min(most, max(-(-total // number_of), total * loads[0] // sum(loads)))
    least = 1 if total - largest >= number_of - 1 else 0
    counts, spare = [largest] + [least] * (number_of - 1), total - largest - least * (number_of - 1)
    while spare > 0:
        free = [i for i in range(1, number_of) if counts[i] < largest] or [i for i in range(1, number_of) if counts[i] < most]
        mass, left = sum([loads[i] for i in free]), spare
        for i in free:
            addition = min(most - counts[i], max(1, left * loads[i] // mass), spare)
            counts[i] = counts[i] + addition
            spare = spare - addition
    return np.array(counts)


def gaussian(key, extent, spread, limit, shards=(), kind=jnp.bfloat16):
    result = jax.random.normal(key, extent, jnp.float32) * spread
    if len(shards) > 0:
        result = level_of(key, extent, shards, -0.22, 0.18) * result
    return jnp.clip(result, min=-limit, max=limit).astype(kind)


def setup_inputs(seed: int = 0) -> dict:
    arg_keys = jax.random.split(jax.random.key(seed), 16)
    activations = gaussian(arg_keys[0], (TOKENS, MODEL_WIDTH), 1.0, 6.0, ((0, 32),))
    attn_gain = jnp.clip(1.0 + 0.18 * jax.random.normal(arg_keys[1], (MODEL_WIDTH,), jnp.float32), 0.1, 1.9)
    w_query = gaussian(arg_keys[2], (MODEL_WIDTH, QUERY_HEADS * HEAD_SIZE), MODEL_WIDTH ** -0.5, 0.15625, ((1, 4),))
    key_value_weight = gaussian(arg_keys[3], (MODEL_WIDTH, 2, KEY_VALUE_HEADS * HEAD_SIZE), MODEL_WIDTH ** -0.5, 0.15625)
    w_output = gaussian(arg_keys[4], (QUERY_HEADS * HEAD_SIZE, MODEL_WIDTH), (QUERY_HEADS * HEAD_SIZE) ** -0.5, 0.15625, ((0, 4),))
    group_prefix_cache = draw_group_prefix_cache(jax.random.fold_in(arg_keys[15], 71), 0)
    lengths = draw_lengths(jax.random.fold_in(arg_keys[15], 71), 0)
    groups = place_ends(jax.random.randint(arg_keys[7], (REQUESTS,), 0, GROUPS), jax.random.fold_in(arg_keys[7], 1), 0, GROUPS - 1).astype(jnp.int32)
    owners = jax.random.permutation(arg_keys[8], N_REQ).astype(jnp.int32)
    moe_gain = jnp.clip(1.0 + 0.18 * jax.random.normal(arg_keys[9], (MODEL_WIDTH,), jnp.float32), 0.1, 1.9)
    w_gate = gaussian(arg_keys[10], (EXPERTS, MODEL_WIDTH, FF), MODEL_WIDTH ** -0.5, 0.15625, ((0, 32), (2, 4)))
    w_up = gaussian(arg_keys[11], (EXPERTS, MODEL_WIDTH, FF), MODEL_WIDTH ** -0.5, 0.15625, ((0, 32), (2, 4)))
    w_down = gaussian(arg_keys[12], (EXPERTS, FF, MODEL_WIDTH), FF ** -0.5, 0.21875, ((0, 32), (1, 4)))
    picks_keys = jax.random.split(jax.random.fold_in(arg_keys[13], 1), TOKENS // TOKENS_PER_SHARD)
    picks_turns = jax.random.permutation(jax.random.fold_in(arg_keys[13], 3), TOKENS // TOKENS_PER_SHARD)
    picks = jax.vmap(lambda own, number: deal_out(jax.random.fold_in(arg_keys[13], 2), own, number, TOKENS_PER_SHARD, EXPERTS, TOP, CAP, 2))(picks_keys, picks_turns).reshape((TOKENS, TOP))
    pick_weight = jnp.clip(0.05 + 0.55 * jax.random.uniform(arg_keys[14], (TOKENS, TOP), jnp.float32) ** level_of(arg_keys[14], (TOKENS, TOP), ((0, 32),), -0.2, 0.2), 0.05, 0.6)
    return {"activations": activations, "attn_gain": attn_gain, "w_query": w_query, "key_value_weight": key_value_weight, "w_output": w_output, "group_prefix_cache": group_prefix_cache, "lengths": lengths, "groups": groups, "owners": owners, "moe_gain": moe_gain, "w_gate": w_gate, "w_up": w_up, "w_down": w_down, "picks": picks, "pick_weight": pick_weight}


EPS = 1e-06

def rms_scale(rows, gain):
    rows32 = rows.astype(jnp.float32)
    inverse = lax.rsqrt(lax.optimization_barrier(jnp.mean(rows32 * rows32, axis=-1, keepdims=True)) + EPS)
    return (rows32 * inverse * gain).astype(jnp.bfloat16)

def block_attention(activations, attn_gain, w_query, key_value_weight, w_output, layer_cache, lengths, groups, owners, block):
    rows = lax.dynamic_slice_in_dim(activations, block * TOKENS_PER_SHARD, TOKENS_PER_SHARD, 0)
    normalized_input = rms_scale(rows, attn_gain)
    queries_per_key_head = QUERY_HEADS // KEY_VALUE_HEADS
    query_rows = (jnp.dot(normalized_input, w_query, preferred_element_type=jnp.float32) * HEAD_SIZE ** (-0.5)).astype(jnp.bfloat16)
    query_rows = query_rows.reshape(TOKENS_PER_SHARD, KEY_VALUE_HEADS, queries_per_key_head, HEAD_SIZE).astype(jnp.float32)
    local_key_value = jnp.dot(normalized_input, key_value_weight.reshape(MODEL_WIDTH, 2 * KEY_VALUE_HEADS * HEAD_SIZE), preferred_element_type=jnp.float32).astype(jnp.bfloat16)
    local_key_value = local_key_value.reshape(TOKENS_PER_SHARD, 2, KEY_VALUE_HEADS, HEAD_SIZE).astype(jnp.float32)
    pair = lax.dynamic_slice_in_dim(lengths, block * REQ_DEV, REQ_DEV, 0)
    pair_groups = lax.dynamic_slice_in_dim(groups, block * REQ_DEV, REQ_DEV, 0)
    positions = jnp.arange(TOKENS_PER_SHARD)
    in_first = positions < pair[0]
    score_parts = []
    value_parts = []
    for which in range(2):
        prefix_segments = lax.dynamic_slice_in_dim(owners, pair_groups[which] * OWNERS_G, OWNERS_G, 0)
        group_prefix = layer_cache[prefix_segments].reshape(GROUP_PREFIX_LEN, 2, KEY_VALUE_HEADS, HEAD_SIZE).astype(jnp.float32)
        scores = jnp.einsum('tkgd,pkd->kgtp', query_rows, group_prefix[:, 0])
        mine = in_first if which == 0 else jnp.logical_not(in_first)
        score_parts.append(jnp.where(mine[None, None, :, None], scores, -jnp.inf))
        value_parts.append(group_prefix[:, 1])
    scores = jnp.einsum('tkgd,skd->kgts', query_rows, local_key_value[:, 0])
    allowed = (positions[None, :] <= positions[:, None]) & (in_first[:, None] == in_first[None, :])
    score_parts.append(jnp.where(allowed[None, None], scores, -jnp.inf))
    value_parts.append(local_key_value[:, 1])
    total_scores = jnp.concatenate(score_parts, axis=-1)
    values = jnp.concatenate(value_parts, axis=0)
    top = lax.optimization_barrier(jnp.max(total_scores, axis=-1, keepdims=True))
    expo = jnp.exp(total_scores - top)
    weights = (expo / lax.optimization_barrier(jnp.sum(expo, axis=-1, keepdims=True))).astype(jnp.bfloat16)
    weights = lax.optimization_barrier(weights).astype(jnp.float32)
    context = jnp.einsum('kgts,skd->tkgd', weights, values).astype(jnp.bfloat16)
    return jnp.dot(context.reshape(TOKENS_PER_SHARD, QUERY_HEADS * HEAD_SIZE), w_output, preferred_element_type=jnp.float32)

def reference(activations, attn_gain, w_query, key_value_weight, w_output, group_prefix_cache, lengths, groups, owners, moe_gain, w_gate, w_up, w_down, picks, pick_weight):
    layer_cache = group_prefix_cache.reshape(N_REQ, PREFIX_SEGMENT, 2, KEY_VALUE_HEADS, HEAD_SIZE)
    attend = partial(block_attention, activations, attn_gain, w_query, key_value_weight, w_output, layer_cache, lengths, groups, owners)
    attn = lax.map(attend, jnp.arange(N_REQ, dtype=jnp.int32)).reshape(TOKENS, MODEL_WIDTH)
    resid = (activations.astype(jnp.float32) + attn).astype(jnp.bfloat16)
    normed_moe = rms_scale(resid, moe_gain)
    flat = picks.reshape(N_REQ, TOKENS_PER_SHARD * TOP)
    onehot = (flat[:, :, None] == jnp.arange(EXPERTS, dtype=jnp.int32)[None, None, :]).astype(jnp.int32)
    before = jnp.cumsum(onehot, axis=1) - onehot
    slot = lax.optimization_barrier(jnp.sum(before * onehot, axis=2)).astype(jnp.int32)
    block_ids = jnp.broadcast_to(jnp.arange(N_REQ, dtype=jnp.int32)[:, None], flat.shape)
    token_ids = block_ids * TOKENS_PER_SHARD + jnp.arange(TOKENS_PER_SHARD * TOP, dtype=jnp.int32)[None, :] // TOP
    source = jnp.full((EXPERTS, N_REQ, CAP), TOKENS, jnp.int32).at[flat, block_ids, slot].set(token_ids)
    weight_table = jnp.zeros((EXPERTS, N_REQ, CAP), jnp.float32).at[flat, block_ids, slot].set(pick_weight.reshape(N_REQ, TOKENS_PER_SHARD * TOP))
    padded = jnp.concatenate([normed_moe, jnp.zeros((1, MODEL_WIDTH), jnp.bfloat16)], axis=0)

    def expert_step(acc, inputs):
        gate_w, up_w, down_w, src, wts = inputs
        index = src.reshape(-1)
        rows = padded[index]
        gate = jnp.dot(rows, gate_w, preferred_element_type=jnp.float32)
        up = jnp.dot(rows, up_w, preferred_element_type=jnp.float32)
        hidden = (jnp.maximum(gate, 0.0) * up).astype(jnp.bfloat16)
        part = jnp.dot(hidden, down_w, preferred_element_type=jnp.float32).astype(jnp.bfloat16)
        part = lax.optimization_barrier(part)
        acc = acc.at[index].add(wts.reshape(-1)[:, None] * part.astype(jnp.float32))
        return (acc, None)
    acc, _ = lax.scan(expert_step, jnp.zeros((TOKENS + 1, MODEL_WIDTH), jnp.float32), (w_gate, w_up, w_down, source, weight_table))
    return (resid.astype(jnp.float32) + acc[:TOKENS]).astype(jnp.bfloat16)
```

```python
import jax
import jax.numpy as jnp
from jax import lax
from jax.sharding import PartitionSpec as P

QUERY_HEADS = 12
KEY_VALUE_HEADS = 2
HEAD_SIZE = 128
TOP = 4
GROUPS = 4
REQ_DEV = 2
LMIN = 64


EPS = 1e-06


def rms_scale(rows, gain):
    rows32 = rows.astype(jnp.float32)
    inverse = lax.rsqrt(jnp.mean(rows32 * rows32, axis=-1, keepdims=True) + EPS)
    return (rows32 * inverse * gain).astype(jnp.bfloat16)


def prefix_for(gathered, owners, group, per_group):
    prefix_segments = lax.dynamic_slice_in_dim(owners, group * per_group, per_group, 0)
    return gathered[prefix_segments].reshape(per_group * gathered.shape[1], 2, gathered.shape[3])


def body(
    activations,
    attn_gain,
    w_query,
    key_value_weight,
    w_output,
    group_prefix_cache,
    lengths,
    groups,
    owners,
    moe_gain,
    w_gate,
    w_up,
    w_down,
    picks,
    pick_weight,
):
    req_index = lax.axis_index("req")
    expert_index = lax.axis_index("exp")
    n_req = lax.axis_size("req")
    n_exp = lax.axis_size("exp")
    tok = activations.shape[0]
    width_model = activations.shape[1]
    heads_per_shard = w_query.shape[1] // HEAD_SIZE
    key_value_head = expert_index * heads_per_shard // (QUERY_HEADS // KEY_VALUE_HEADS)

    own_piece = lax.dynamic_index_in_dim(group_prefix_cache, key_value_head, 2, keepdims=False)
    gathered = lax.all_gather(own_piece, "req", axis=0, tiled=False)
    w_output_full = lax.all_gather(w_output, "exp", axis=0, tiled=True)
    gate_full = lax.all_gather(w_gate[0], "exp", axis=1, tiled=True)
    up_full = lax.all_gather(w_up[0], "exp", axis=1, tiled=True)
    down_full = lax.all_gather(w_down[0], "exp", axis=0, tiled=True)

    normalized_input = rms_scale(activations, attn_gain)
    query_rows = (
        jnp.dot(normalized_input, w_query, preferred_element_type=jnp.float32) * HEAD_SIZE ** (-0.5)
    ).astype(jnp.bfloat16)
    query_rows = query_rows.reshape(tok, heads_per_shard, HEAD_SIZE)
    kv_weight = lax.dynamic_slice_in_dim(key_value_weight, key_value_head * HEAD_SIZE, HEAD_SIZE, 2)
    local_key_value = jnp.einsum(
        "td,dcf->tcf", normalized_input, kv_weight, preferred_element_type=jnp.float32
    ).astype(jnp.bfloat16)

    pair = lax.dynamic_slice_in_dim(lengths, req_index * REQ_DEV, REQ_DEV, 0)
    pair_groups = lax.dynamic_slice_in_dim(groups, req_index * REQ_DEV, REQ_DEV, 0)
    per_group = n_req // GROUPS
    positions = jnp.arange(tok)
    in_first = positions < pair[0]
    prefix_a = prefix_for(gathered, owners, pair_groups[0], per_group)
    prefix_b = prefix_for(gathered, owners, pair_groups[1], per_group)
    zero_q = jnp.zeros_like(query_rows)
    first3 = in_first[:, None, None]
    query_ab = jnp.concatenate(
        [jnp.where(first3, query_rows, zero_q), jnp.where(first3, zero_q, query_rows)], axis=-1
    )
    keys_ab = jnp.concatenate([prefix_a[:, 0], prefix_b[:, 0]], axis=-1)
    values_ab = jnp.concatenate([prefix_a[:, 1], prefix_b[:, 1]], axis=-1)
    pre_scores = jnp.einsum("thd,pd->htp", query_ab, keys_ab, preferred_element_type=jnp.float32)
    suf_scores = jnp.einsum(
        "thd,sd->hts", query_rows, local_key_value[:, 0], preferred_element_type=jnp.float32
    )
    allowed = (positions[None, :] <= positions[:, None]) & (in_first[:, None] == in_first[None, :])
    suf_scores = jnp.where(allowed[None], suf_scores, -jnp.inf)
    top = jnp.maximum(
        jnp.max(pre_scores, axis=-1, keepdims=True), jnp.max(suf_scores, axis=-1, keepdims=True)
    )
    pre_exp = jnp.exp(pre_scores - top)
    suf_exp = jnp.exp(suf_scores - top)
    denom = jnp.sum(pre_exp, axis=-1, keepdims=True) + jnp.sum(suf_exp, axis=-1, keepdims=True)
    pre_w = (pre_exp / denom).astype(jnp.bfloat16)
    suf_w = (suf_exp / denom).astype(jnp.bfloat16)
    pre_ctx_ab = jnp.einsum("htp,pd->thd", pre_w, values_ab, preferred_element_type=jnp.float32)
    pre_ctx = jnp.where(first3, pre_ctx_ab[..., :HEAD_SIZE], pre_ctx_ab[..., HEAD_SIZE:])
    suf_ctx = jnp.einsum(
        "hts,sd->thd", suf_w, local_key_value[:, 1], preferred_element_type=jnp.float32
    )
    context = (pre_ctx + suf_ctx).astype(jnp.bfloat16)
    context = context.reshape(tok, heads_per_shard * HEAD_SIZE)
    context_full = lax.all_gather(context, "exp", axis=1, tiled=True)
    attn = jnp.dot(context_full, w_output_full, preferred_element_type=jnp.float32)
    resid = (activations.astype(jnp.float32) + attn).astype(jnp.bfloat16)
    normed_moe = rms_scale(resid, moe_gain)

    n_experts = n_req
    cap = min(tok, 2 * tok * TOP // n_req)
    quarter = cap // n_exp
    expert_ids = jnp.arange(n_experts, dtype=jnp.int32)
    chose = jnp.any(picks[:, :, None] == expert_ids[None, None, :], axis=1).astype(jnp.bfloat16)
    earlier = (positions[None, :] < positions[:, None]).astype(jnp.bfloat16)
    before = jnp.dot(earlier, chose, preferred_element_type=jnp.float32).astype(jnp.int32)
    slot = jnp.take_along_axis(before, picks, axis=1)
    local = slot - expert_index * quarter
    keep = (local >= 0) & (local < quarter)
    target = jnp.where(keep, picks * quarter + local, -1)
    columns = jnp.arange(n_experts * quarter, dtype=jnp.int32)
    hits = target[:, :, None] == columns[None, None, :]
    dispatch = jnp.any(hits, axis=1).astype(jnp.bfloat16)
    send = jnp.einsum("tq,td->qd", dispatch, normed_moe, preferred_element_type=jnp.float32)
    send = send.astype(jnp.bfloat16).reshape(n_experts, quarter, width_model)
    received = lax.all_to_all(send, "req", split_axis=0, concat_axis=0, tiled=True)
    rows = received.reshape(-1, width_model)
    gate = jnp.dot(rows, gate_full, preferred_element_type=jnp.float32)
    up = jnp.dot(rows, up_full, preferred_element_type=jnp.float32)
    hidden = (jnp.maximum(gate, 0.0) * up).astype(jnp.bfloat16)
    part = jnp.dot(hidden, down_full, preferred_element_type=jnp.float32).astype(jnp.bfloat16)
    part = part.reshape(n_experts, quarter, width_model)
    back = lax.all_to_all(part, "req", split_axis=0, concat_axis=0, tiled=True)
    back = back.reshape(-1, width_model)
    combine = jnp.sum(jnp.where(hits, pick_weight[:, :, None], 0.0), axis=1)
    combine_hi = combine.astype(jnp.bfloat16)
    combine_lo = (combine - combine_hi.astype(jnp.float32)).astype(jnp.bfloat16)
    mix = jnp.dot(combine_hi, back, preferred_element_type=jnp.float32) + jnp.dot(
        combine_lo, back, preferred_element_type=jnp.float32
    )
    total = lax.psum(mix, "exp")
    return (resid.astype(jnp.float32) + total).astype(jnp.bfloat16)


def solution(mesh):
    return jax.shard_map(
        body,
        mesh=mesh,
        in_specs=(
            P("req", None),
            P(),
            P(None, "exp"),
            P(),
            P("exp", None),
            P("req", None, None, None),
            P(),
            P(),
            P(),
            P(),
            P("req", None, "exp"),
            P("req", None, "exp"),
            P("req", "exp", None),
            P("req", None),
            P("req", None),
        ),
        out_specs=P("req", None),
        check_vma=False,
    )
```

```python
import jax
import jax.numpy as jnp
from jax import lax
from jax.sharding import PartitionSpec as P

QUERY_HEADS = 12
KEY_VALUE_HEADS = 2
HEAD_SIZE = 128
TOP = 4
GROUPS = 4
REQ_DEV = 2
LMIN = 64


EPS = 1e-06


def rms_scale(rows, gain):
    rows32 = rows.astype(jnp.float32)
    inverse = lax.rsqrt(jnp.mean(rows32 * rows32, axis=-1, keepdims=True) + EPS)
    return (rows32 * inverse * gain).astype(jnp.bfloat16)


def prefix_for(gathered, owners, group, per_group):
    prefix_segments = lax.dynamic_slice_in_dim(owners, group * per_group, per_group, 0)
    return gathered[prefix_segments].reshape(per_group * gathered.shape[1], 2, gathered.shape[3])


def req_shift_pairs(n_req, kind, d):
    pairs = []
    for r in range(n_req):
        if kind == "x":
            dest = (r // 4) * 4 + (r % 4 + d) % 4
        elif kind == "z":
            dest = r ^ 4
        else:
            dest = (r + 8 * d) % n_req
        pairs.append((r, dest))
    return pairs


def exp_flip(x, n_exp, bit):
    return lax.ppermute(x, "exp", [(e, e ^ bit) for e in range(n_exp)])


def gather_exp(x, axis, n_exp):
    far = exp_flip(x, n_exp, 2)
    near = exp_flip(jnp.concatenate([x, far], axis=axis), n_exp, 1)
    return jnp.concatenate([x, far, near], axis=axis)


def gather_prefix_halves(mine, n_req):
    along_x = jnp.stack(
        [mine] + [lax.ppermute(mine, "req", req_shift_pairs(n_req, "x", d)) for d in (1, 2, 3)]
    )
    along_z = jnp.stack([along_x, lax.ppermute(along_x, "req", req_shift_pairs(n_req, "z", 1))])
    along_y = jnp.stack(
        [along_z] + [lax.ppermute(along_z, "req", req_shift_pairs(n_req, "y", d)) for d in (1, 2, 3)]
    )
    return along_y.reshape((n_req,) + mine.shape)


def body(
    activations,
    attn_gain,
    w_query,
    key_value_weight,
    w_output,
    group_prefix_cache,
    lengths,
    groups,
    owners,
    moe_gain,
    w_gate,
    w_up,
    w_down,
    picks,
    pick_weight,
):
    req_index = lax.axis_index("req")
    expert_index = lax.axis_index("exp")
    n_req = lax.axis_size("req")
    n_exp = lax.axis_size("exp")
    tok = activations.shape[0]
    width_model = activations.shape[1]
    heads_per_shard = w_query.shape[1] // HEAD_SIZE
    key_value_head = expert_index * heads_per_shard // (QUERY_HEADS // KEY_VALUE_HEADS)

    own_piece = lax.dynamic_index_in_dim(group_prefix_cache, key_value_head, 2, keepdims=False)
    core = expert_index % 2
    far_half = expert_index // 2
    half_rows = own_piece.shape[0] // 2
    mine = lax.dynamic_slice_in_dim(own_piece, core * half_rows, half_rows, 0)
    halves_mine = gather_prefix_halves(mine, n_req)
    halves_other = exp_flip(halves_mine, n_exp, 1)
    w_output_full = gather_exp(w_output, 0, n_exp)
    gate_full = gather_exp(w_gate[0], 1, n_exp)
    up_full = gather_exp(w_up[0], 1, n_exp)
    down_full = gather_exp(w_down[0], 0, n_exp)

    normalized_input = rms_scale(activations, attn_gain)
    query_rows = (
        jnp.dot(normalized_input, w_query, preferred_element_type=jnp.float32) * HEAD_SIZE ** (-0.5)
    ).astype(jnp.bfloat16)
    query_rows = query_rows.reshape(tok, heads_per_shard, HEAD_SIZE)
    kv_weight = lax.dynamic_slice_in_dim(key_value_weight, key_value_head * HEAD_SIZE, HEAD_SIZE, 2)
    local_key_value = jnp.einsum(
        "td,dcf->tcf", normalized_input, kv_weight, preferred_element_type=jnp.float32
    ).astype(jnp.bfloat16)

    pair = lax.dynamic_slice_in_dim(lengths, req_index * REQ_DEV, REQ_DEV, 0)
    pair_groups = lax.dynamic_slice_in_dim(groups, req_index * REQ_DEV, REQ_DEV, 0)
    per_group = n_req // GROUPS
    positions = jnp.arange(tok)
    in_first = positions < pair[0]
    my_y, my_z, my_x = req_index // 8, (req_index // 4) % 2, req_index % 4

    def prefix_of(group):
        owner = lax.dynamic_slice_in_dim(owners, group * per_group, per_group, 0)
        where = ((my_y - owner // 8) % 4) * 8 + ((my_z - (owner // 4) % 2) % 2) * 4 + (my_x - owner % 4) % 4
        part_mine = halves_mine[where]
        part_other = halves_other[where]
        rows = jnp.where(
            core == 0,
            jnp.concatenate([part_mine, part_other], axis=1),
            jnp.concatenate([part_other, part_mine], axis=1),
        )
        return rows.reshape(per_group * 2 * half_rows, 2, HEAD_SIZE)

    prefix_a = prefix_of(pair_groups[0])
    prefix_b = prefix_of(pair_groups[1])
    zero_q = jnp.zeros_like(query_rows)
    first3 = in_first[:, None, None]
    query_ab = jnp.concatenate(
        [jnp.where(first3, query_rows, zero_q), jnp.where(first3, zero_q, query_rows)], axis=-1
    )
    keys_ab = jnp.concatenate([prefix_a[:, 0], prefix_b[:, 0]], axis=-1)
    values_ab = jnp.concatenate([prefix_a[:, 1], prefix_b[:, 1]], axis=-1)
    pre_scores = jnp.einsum("thd,pd->htp", query_ab, keys_ab, preferred_element_type=jnp.float32)
    suf_scores = jnp.einsum(
        "thd,sd->hts", query_rows, local_key_value[:, 0], preferred_element_type=jnp.float32
    )
    allowed = (positions[None, :] <= positions[:, None]) & (in_first[:, None] == in_first[None, :])
    suf_scores = jnp.where(allowed[None], suf_scores, -jnp.inf)
    top = jnp.maximum(
        jnp.max(pre_scores, axis=-1, keepdims=True), jnp.max(suf_scores, axis=-1, keepdims=True)
    )
    pre_exp = jnp.exp(pre_scores - top)
    suf_exp = jnp.exp(suf_scores - top)
    denom = jnp.sum(pre_exp, axis=-1, keepdims=True) + jnp.sum(suf_exp, axis=-1, keepdims=True)
    pre_w = (pre_exp / denom).astype(jnp.bfloat16)
    suf_w = (suf_exp / denom).astype(jnp.bfloat16)
    pre_ctx_ab = jnp.einsum("htp,pd->thd", pre_w, values_ab, preferred_element_type=jnp.float32)
    pre_ctx = jnp.where(first3, pre_ctx_ab[..., :HEAD_SIZE], pre_ctx_ab[..., HEAD_SIZE:])
    suf_ctx = jnp.einsum(
        "hts,sd->thd", suf_w, local_key_value[:, 1], preferred_element_type=jnp.float32
    )
    context = (pre_ctx + suf_ctx).astype(jnp.bfloat16)
    context = context.reshape(tok, heads_per_shard * HEAD_SIZE)
    context_full = gather_exp(context, 1, n_exp)
    attn = jnp.dot(context_full, w_output_full, preferred_element_type=jnp.float32)
    resid = (activations.astype(jnp.float32) + attn).astype(jnp.bfloat16)
    normed_moe = rms_scale(resid, moe_gain)

    n_experts = n_req
    cap = min(tok, 2 * tok * TOP // n_req)
    quarter = cap // n_exp
    expert_ids = jnp.arange(n_experts, dtype=jnp.int32)
    chose = jnp.any(picks[:, :, None] == expert_ids[None, None, :], axis=1).astype(jnp.bfloat16)
    earlier = (positions[None, :] < positions[:, None]).astype(jnp.bfloat16)
    before = jnp.dot(earlier, chose, preferred_element_type=jnp.float32).astype(jnp.int32)
    slot = jnp.take_along_axis(before, picks, axis=1)
    local = slot - expert_index * quarter
    keep = (local >= 0) & (local < quarter)
    target = jnp.where(keep, picks * quarter + local, -1)
    columns = jnp.arange(n_experts * quarter, dtype=jnp.int32)
    hits = target[:, :, None] == columns[None, None, :]
    dispatch = jnp.any(hits, axis=1).astype(jnp.bfloat16)
    send = jnp.einsum("tq,td->qd", dispatch, normed_moe, preferred_element_type=jnp.float32)
    send = send.astype(jnp.bfloat16).reshape(n_experts, quarter, width_model)
    received = lax.all_to_all(send, "req", split_axis=0, concat_axis=0, tiled=True)
    rows = received.reshape(-1, width_model)
    gate = jnp.dot(rows, gate_full, preferred_element_type=jnp.float32)
    up = jnp.dot(rows, up_full, preferred_element_type=jnp.float32)
    hidden = (jnp.maximum(gate, 0.0) * up).astype(jnp.bfloat16)
    part = jnp.dot(hidden, down_full, preferred_element_type=jnp.float32).astype(jnp.bfloat16)
    part = part.reshape(n_experts, quarter, width_model)
    back = lax.all_to_all(part, "req", split_axis=0, concat_axis=0, tiled=True)
    back = back.reshape(-1, width_model)
    combine = jnp.sum(jnp.where(hits, pick_weight[:, :, None], 0.0), axis=1)
    combine_hi = combine.astype(jnp.bfloat16)
    combine_lo = (combine - combine_hi.astype(jnp.float32)).astype(jnp.bfloat16)
    mix = jnp.dot(combine_hi, back, preferred_element_type=jnp.float32) + jnp.dot(
        combine_lo, back, preferred_element_type=jnp.float32
    )
    half_tok = tok // 2
    quarter_tok = tok // 4
    keep_half = lax.dynamic_slice_in_dim(mix, core * half_tok, half_tok, 0)
    give_half = lax.dynamic_slice_in_dim(mix, (1 - core) * half_tok, half_tok, 0)
    half_sum = keep_half + exp_flip(give_half, n_exp, 1)
    keep_q = lax.dynamic_slice_in_dim(half_sum, far_half * quarter_tok, quarter_tok, 0)
    give_q = lax.dynamic_slice_in_dim(half_sum, (1 - far_half) * quarter_tok, quarter_tok, 0)
    quarter_sum = keep_q + exp_flip(give_q, n_exp, 2)
    my_rows = core * half_tok + far_half * quarter_tok
    resid_rows = lax.dynamic_slice_in_dim(resid, my_rows, quarter_tok, 0)
    out_q = (resid_rows.astype(jnp.float32) + quarter_sum).astype(jnp.bfloat16)
    other_q = exp_flip(out_q, n_exp, 2)
    out_half = jnp.where(
        far_half == 0,
        jnp.concatenate([out_q, other_q], axis=0),
        jnp.concatenate([other_q, out_q], axis=0),
    )
    other_half = exp_flip(out_half, n_exp, 1)
    return jnp.where(
        core == 0,
        jnp.concatenate([out_half, other_half], axis=0),
        jnp.concatenate([other_half, out_half], axis=0),
    )


def solution(mesh):
    return jax.shard_map(
        body,
        mesh=mesh,
        in_specs=(
            P("req", None),
            P(),
            P(None, "exp"),
            P(),
            P("exp", None),
            P("req", None, None, None),
            P(),
            P(),
            P(),
            P(),
            P("req", None, "exp"),
            P("req", None, "exp"),
            P("req", "exp", None),
            P("req", None),
            P("req", None),
        ),
        out_specs=P("req", None),
        check_vma=False,
    )
```

```python
import jax
import jax.numpy as jnp
from jax import lax
from jax.sharding import PartitionSpec as P

QUERY_HEADS = 12
KEY_VALUE_HEADS = 2
HEAD_SIZE = 128
TOP = 4
GROUPS = 4
REQ_DEV = 2
LMIN = 64


EPS = 1e-06


def rms_scale(rows, gain):
    rows32 = rows.astype(jnp.float32)
    inverse = lax.rsqrt(jnp.mean(rows32 * rows32, axis=-1, keepdims=True) + EPS)
    return (rows32 * inverse * gain).astype(jnp.bfloat16)


def prefix_for(gathered, owners, group, per_group):
    prefix_segments = lax.dynamic_slice_in_dim(owners, group * per_group, per_group, 0)
    return gathered[prefix_segments].reshape(per_group * gathered.shape[1], 2, gathered.shape[3])


def req_shift_pairs(n_req, kind, d):
    pairs = []
    for r in range(n_req):
        if kind == "x":
            dest = (r // 4) * 4 + (r % 4 + d) % 4
        elif kind == "z":
            dest = r ^ 4
        else:
            dest = (r + 8 * d) % n_req
        pairs.append((r, dest))
    return pairs


def exp_flip(x, n_exp, bit):
    return lax.ppermute(x, "exp", [(e, e ^ bit) for e in range(n_exp)])


def gather_exp(x, axis, n_exp):
    far = exp_flip(x, n_exp, 2)
    near = exp_flip(jnp.concatenate([x, far], axis=axis), n_exp, 1)
    return jnp.concatenate([x, far, near], axis=axis)


def far_relay(x, n_req, n_exp):
    def index(r, e):
        return r * n_exp + e

    first = []
    second = []
    for r in range(n_req):
        for e in range(n_exp):
            if e % 2 == 0:
                first.append((index(r, e), index(r ^ 4, e)))
                second.append((index(r, e), index(r ^ 4, e ^ 2)))
            else:
                first.append((index(r, e), index(r ^ 4, e ^ 2)))
                second.append((index(r, e), index(r ^ 4, e)))
    hop = lax.ppermute(x, ("req", "exp"), first)
    return lax.ppermute(hop, ("req", "exp"), second)


def gather_exp_relay(x, axis, n_req, n_exp):
    far = far_relay(x, n_req, n_exp)
    near = exp_flip(jnp.concatenate([x, far], axis=axis), n_exp, 1)
    return jnp.concatenate([x, far, near], axis=axis)


def gather_prefix_near(mine, n_req):
    along_x = jnp.stack(
        [mine] + [lax.ppermute(mine, "req", req_shift_pairs(n_req, "x", d)) for d in (1, 2, 3)]
    )
    return jnp.stack([along_x, lax.ppermute(along_x, "req", req_shift_pairs(n_req, "z", 1))])


def gather_prefix_halves(along_z, n_req):
    along_y = jnp.stack(
        [along_z] + [lax.ppermute(along_z, "req", req_shift_pairs(n_req, "y", d)) for d in (1, 2, 3)]
    )
    return along_y.reshape((n_req,) + along_z.shape[2:])


def body(
    activations,
    attn_gain,
    w_query,
    key_value_weight,
    w_output,
    group_prefix_cache,
    lengths,
    groups,
    owners,
    moe_gain,
    w_gate,
    w_up,
    w_down,
    picks,
    pick_weight,
):
    req_index = lax.axis_index("req")
    expert_index = lax.axis_index("exp")
    n_req = lax.axis_size("req")
    n_exp = lax.axis_size("exp")
    tok = activations.shape[0]
    width_model = activations.shape[1]
    heads_per_shard = w_query.shape[1] // HEAD_SIZE
    key_value_head = expert_index * heads_per_shard // (QUERY_HEADS // KEY_VALUE_HEADS)

    own_piece = lax.dynamic_index_in_dim(group_prefix_cache, key_value_head, 2, keepdims=False)
    core = expert_index % 2
    far_half = expert_index // 2
    half_rows = own_piece.shape[0] // 2
    mine = lax.dynamic_slice_in_dim(own_piece, core * half_rows, half_rows, 0)
    along_z = gather_prefix_near(mine, n_req)
    ff_shard = w_gate.shape[2]
    packed = jnp.concatenate([w_gate[0].T, w_up[0].T, w_down[0]], axis=0)
    w_output_late, packed_late, along_z = lax.optimization_barrier((w_output, packed, along_z))
    halves_mine = gather_prefix_halves(along_z, n_req)
    halves_other = exp_flip(halves_mine, n_exp, 1)
    w_output_full = gather_exp_relay(w_output_late, 0, n_req, n_exp)
    packed_full = gather_exp_relay(packed_late.reshape(1, 3 * ff_shard, -1), 0, n_req, n_exp)
    gate_full = packed_full[:, :ff_shard].reshape(-1, packed.shape[1]).T
    up_full = packed_full[:, ff_shard : 2 * ff_shard].reshape(-1, packed.shape[1]).T
    down_full = packed_full[:, 2 * ff_shard :].reshape(-1, packed.shape[1])

    normalized_input = rms_scale(activations, attn_gain)
    query_rows = (
        jnp.dot(normalized_input, w_query, preferred_element_type=jnp.float32) * HEAD_SIZE ** (-0.5)
    ).astype(jnp.bfloat16)
    query_rows = query_rows.reshape(tok, heads_per_shard, HEAD_SIZE)
    kv_weight = lax.dynamic_slice_in_dim(key_value_weight, key_value_head * HEAD_SIZE, HEAD_SIZE, 2)
    local_key_value = jnp.einsum(
        "td,dcf->tcf", normalized_input, kv_weight, preferred_element_type=jnp.float32
    ).astype(jnp.bfloat16)

    pair = lax.dynamic_slice_in_dim(lengths, req_index * REQ_DEV, REQ_DEV, 0)
    pair_groups = lax.dynamic_slice_in_dim(groups, req_index * REQ_DEV, REQ_DEV, 0)
    per_group = n_req // GROUPS
    positions = jnp.arange(tok)
    in_first = positions < pair[0]
    my_y, my_z, my_x = req_index // 8, (req_index // 4) % 2, req_index % 4

    def prefix_of(group):
        owner = lax.dynamic_slice_in_dim(owners, group * per_group, per_group, 0)
        where = ((my_y - owner // 8) % 4) * 8 + ((my_z - (owner // 4) % 2) % 2) * 4 + (my_x - owner % 4) % 4
        part_mine = halves_mine[where]
        part_other = halves_other[where]
        rows = jnp.where(
            core == 0,
            jnp.concatenate([part_mine, part_other], axis=1),
            jnp.concatenate([part_other, part_mine], axis=1),
        )
        return rows.reshape(per_group * 2 * half_rows, 2, HEAD_SIZE)

    prefix_a = prefix_of(pair_groups[0])
    prefix_b = prefix_of(pair_groups[1])
    zero_q = jnp.zeros_like(query_rows)
    first3 = in_first[:, None, None]
    query_ab = jnp.concatenate(
        [jnp.where(first3, query_rows, zero_q), jnp.where(first3, zero_q, query_rows)], axis=-1
    )
    keys_ab = jnp.concatenate([prefix_a[:, 0], prefix_b[:, 0]], axis=-1)
    values_ab = jnp.concatenate([prefix_a[:, 1], prefix_b[:, 1]], axis=-1)
    pre_scores = jnp.einsum("thd,pd->htp", query_ab, keys_ab, preferred_element_type=jnp.float32)
    suf_scores = jnp.einsum(
        "thd,sd->hts", query_rows, local_key_value[:, 0], preferred_element_type=jnp.float32
    )
    allowed = (positions[None, :] <= positions[:, None]) & (in_first[:, None] == in_first[None, :])
    suf_scores = jnp.where(allowed[None], suf_scores, -jnp.inf)
    top = jnp.maximum(
        jnp.max(pre_scores, axis=-1, keepdims=True), jnp.max(suf_scores, axis=-1, keepdims=True)
    )
    pre_exp = jnp.exp(pre_scores - top)
    suf_exp = jnp.exp(suf_scores - top)
    denom = jnp.sum(pre_exp, axis=-1, keepdims=True) + jnp.sum(suf_exp, axis=-1, keepdims=True)
    pre_w = (pre_exp / denom).astype(jnp.bfloat16)
    suf_w = (suf_exp / denom).astype(jnp.bfloat16)
    pre_ctx_ab = jnp.einsum("htp,pd->thd", pre_w, values_ab, preferred_element_type=jnp.float32)
    pre_ctx = jnp.where(first3, pre_ctx_ab[..., :HEAD_SIZE], pre_ctx_ab[..., HEAD_SIZE:])
    suf_ctx = jnp.einsum(
        "hts,sd->thd", suf_w, local_key_value[:, 1], preferred_element_type=jnp.float32
    )
    context = (pre_ctx + suf_ctx).astype(jnp.bfloat16)
    context = context.reshape(tok, heads_per_shard * HEAD_SIZE)
    context_full = gather_exp(context, 1, n_exp)
    attn = jnp.dot(context_full, w_output_full, preferred_element_type=jnp.float32)
    resid = (activations.astype(jnp.float32) + attn).astype(jnp.bfloat16)
    normed_moe = rms_scale(resid, moe_gain)

    n_experts = n_req
    cap = min(tok, 2 * tok * TOP // n_req)
    quarter = cap // n_exp
    expert_ids = jnp.arange(n_experts, dtype=jnp.int32)
    chose = jnp.any(picks[:, :, None] == expert_ids[None, None, :], axis=1).astype(jnp.bfloat16)
    earlier = (positions[None, :] < positions[:, None]).astype(jnp.bfloat16)
    before = jnp.dot(earlier, chose, preferred_element_type=jnp.float32).astype(jnp.int32)
    pick_hot = picks[:, :, None] == expert_ids[None, None, :]
    slot = jnp.sum(jnp.where(pick_hot, before[:, None, :], 0), axis=2)
    local = slot - expert_index * quarter
    keep = (local >= 0) & (local < quarter)
    target = jnp.where(keep, picks * quarter + local, -1)
    columns = jnp.arange(n_experts * quarter, dtype=jnp.int32)
    hits = target[:, :, None] == columns[None, None, :]
    dispatch = jnp.any(hits, axis=1).astype(jnp.bfloat16)
    send = jnp.einsum("tq,td->qd", dispatch, normed_moe, preferred_element_type=jnp.float32)
    send = send.astype(jnp.bfloat16).reshape(n_experts, quarter, width_model)
    received = lax.all_to_all(send, "req", split_axis=0, concat_axis=0, tiled=True)
    rows = received.reshape(-1, width_model)
    gate = jnp.dot(rows, gate_full, preferred_element_type=jnp.float32)
    up = jnp.dot(rows, up_full, preferred_element_type=jnp.float32)
    hidden = (jnp.maximum(gate, 0.0) * up).astype(jnp.bfloat16)
    part = jnp.dot(hidden, down_full, preferred_element_type=jnp.float32).astype(jnp.bfloat16)
    part = part.reshape(n_experts, quarter, width_model)
    back = lax.all_to_all(part, "req", split_axis=0, concat_axis=0, tiled=True)
    back = back.reshape(-1, width_model)
    combine = jnp.sum(jnp.where(hits, pick_weight[:, :, None], 0.0), axis=1)
    combine_hi = combine.astype(jnp.bfloat16)
    combine_lo = (combine - combine_hi.astype(jnp.float32)).astype(jnp.bfloat16)
    mix = jnp.dot(combine_hi, back, preferred_element_type=jnp.float32) + jnp.dot(
        combine_lo, back, preferred_element_type=jnp.float32
    )
    half_tok = tok // 2
    quarter_tok = tok // 4
    keep_half = lax.dynamic_slice_in_dim(mix, core * half_tok, half_tok, 0)
    give_half = lax.dynamic_slice_in_dim(mix, (1 - core) * half_tok, half_tok, 0)
    half_sum = keep_half + exp_flip(give_half, n_exp, 1)
    keep_q = lax.dynamic_slice_in_dim(half_sum, far_half * quarter_tok, quarter_tok, 0)
    give_q = lax.dynamic_slice_in_dim(half_sum, (1 - far_half) * quarter_tok, quarter_tok, 0)
    quarter_sum = keep_q + exp_flip(give_q, n_exp, 2)
    my_rows = core * half_tok + far_half * quarter_tok
    resid_rows = lax.dynamic_slice_in_dim(resid, my_rows, quarter_tok, 0)
    out_q = (resid_rows.astype(jnp.float32) + quarter_sum).astype(jnp.bfloat16)
    other_q = exp_flip(out_q, n_exp, 2)
    out_half = jnp.where(
        far_half == 0,
        jnp.concatenate([out_q, other_q], axis=0),
        jnp.concatenate([other_q, out_q], axis=0),
    )
    other_half = exp_flip(out_half, n_exp, 1)
    return jnp.where(
        core == 0,
        jnp.concatenate([out_half, other_half], axis=0),
        jnp.concatenate([other_half, out_half], axis=0),
    )


def solution(mesh):
    return jax.shard_map(
        body,
        mesh=mesh,
        in_specs=(
            P("req", None),
            P(),
            P(None, "exp"),
            P(),
            P("exp", None),
            P("req", None, None, None),
            P(),
            P(),
            P(),
            P(),
            P("req", None, "exp"),
            P("req", None, "exp"),
            P("req", "exp", None),
            P("req", None),
            P("req", None),
        ),
        out_specs=P("req", None),
        check_vma=False,
    )
```

```python
import jax
import jax.numpy as jnp
from jax import lax
from jax.sharding import PartitionSpec as P

QUERY_HEADS = 12
KEY_VALUE_HEADS = 2
HEAD_SIZE = 128
TOP = 4
GROUPS = 4
REQ_DEV = 2
LMIN = 64


EPS = 1e-06


def rms_scale(rows, gain):
    rows32 = rows.astype(jnp.float32)
    inverse = lax.rsqrt(jnp.mean(rows32 * rows32, axis=-1, keepdims=True) + EPS)
    return (rows32 * inverse * gain).astype(jnp.bfloat16)


def prefix_for(gathered, owners, group, per_group):
    prefix_segments = lax.dynamic_slice_in_dim(owners, group * per_group, per_group, 0)
    return gathered[prefix_segments].reshape(per_group * gathered.shape[1], 2, gathered.shape[3])


def req_shift_pairs(n_req, kind, d):
    pairs = []
    for r in range(n_req):
        if kind == "x":
            dest = (r // 4) * 4 + (r % 4 + d) % 4
        elif kind == "z":
            dest = r ^ 4
        else:
            dest = (r + 8 * d) % n_req
        pairs.append((r, dest))
    return pairs


def exp_flip(x, n_exp, bit):
    return lax.ppermute(x, "exp", [(e, e ^ bit) for e in range(n_exp)])


def gather_exp(x, axis, n_exp):
    far = exp_flip(x, n_exp, 2)
    near = exp_flip(jnp.concatenate([x, far], axis=axis), n_exp, 1)
    return jnp.concatenate([x, far, near], axis=axis)


def far_relay(x, n_req, n_exp):
    def index(r, e):
        return r * n_exp + e

    first = []
    second = []
    for r in range(n_req):
        for e in range(n_exp):
            if e % 2 == 0:
                first.append((index(r, e), index(r ^ 4, e)))
                second.append((index(r, e), index(r ^ 4, e ^ 2)))
            else:
                first.append((index(r, e), index(r ^ 4, e ^ 2)))
                second.append((index(r, e), index(r ^ 4, e)))
    hop = lax.ppermute(x, ("req", "exp"), first)
    return lax.ppermute(hop, ("req", "exp"), second)


def gather_exp_relay(x, axis, n_req, n_exp):
    far = far_relay(x, n_req, n_exp)
    near = exp_flip(jnp.concatenate([x, far], axis=axis), n_exp, 1)
    return jnp.concatenate([x, far, near], axis=axis)


def gather_prefix_near(mine, n_req):
    along_x = jnp.stack(
        [mine] + [lax.ppermute(mine, "req", req_shift_pairs(n_req, "x", d)) for d in (1, 2, 3)]
    )
    return jnp.stack([along_x, lax.ppermute(along_x, "req", req_shift_pairs(n_req, "z", 1))])


def gather_prefix_halves(along_z, n_req):
    along_y = jnp.stack(
        [along_z] + [lax.ppermute(along_z, "req", req_shift_pairs(n_req, "y", d)) for d in (1, 2, 3)]
    )
    return along_y.reshape((n_req,) + along_z.shape[2:])


def body(
    activations,
    attn_gain,
    w_query,
    key_value_weight,
    w_output,
    group_prefix_cache,
    lengths,
    groups,
    owners,
    moe_gain,
    w_gate,
    w_up,
    w_down,
    picks,
    pick_weight,
):
    req_index = lax.axis_index("req")
    expert_index = lax.axis_index("exp")
    n_req = lax.axis_size("req")
    n_exp = lax.axis_size("exp")
    tok = activations.shape[0]
    width_model = activations.shape[1]
    heads_per_shard = w_query.shape[1] // HEAD_SIZE
    key_value_head = expert_index * heads_per_shard // (QUERY_HEADS // KEY_VALUE_HEADS)

    own_piece = lax.dynamic_index_in_dim(group_prefix_cache, key_value_head, 2, keepdims=False)
    core = expert_index % 2
    far_half = expert_index // 2
    half_rows = own_piece.shape[0] // 2
    mine = lax.dynamic_slice_in_dim(own_piece, core * half_rows, half_rows, 0)
    along_z = gather_prefix_near(mine, n_req)
    ff_shard = w_gate.shape[2]
    packed = jnp.concatenate([w_gate[0].T, w_up[0].T, w_down[0]], axis=0)
    w_output_late, packed_late, along_z = lax.optimization_barrier((w_output, packed, along_z))
    halves_mine = gather_prefix_halves(along_z, n_req)
    halves_other = exp_flip(halves_mine, n_exp, 1)
    w_output_full = gather_exp_relay(w_output_late, 0, n_req, n_exp)
    packed_full = gather_exp_relay(packed_late.reshape(1, 3 * ff_shard, -1), 0, n_req, n_exp)
    gate_full = packed_full[:, :ff_shard].reshape(-1, packed.shape[1]).T
    up_full = packed_full[:, ff_shard : 2 * ff_shard].reshape(-1, packed.shape[1]).T
    down_full = packed_full[:, 2 * ff_shard :].reshape(-1, packed.shape[1])

    normalized_input = rms_scale(activations, attn_gain)
    query_rows = (
        jnp.dot(normalized_input, w_query, preferred_element_type=jnp.float32) * HEAD_SIZE ** (-0.5)
    ).astype(jnp.bfloat16)
    query_rows = query_rows.reshape(tok, heads_per_shard, HEAD_SIZE)
    kv_weight = lax.dynamic_slice_in_dim(key_value_weight, key_value_head * HEAD_SIZE, HEAD_SIZE, 2)
    local_key_value = jnp.einsum(
        "td,dcf->tcf", normalized_input, kv_weight, preferred_element_type=jnp.float32
    ).astype(jnp.bfloat16)

    pair = lax.dynamic_slice_in_dim(lengths, req_index * REQ_DEV, REQ_DEV, 0)
    pair_groups = lax.dynamic_slice_in_dim(groups, req_index * REQ_DEV, REQ_DEV, 0)
    per_group = n_req // GROUPS
    positions = jnp.arange(tok)
    in_first = positions < pair[0]
    my_y, my_z, my_x = req_index // 8, (req_index // 4) % 2, req_index % 4

    def prefix_of(group):
        owner = lax.dynamic_slice_in_dim(owners, group * per_group, per_group, 0)
        where = ((my_y - owner // 8) % 4) * 8 + ((my_z - (owner // 4) % 2) % 2) * 4 + (my_x - owner % 4) % 4
        part_mine = halves_mine[where]
        part_other = halves_other[where]
        rows = jnp.where(
            core == 0,
            jnp.concatenate([part_mine, part_other], axis=1),
            jnp.concatenate([part_other, part_mine], axis=1),
        )
        return rows.reshape(per_group * 2 * half_rows, 2, HEAD_SIZE)

    prefix_a = prefix_of(pair_groups[0])
    prefix_b = prefix_of(pair_groups[1])
    zero_q = jnp.zeros_like(query_rows)
    first3 = in_first[:, None, None]
    query_ab = jnp.concatenate(
        [jnp.where(first3, query_rows, zero_q), jnp.where(first3, zero_q, query_rows)], axis=-1
    )
    keys_ab = jnp.concatenate([prefix_a[:, 0], prefix_b[:, 0]], axis=-1)
    values_ab = jnp.concatenate([prefix_a[:, 1], prefix_b[:, 1]], axis=-1)
    pre_scores = jnp.einsum("thd,pd->htp", query_ab, keys_ab, preferred_element_type=jnp.float32)
    suf_scores = jnp.einsum(
        "thd,sd->hts", query_rows, local_key_value[:, 0], preferred_element_type=jnp.float32
    )
    allowed = (positions[None, :] <= positions[:, None]) & (in_first[:, None] == in_first[None, :])
    suf_scores = jnp.where(allowed[None], suf_scores, -jnp.inf)
    top = jnp.maximum(
        jnp.max(pre_scores, axis=-1, keepdims=True), jnp.max(suf_scores, axis=-1, keepdims=True)
    )
    pre_exp = jnp.exp(pre_scores - top)
    suf_exp = jnp.exp(suf_scores - top)
    denom = jnp.sum(pre_exp, axis=-1, keepdims=True) + jnp.sum(suf_exp, axis=-1, keepdims=True)
    pre_w = (pre_exp / denom).astype(jnp.bfloat16)
    suf_w = (suf_exp / denom).astype(jnp.bfloat16)
    pre_ctx_ab = jnp.einsum("htp,pd->thd", pre_w, values_ab, preferred_element_type=jnp.float32)
    pre_ctx = jnp.where(first3, pre_ctx_ab[..., :HEAD_SIZE], pre_ctx_ab[..., HEAD_SIZE:])
    suf_ctx = jnp.einsum(
        "hts,sd->thd", suf_w, local_key_value[:, 1], preferred_element_type=jnp.float32
    )
    context = (pre_ctx + suf_ctx).astype(jnp.bfloat16)
    context = context.reshape(tok, heads_per_shard * HEAD_SIZE)
    context_full = gather_exp(context, 1, n_exp)
    attn = jnp.dot(context_full, w_output_full, preferred_element_type=jnp.float32)
    resid = (activations.astype(jnp.float32) + attn).astype(jnp.bfloat16)
    normed_moe = rms_scale(resid, moe_gain)

    n_experts = n_req
    cap = min(tok, 2 * tok * TOP // n_req)
    quarter = cap // n_exp
    expert_ids = jnp.arange(n_experts, dtype=jnp.int32)
    chose = jnp.any(picks[:, :, None] == expert_ids[None, None, :], axis=1).astype(jnp.bfloat16)
    earlier = (positions[None, :] < positions[:, None]).astype(jnp.bfloat16)
    before = jnp.dot(earlier, chose, preferred_element_type=jnp.float32).astype(jnp.int32)
    pick_hot = picks[:, :, None] == expert_ids[None, None, :]
    slot = jnp.sum(jnp.where(pick_hot, before[:, None, :], 0), axis=2)
    local = slot - expert_index * quarter
    keep = (local >= 0) & (local < quarter)
    target = jnp.where(keep, picks * quarter + local, -1)
    columns = jnp.arange(n_experts * quarter, dtype=jnp.int32)
    hits = target[:, :, None] == columns[None, None, :]
    dispatch = jnp.any(hits, axis=1).astype(jnp.bfloat16)
    send = jnp.einsum("tq,td->qd", dispatch, normed_moe, preferred_element_type=jnp.float32)
    send = send.astype(jnp.bfloat16).reshape(n_experts, quarter, width_model)
    combine = jnp.sum(jnp.where(hits, pick_weight[:, :, None], 0.0), axis=1)
    combine = combine.reshape(tok, n_experts, quarter)
    chunks = 2
    step = quarter // chunks
    mix = None
    for k in range(chunks):
        received = lax.all_to_all(
            send[:, k * step : (k + 1) * step], "req", split_axis=0, concat_axis=0, tiled=True
        )
        rows = received.reshape(-1, width_model)
        gate = jnp.dot(rows, gate_full, preferred_element_type=jnp.float32)
        up = jnp.dot(rows, up_full, preferred_element_type=jnp.float32)
        hidden = (jnp.maximum(gate, 0.0) * up).astype(jnp.bfloat16)
        part = jnp.dot(hidden, down_full, preferred_element_type=jnp.float32).astype(jnp.bfloat16)
        part = part.reshape(n_experts, step, width_model)
        back = lax.all_to_all(part, "req", split_axis=0, concat_axis=0, tiled=True)
        back = back.reshape(-1, width_model)
        weights_k = combine[:, :, k * step : (k + 1) * step].reshape(tok, -1)
        weights_hi = weights_k.astype(jnp.bfloat16)
        weights_lo = (weights_k - weights_hi.astype(jnp.float32)).astype(jnp.bfloat16)
        mix_k = jnp.dot(weights_hi, back, preferred_element_type=jnp.float32) + jnp.dot(
            weights_lo, back, preferred_element_type=jnp.float32
        )
        mix = mix_k if mix is None else mix + mix_k
    half_tok = tok // 2
    quarter_tok = tok // 4
    keep_half = lax.dynamic_slice_in_dim(mix, core * half_tok, half_tok, 0)
    give_half = lax.dynamic_slice_in_dim(mix, (1 - core) * half_tok, half_tok, 0)
    half_sum = keep_half + exp_flip(give_half, n_exp, 1)
    keep_q = lax.dynamic_slice_in_dim(half_sum, far_half * quarter_tok, quarter_tok, 0)
    give_q = lax.dynamic_slice_in_dim(half_sum, (1 - far_half) * quarter_tok, quarter_tok, 0)
    quarter_sum = keep_q + far_relay(give_q, n_req, n_exp)
    my_rows = core * half_tok + far_half * quarter_tok
    resid_rows = lax.dynamic_slice_in_dim(resid, my_rows, quarter_tok, 0)
    out_q = (resid_rows.astype(jnp.float32) + quarter_sum).astype(jnp.bfloat16)
    other_q = far_relay(out_q, n_req, n_exp)
    out_half = jnp.where(
        far_half == 0,
        jnp.concatenate([out_q, other_q], axis=0),
        jnp.concatenate([other_q, out_q], axis=0),
    )
    other_half = exp_flip(out_half, n_exp, 1)
    return jnp.where(
        core == 0,
        jnp.concatenate([out_half, other_half], axis=0),
        jnp.concatenate([other_half, out_half], axis=0),
    )


def solution(mesh):
    return jax.shard_map(
        body,
        mesh=mesh,
        in_specs=(
            P("req", None),
            P(),
            P(None, "exp"),
            P(),
            P("exp", None),
            P("req", None, None, None),
            P(),
            P(),
            P(),
            P(),
            P("req", None, "exp"),
            P("req", None, "exp"),
            P("req", "exp", None),
            P("req", None),
            P("req", None),
        ),
        out_specs=P("req", None),
        check_vma=False,
    )
```

```python
import jax
import jax.numpy as jnp
from jax import lax
from jax.sharding import PartitionSpec as P

QUERY_HEADS = 12
KEY_VALUE_HEADS = 2
HEAD_SIZE = 128
TOP = 4
GROUPS = 4
REQ_DEV = 2
LMIN = 64


EPS = 1e-06


def rms_scale(rows, gain):
    rows32 = rows.astype(jnp.float32)
    inverse = lax.rsqrt(jnp.mean(rows32 * rows32, axis=-1, keepdims=True) + EPS)
    return (rows32 * inverse * gain).astype(jnp.bfloat16)


def prefix_for(gathered, owners, group, per_group):
    prefix_segments = lax.dynamic_slice_in_dim(owners, group * per_group, per_group, 0)
    return gathered[prefix_segments].reshape(per_group * gathered.shape[1], 2, gathered.shape[3])


def req_shift_pairs(n_req, kind, d):
    pairs = []
    for r in range(n_req):
        if kind == "x":
            dest = (r // 4) * 4 + (r % 4 + d) % 4
        elif kind == "z":
            dest = r ^ 4
        else:
            dest = (r + 8 * d) % n_req
        pairs.append((r, dest))
    return pairs


def exp_flip(x, n_exp, bit):
    return lax.ppermute(x, "exp", [(e, e ^ bit) for e in range(n_exp)])


def gather_exp(x, axis, n_exp):
    far = exp_flip(x, n_exp, 2)
    near = exp_flip(jnp.concatenate([x, far], axis=axis), n_exp, 1)
    return jnp.concatenate([x, far, near], axis=axis)


def far_relay(x, n_req, n_exp):
    def index(r, e):
        return r * n_exp + e

    first = []
    second = []
    for r in range(n_req):
        for e in range(n_exp):
            if e % 2 == 0:
                first.append((index(r, e), index(r ^ 4, e)))
                second.append((index(r, e), index(r ^ 4, e ^ 2)))
            else:
                first.append((index(r, e), index(r ^ 4, e ^ 2)))
                second.append((index(r, e), index(r ^ 4, e)))
    hop = lax.ppermute(x, ("req", "exp"), first)
    return lax.ppermute(hop, ("req", "exp"), second)


def gather_exp_relay(x, axis, n_req, n_exp):
    far = far_relay(x, n_req, n_exp)
    near = exp_flip(jnp.concatenate([x, far], axis=axis), n_exp, 1)
    return jnp.concatenate([x, far, near], axis=axis)


def gather_prefix_near(mine, n_req):
    along_x = jnp.stack(
        [mine] + [lax.ppermute(mine, "req", req_shift_pairs(n_req, "x", d)) for d in (1, 2, 3)]
    )
    return jnp.stack([along_x, lax.ppermute(along_x, "req", req_shift_pairs(n_req, "z", 1))])


def gather_prefix_halves(along_z, n_req):
    along_y = jnp.stack(
        [along_z] + [lax.ppermute(along_z, "req", req_shift_pairs(n_req, "y", d)) for d in (1, 2, 3)]
    )
    return along_y.reshape((n_req,) + along_z.shape[2:])


def body(
    activations,
    attn_gain,
    w_query,
    key_value_weight,
    w_output,
    group_prefix_cache,
    lengths,
    groups,
    owners,
    moe_gain,
    w_gate,
    w_up,
    w_down,
    picks,
    pick_weight,
):
    req_index = lax.axis_index("req")
    expert_index = lax.axis_index("exp")
    n_req = lax.axis_size("req")
    n_exp = lax.axis_size("exp")
    tok = activations.shape[0]
    width_model = activations.shape[1]
    heads_per_shard = w_query.shape[1] // HEAD_SIZE
    key_value_head = expert_index * heads_per_shard // (QUERY_HEADS // KEY_VALUE_HEADS)

    own_piece = lax.dynamic_index_in_dim(group_prefix_cache, key_value_head, 2, keepdims=False)
    core = expert_index % 2
    far_half = expert_index // 2
    half_rows = own_piece.shape[0] // 2
    mine = lax.dynamic_slice_in_dim(own_piece, core * half_rows, half_rows, 0)
    along_z = gather_prefix_near(mine, n_req)
    ff_shard = w_gate.shape[2]
    packed = jnp.concatenate([w_gate[0].T, w_up[0].T, w_down[0]], axis=0)
    w_output_late, along_z = lax.optimization_barrier((w_output, along_z))
    halves_mine = gather_prefix_halves(along_z, n_req)
    halves_other = exp_flip(halves_mine, n_exp, 1)
    packed_late, halves_other = lax.optimization_barrier((packed, halves_other))
    w_output_far = far_relay(w_output_late, n_req, n_exp)
    w_output_far, halves_other = lax.optimization_barrier((w_output_far, halves_other))
    w_output_near = exp_flip(jnp.concatenate([w_output, w_output_far], axis=0), n_exp, 1)
    w_output_full = jnp.concatenate([w_output, w_output_far, w_output_near], axis=0)
    packed_full = gather_exp_relay(packed_late.reshape(1, 3 * ff_shard, -1), 0, n_req, n_exp)
    gate_full = packed_full[:, :ff_shard].reshape(-1, packed.shape[1]).T
    up_full = packed_full[:, ff_shard : 2 * ff_shard].reshape(-1, packed.shape[1]).T
    down_full = packed_full[:, 2 * ff_shard :].reshape(-1, packed.shape[1])

    normalized_input = rms_scale(activations, attn_gain)
    query_rows = (
        jnp.dot(normalized_input, w_query, preferred_element_type=jnp.float32) * HEAD_SIZE ** (-0.5)
    ).astype(jnp.bfloat16)
    query_rows = query_rows.reshape(tok, heads_per_shard, HEAD_SIZE)
    kv_weight = lax.dynamic_slice_in_dim(key_value_weight, key_value_head * HEAD_SIZE, HEAD_SIZE, 2)
    local_key_value = jnp.einsum(
        "td,dcf->tcf", normalized_input, kv_weight, preferred_element_type=jnp.float32
    ).astype(jnp.bfloat16)

    pair = lax.dynamic_slice_in_dim(lengths, req_index * REQ_DEV, REQ_DEV, 0)
    pair_groups = lax.dynamic_slice_in_dim(groups, req_index * REQ_DEV, REQ_DEV, 0)
    per_group = n_req // GROUPS
    positions = jnp.arange(tok)
    in_first = positions < pair[0]
    my_y, my_z, my_x = req_index // 8, (req_index // 4) % 2, req_index % 4

    owner = jnp.stack(
        [lax.dynamic_slice_in_dim(owners, pair_groups[i] * per_group, per_group, 0) for i in range(2)]
    )
    where = ((my_y - owner // 8) % 4) * 8 + ((my_z - (owner // 4) % 2) % 2) * 4 + (my_x - owner % 4) % 4
    pick = (where[:, :, None] == jnp.arange(n_req, dtype=jnp.int32)[None, None, :]).astype(jnp.bfloat16)
    rows_mine = jnp.einsum("gjp,prcd->gcjrd", pick, halves_mine, preferred_element_type=jnp.float32)
    rows_other = jnp.einsum("gjp,prcd->gcjrd", pick, halves_other, preferred_element_type=jnp.float32)
    rows_both = jnp.stack([rows_mine, rows_other], axis=2).astype(jnp.bfloat16)
    prefix_rows = rows_both.reshape(2, 2, per_group * 2 * half_rows, HEAD_SIZE)
    zero_q = jnp.zeros_like(query_rows)
    first3 = in_first[:, None, None]
    query_ab = jnp.concatenate(
        [jnp.where(first3, query_rows, zero_q), jnp.where(first3, zero_q, query_rows)], axis=-1
    )
    keys_ab = jnp.concatenate([prefix_rows[0, 0], prefix_rows[1, 0]], axis=-1)
    values_ab = jnp.concatenate([prefix_rows[0, 1], prefix_rows[1, 1]], axis=-1)
    pre_scores = jnp.einsum("thd,pd->htp", query_ab, keys_ab, preferred_element_type=jnp.float32)
    suf_scores = jnp.einsum(
        "thd,sd->hts", query_rows, local_key_value[:, 0], preferred_element_type=jnp.float32
    )
    allowed = (positions[None, :] <= positions[:, None]) & (in_first[:, None] == in_first[None, :])
    suf_scores = jnp.where(allowed[None], suf_scores, -jnp.inf)
    top = jnp.maximum(
        jnp.max(pre_scores, axis=-1, keepdims=True), jnp.max(suf_scores, axis=-1, keepdims=True)
    )
    pre_exp = jnp.exp(pre_scores - top)
    suf_exp = jnp.exp(suf_scores - top)
    denom = jnp.sum(pre_exp, axis=-1, keepdims=True) + jnp.sum(suf_exp, axis=-1, keepdims=True)
    pre_w = (pre_exp / denom).astype(jnp.bfloat16)
    suf_w = (suf_exp / denom).astype(jnp.bfloat16)
    pre_ctx_ab = jnp.einsum("htp,pd->thd", pre_w, values_ab, preferred_element_type=jnp.float32)
    pre_ctx = jnp.where(first3, pre_ctx_ab[..., :HEAD_SIZE], pre_ctx_ab[..., HEAD_SIZE:])
    suf_ctx = jnp.einsum(
        "hts,sd->thd", suf_w, local_key_value[:, 1], preferred_element_type=jnp.float32
    )
    context = (pre_ctx + suf_ctx).astype(jnp.bfloat16)
    context = context.reshape(tok, heads_per_shard * HEAD_SIZE)
    context_full = gather_exp(context, 1, n_exp)
    attn = jnp.dot(context_full, w_output_full, preferred_element_type=jnp.float32)
    resid = (activations.astype(jnp.float32) + attn).astype(jnp.bfloat16)
    normed_moe = rms_scale(resid, moe_gain)

    n_experts = n_req
    cap = min(tok, 2 * tok * TOP // n_req)
    quarter = cap // n_exp
    expert_ids = jnp.arange(n_experts, dtype=jnp.int32)
    chose = jnp.any(picks[:, :, None] == expert_ids[None, None, :], axis=1).astype(jnp.bfloat16)
    earlier = (positions[None, :] < positions[:, None]).astype(jnp.bfloat16)
    before = jnp.dot(earlier, chose, preferred_element_type=jnp.float32).astype(jnp.int32)
    pick_hot = picks[:, :, None] == expert_ids[None, None, :]
    slot = jnp.sum(jnp.where(pick_hot, before[:, None, :], 0), axis=2)
    local = slot - expert_index * quarter
    keep = (local >= 0) & (local < quarter)
    target = jnp.where(keep, picks * quarter + local, -1)
    columns = jnp.arange(n_experts * quarter, dtype=jnp.int32)
    hits = target[:, :, None] == columns[None, None, :]
    dispatch = jnp.any(hits, axis=1).astype(jnp.bfloat16)
    send = jnp.einsum("tq,td->qd", dispatch, normed_moe, preferred_element_type=jnp.float32)
    send = send.astype(jnp.bfloat16).reshape(n_experts, quarter, width_model)
    combine = jnp.sum(jnp.where(hits, pick_weight[:, :, None], 0.0), axis=1)
    combine = combine.reshape(tok, n_experts, quarter)
    chunks = 1
    step = quarter // chunks
    mix = None
    for k in range(chunks):
        received = lax.all_to_all(
            send[:, k * step : (k + 1) * step], "req", split_axis=0, concat_axis=0, tiled=True
        )
        rows = received.reshape(-1, width_model)
        gate = jnp.dot(rows, gate_full, preferred_element_type=jnp.float32)
        up = jnp.dot(rows, up_full, preferred_element_type=jnp.float32)
        hidden = (jnp.maximum(gate, 0.0) * up).astype(jnp.bfloat16)
        part = jnp.dot(hidden, down_full, preferred_element_type=jnp.float32).astype(jnp.bfloat16)
        part = part.reshape(n_experts, step, width_model)
        back = lax.all_to_all(part, "req", split_axis=0, concat_axis=0, tiled=True)
        back = back.reshape(-1, width_model)
        weights_k = combine[:, :, k * step : (k + 1) * step].reshape(tok, -1)
        weights_hi = weights_k.astype(jnp.bfloat16)
        weights_lo = (weights_k - weights_hi.astype(jnp.float32)).astype(jnp.bfloat16)
        mix_k = jnp.dot(weights_hi, back, preferred_element_type=jnp.float32) + jnp.dot(
            weights_lo, back, preferred_element_type=jnp.float32
        )
        mix = mix_k if mix is None else mix + mix_k
    half_tok = tok // 2
    quarter_tok = tok // 4
    keep_half = lax.dynamic_slice_in_dim(mix, core * half_tok, half_tok, 0)
    give_half = lax.dynamic_slice_in_dim(mix, (1 - core) * half_tok, half_tok, 0)
    half_sum = keep_half + exp_flip(give_half, n_exp, 1)
    keep_q = lax.dynamic_slice_in_dim(half_sum, far_half * quarter_tok, quarter_tok, 0)
    give_q = lax.dynamic_slice_in_dim(half_sum, (1 - far_half) * quarter_tok, quarter_tok, 0)
    quarter_sum = keep_q + exp_flip(give_q, n_exp, 2)
    my_rows = core * half_tok + far_half * quarter_tok
    resid_rows = lax.dynamic_slice_in_dim(resid, my_rows, quarter_tok, 0)
    out_q = (resid_rows.astype(jnp.float32) + quarter_sum).astype(jnp.bfloat16)
    other_q = exp_flip(out_q, n_exp, 2)
    out_half = jnp.where(
        far_half == 0,
        jnp.concatenate([out_q, other_q], axis=0),
        jnp.concatenate([other_q, out_q], axis=0),
    )
    other_half = exp_flip(out_half, n_exp, 1)
    return jnp.where(
        core == 0,
        jnp.concatenate([out_half, other_half], axis=0),
        jnp.concatenate([other_half, out_half], axis=0),
    )


def solution(mesh):
    return jax.shard_map(
        body,
        mesh=mesh,
        in_specs=(
            P("req", None),
            P(),
            P(None, "exp"),
            P(),
            P("exp", None),
            P("req", None, None, None),
            P(),
            P(),
            P(),
            P(),
            P("req", None, "exp"),
            P("req", None, "exp"),
            P("req", "exp", None),
            P("req", None),
            P("req", None),
        ),
        out_specs=P("req", None),
        check_vma=False,
    )
```

```python
import jax
import jax.numpy as jnp
from jax import lax
from jax.sharding import PartitionSpec as P

QUERY_HEADS = 12
KEY_VALUE_HEADS = 2
HEAD_SIZE = 128
TOP = 4
GROUPS = 4
REQ_DEV = 2
LMIN = 64


EPS = 1e-06


def rms_scale(rows, gain):
    rows32 = rows.astype(jnp.float32)
    inverse = lax.rsqrt(jnp.mean(rows32 * rows32, axis=-1, keepdims=True) + EPS)
    return (rows32 * inverse * gain).astype(jnp.bfloat16)


def prefix_for(gathered, owners, group, per_group):
    prefix_segments = lax.dynamic_slice_in_dim(owners, group * per_group, per_group, 0)
    return gathered[prefix_segments].reshape(per_group * gathered.shape[1], 2, gathered.shape[3])


def req_shift_pairs(n_req, kind, d):
    pairs = []
    for r in range(n_req):
        if kind == "x":
            dest = (r // 4) * 4 + (r % 4 + d) % 4
        elif kind == "z":
            dest = r ^ 4
        else:
            dest = (r + 8 * d) % n_req
        pairs.append((r, dest))
    return pairs


def exp_flip(x, n_exp, bit):
    return lax.ppermute(x, "exp", [(e, e ^ bit) for e in range(n_exp)])


def gather_exp(x, axis, n_exp):
    far = exp_flip(x, n_exp, 2)
    near = exp_flip(jnp.concatenate([x, far], axis=axis), n_exp, 1)
    return jnp.concatenate([x, far, near], axis=axis)


def far_relay(x, n_req, n_exp):
    def index(r, e):
        return r * n_exp + e

    first = []
    second = []
    for r in range(n_req):
        for e in range(n_exp):
            if e % 2 == 0:
                first.append((index(r, e), index(r ^ 4, e)))
                second.append((index(r, e), index(r ^ 4, e ^ 2)))
            else:
                first.append((index(r, e), index(r ^ 4, e ^ 2)))
                second.append((index(r, e), index(r ^ 4, e)))
    hop = lax.ppermute(x, ("req", "exp"), first)
    return lax.ppermute(hop, ("req", "exp"), second)


def gather_exp_relay(x, axis, n_req, n_exp):
    far = far_relay(x, n_req, n_exp)
    near = exp_flip(jnp.concatenate([x, far], axis=axis), n_exp, 1)
    return jnp.concatenate([x, far, near], axis=axis)


def gather_prefix_near(mine, n_req):
    along_x = jnp.stack(
        [mine] + [lax.ppermute(mine, "req", req_shift_pairs(n_req, "x", d)) for d in (1, 2, 3)]
    )
    return jnp.stack([along_x, lax.ppermute(along_x, "req", req_shift_pairs(n_req, "z", 1))])


def gather_prefix_halves(along_z, n_req):
    along_y = jnp.stack(
        [along_z] + [lax.ppermute(along_z, "req", req_shift_pairs(n_req, "y", d)) for d in (1, 2, 3)]
    )
    return along_y.reshape((n_req,) + along_z.shape[2:])


def body(
    activations,
    attn_gain,
    w_query,
    key_value_weight,
    w_output,
    group_prefix_cache,
    lengths,
    groups,
    owners,
    moe_gain,
    w_gate,
    w_up,
    w_down,
    picks,
    pick_weight,
):
    req_index = lax.axis_index("req")
    expert_index = lax.axis_index("exp")
    n_req = lax.axis_size("req")
    n_exp = lax.axis_size("exp")
    tok = activations.shape[0]
    width_model = activations.shape[1]
    heads_per_shard = w_query.shape[1] // HEAD_SIZE
    key_value_head = expert_index * heads_per_shard // (QUERY_HEADS // KEY_VALUE_HEADS)

    own_piece = lax.dynamic_index_in_dim(group_prefix_cache, key_value_head, 2, keepdims=False)
    core = expert_index % 2
    far_half = expert_index // 2
    half_rows = own_piece.shape[0] // 2
    mine = lax.dynamic_slice_in_dim(own_piece, core * half_rows, half_rows, 0)
    along_z = gather_prefix_near(mine, n_req)
    ff_shard = w_gate.shape[2]
    packed = jnp.concatenate([w_gate[0].T, w_up[0].T, w_down[0]], axis=0)
    w_output_late, packed_late, along_z = lax.optimization_barrier((w_output, packed, along_z))
    halves_mine = gather_prefix_halves(along_z, n_req)
    halves_other = exp_flip(halves_mine, n_exp, 1)
    w_output_far = far_relay(w_output_late, n_req, n_exp)
    w_output_far, halves_other = lax.optimization_barrier((w_output_far, halves_other))
    w_output_near = exp_flip(jnp.concatenate([w_output, w_output_far], axis=0), n_exp, 1)
    w_output_full = jnp.concatenate([w_output, w_output_far, w_output_near], axis=0)
    packed_full = gather_exp_relay(packed_late.reshape(1, 3 * ff_shard, -1), 0, n_req, n_exp)
    gate_full = packed_full[:, :ff_shard].reshape(-1, packed.shape[1]).T
    up_full = packed_full[:, ff_shard : 2 * ff_shard].reshape(-1, packed.shape[1]).T
    down_full = packed_full[:, 2 * ff_shard :].reshape(-1, packed.shape[1])

    normalized_input = rms_scale(activations, attn_gain)
    query_rows = (
        jnp.dot(normalized_input, w_query, preferred_element_type=jnp.float32) * HEAD_SIZE ** (-0.5)
    ).astype(jnp.bfloat16)
    query_rows = query_rows.reshape(tok, heads_per_shard, HEAD_SIZE)
    kv_weight = lax.dynamic_slice_in_dim(key_value_weight, key_value_head * HEAD_SIZE, HEAD_SIZE, 2)
    local_key_value = jnp.einsum(
        "td,dcf->tcf", normalized_input, kv_weight, preferred_element_type=jnp.float32
    ).astype(jnp.bfloat16)

    pair = lax.dynamic_slice_in_dim(lengths, req_index * REQ_DEV, REQ_DEV, 0)
    pair_groups = lax.dynamic_slice_in_dim(groups, req_index * REQ_DEV, REQ_DEV, 0)
    per_group = n_req // GROUPS
    positions = jnp.arange(tok)
    in_first = positions < pair[0]
    my_y, my_z, my_x = req_index // 8, (req_index // 4) % 2, req_index % 4

    owner = jnp.stack(
        [lax.dynamic_slice_in_dim(owners, pair_groups[i] * per_group, per_group, 0) for i in range(2)]
    )
    where = ((my_y - owner // 8) % 4) * 8 + ((my_z - (owner // 4) % 2) % 2) * 4 + (my_x - owner % 4) % 4
    pick = (where[:, :, None] == jnp.arange(n_req, dtype=jnp.int32)[None, None, :]).astype(jnp.bfloat16)
    rows_mine = jnp.einsum("gjp,prcd->gcjrd", pick, halves_mine, preferred_element_type=jnp.float32)
    rows_other = jnp.einsum("gjp,prcd->gcjrd", pick, halves_other, preferred_element_type=jnp.float32)
    rows_both = jnp.stack([rows_mine, rows_other], axis=2).astype(jnp.bfloat16)
    prefix_rows = rows_both.reshape(2, 2, per_group * 2 * half_rows, HEAD_SIZE)
    zero_q = jnp.zeros_like(query_rows)
    first3 = in_first[:, None, None]
    query_ab = jnp.concatenate(
        [jnp.where(first3, query_rows, zero_q), jnp.where(first3, zero_q, query_rows)], axis=-1
    )
    keys_ab = jnp.concatenate([prefix_rows[0, 0], prefix_rows[1, 0]], axis=-1)
    values_ab = jnp.concatenate([prefix_rows[0, 1], prefix_rows[1, 1]], axis=-1)
    pre_scores = jnp.einsum("thd,pd->htp", query_ab, keys_ab, preferred_element_type=jnp.float32)
    suf_scores = jnp.einsum(
        "thd,sd->hts", query_rows, local_key_value[:, 0], preferred_element_type=jnp.float32
    )
    allowed = (positions[None, :] <= positions[:, None]) & (in_first[:, None] == in_first[None, :])
    suf_scores = jnp.where(allowed[None], suf_scores, -jnp.inf)
    top = jnp.maximum(
        jnp.max(pre_scores, axis=-1, keepdims=True), jnp.max(suf_scores, axis=-1, keepdims=True)
    )
    pre_exp = jnp.exp(pre_scores - top)
    suf_exp = jnp.exp(suf_scores - top)
    denom = jnp.sum(pre_exp, axis=-1, keepdims=True) + jnp.sum(suf_exp, axis=-1, keepdims=True)
    pre_w = (pre_exp / denom).astype(jnp.bfloat16)
    suf_w = (suf_exp / denom).astype(jnp.bfloat16)
    pre_ctx_ab = jnp.einsum("htp,pd->thd", pre_w, values_ab, preferred_element_type=jnp.float32)
    pre_ctx = jnp.where(first3, pre_ctx_ab[..., :HEAD_SIZE], pre_ctx_ab[..., HEAD_SIZE:])
    suf_ctx = jnp.einsum(
        "hts,sd->thd", suf_w, local_key_value[:, 1], preferred_element_type=jnp.float32
    )
    context = (pre_ctx + suf_ctx).astype(jnp.bfloat16)
    context = context.reshape(tok, heads_per_shard * HEAD_SIZE)
    context_full = gather_exp(context, 1, n_exp)
    attn = jnp.dot(context_full, w_output_full, preferred_element_type=jnp.float32)
    resid = (activations.astype(jnp.float32) + attn).astype(jnp.bfloat16)
    normed_moe = rms_scale(resid, moe_gain)

    n_experts = n_req
    cap = min(tok, 2 * tok * TOP // n_req)
    quarter = cap // n_exp
    expert_ids = jnp.arange(n_experts, dtype=jnp.int32)
    chose = jnp.any(picks[:, :, None] == expert_ids[None, None, :], axis=1).astype(jnp.bfloat16)
    earlier = (positions[None, :] < positions[:, None]).astype(jnp.bfloat16)
    before = jnp.dot(earlier, chose, preferred_element_type=jnp.float32).astype(jnp.int32)
    pick_hot = picks[:, :, None] == expert_ids[None, None, :]
    slot = jnp.sum(jnp.where(pick_hot, before[:, None, :], 0), axis=2)
    local = slot - expert_index * quarter
    keep = (local >= 0) & (local < quarter)
    target = jnp.where(keep, picks * quarter + local, -1)
    columns = jnp.arange(n_experts * quarter, dtype=jnp.int32)
    hits = target[:, :, None] == columns[None, None, :]
    dispatch = jnp.any(hits, axis=1).astype(jnp.bfloat16)
    send = jnp.einsum("tq,td->qd", dispatch, normed_moe, preferred_element_type=jnp.float32)
    send = send.astype(jnp.bfloat16).reshape(n_experts, quarter, width_model)
    combine = jnp.sum(jnp.where(hits, pick_weight[:, :, None], 0.0), axis=1)
    combine = combine.reshape(tok, n_experts, quarter)
    chunks = 1
    step = quarter // chunks
    mix = None
    for k in range(chunks):
        received = lax.all_to_all(
            send[:, k * step : (k + 1) * step], "req", split_axis=0, concat_axis=0, tiled=True
        )
        rows = received.reshape(-1, width_model)
        gate = jnp.dot(rows, gate_full, preferred_element_type=jnp.float32)
        up = jnp.dot(rows, up_full, preferred_element_type=jnp.float32)
        hidden = (jnp.maximum(gate, 0.0) * up).astype(jnp.bfloat16)
        part = jnp.dot(hidden, down_full, preferred_element_type=jnp.float32).astype(jnp.bfloat16)
        part = part.reshape(n_experts, step, width_model)
        back = lax.all_to_all(part, "req", split_axis=0, concat_axis=0, tiled=True)
        back = back.reshape(-1, width_model)
        weights_k = combine[:, :, k * step : (k + 1) * step].reshape(tok, -1)
        weights_hi = weights_k.astype(jnp.bfloat16)
        weights_lo = (weights_k - weights_hi.astype(jnp.float32)).astype(jnp.bfloat16)
        mix_k = jnp.dot(weights_hi, back, preferred_element_type=jnp.float32) + jnp.dot(
            weights_lo, back, preferred_element_type=jnp.float32
        )
        mix = mix_k if mix is None else mix + mix_k
    half_tok = tok // 2
    quarter_tok = tok // 4
    keep_half = lax.dynamic_slice_in_dim(mix, core * half_tok, half_tok, 0)
    give_half = lax.dynamic_slice_in_dim(mix, (1 - core) * half_tok, half_tok, 0)
    half_sum = keep_half + exp_flip(give_half, n_exp, 1)
    keep_q = lax.dynamic_slice_in_dim(half_sum, far_half * quarter_tok, quarter_tok, 0)
    give_q = lax.dynamic_slice_in_dim(half_sum, (1 - far_half) * quarter_tok, quarter_tok, 0)
    quarter_sum = keep_q + exp_flip(give_q, n_exp, 2)
    my_rows = core * half_tok + far_half * quarter_tok
    resid_rows = lax.dynamic_slice_in_dim(resid, my_rows, quarter_tok, 0)
    out_q = (resid_rows.astype(jnp.float32) + quarter_sum).astype(jnp.bfloat16)
    other_q = exp_flip(out_q, n_exp, 2)
    out_half = jnp.where(
        far_half == 0,
        jnp.concatenate([out_q, other_q], axis=0),
        jnp.concatenate([other_q, out_q], axis=0),
    )
    other_half = exp_flip(out_half, n_exp, 1)
    return jnp.where(
        core == 0,
        jnp.concatenate([out_half, other_half], axis=0),
        jnp.concatenate([other_half, out_half], axis=0),
    )


def solution(mesh):
    return jax.shard_map(
        body,
        mesh=mesh,
        in_specs=(
            P("req", None),
            P(),
            P(None, "exp"),
            P(),
            P("exp", None),
            P("req", None, None, None),
            P(),
            P(),
            P(),
            P(),
            P("req", None, "exp"),
            P("req", None, "exp"),
            P("req", "exp", None),
            P("req", None),
            P("req", None),
        ),
        out_specs=P("req", None),
        check_vma=False,
    )
```

```python
import jax
import jax.numpy as jnp
from jax import lax
from jax.sharding import PartitionSpec as P

QUERY_HEADS = 12
KEY_VALUE_HEADS = 2
HEAD_SIZE = 128
TOP = 4
GROUPS = 4
REQ_DEV = 2
LMIN = 64


EPS = 1e-06


def rms_scale(rows, gain):
    rows32 = rows.astype(jnp.float32)
    inverse = lax.rsqrt(jnp.mean(rows32 * rows32, axis=-1, keepdims=True) + EPS)
    return (rows32 * inverse * gain).astype(jnp.bfloat16)


def prefix_for(gathered, owners, group, per_group):
    prefix_segments = lax.dynamic_slice_in_dim(owners, group * per_group, per_group, 0)
    return gathered[prefix_segments].reshape(per_group * gathered.shape[1], 2, gathered.shape[3])


def req_shift_pairs(n_req, kind, d):
    pairs = []
    for r in range(n_req):
        if kind == "x":
            dest = (r // 4) * 4 + (r % 4 + d) % 4
        elif kind == "z":
            dest = r ^ 4
        else:
            dest = (r + 8 * d) % n_req
        pairs.append((r, dest))
    return pairs


def exp_flip(x, n_exp, bit):
    return lax.ppermute(x, "exp", [(e, e ^ bit) for e in range(n_exp)])


def gather_exp(x, axis, n_exp):
    far = exp_flip(x, n_exp, 2)
    near = exp_flip(jnp.concatenate([x, far], axis=axis), n_exp, 1)
    return jnp.concatenate([x, far, near], axis=axis)


def relay_pairs(n_req, n_exp):
    def index(r, e):
        return r * n_exp + e

    first = []
    second = []
    for r in range(n_req):
        for e in range(n_exp):
            if e % 2 == 0:
                first.append((index(r, e), index(r ^ 4, e)))
                second.append((index(r, e), index(r ^ 4, e ^ 2)))
            else:
                first.append((index(r, e), index(r ^ 4, e ^ 2)))
                second.append((index(r, e), index(r ^ 4, e)))
    return first, second


def far_relay_first(x, n_req, n_exp):
    return lax.ppermute(x, ("req", "exp"), relay_pairs(n_req, n_exp)[0])


def far_relay_second(x, n_req, n_exp):
    return lax.ppermute(x, ("req", "exp"), relay_pairs(n_req, n_exp)[1])


def far_relay(x, n_req, n_exp):
    def index(r, e):
        return r * n_exp + e

    first = []
    second = []
    for r in range(n_req):
        for e in range(n_exp):
            if e % 2 == 0:
                first.append((index(r, e), index(r ^ 4, e)))
                second.append((index(r, e), index(r ^ 4, e ^ 2)))
            else:
                first.append((index(r, e), index(r ^ 4, e ^ 2)))
                second.append((index(r, e), index(r ^ 4, e)))
    hop = lax.ppermute(x, ("req", "exp"), first)
    return lax.ppermute(hop, ("req", "exp"), second)


def gather_exp_relay(x, axis, n_req, n_exp):
    far = far_relay(x, n_req, n_exp)
    near = exp_flip(jnp.concatenate([x, far], axis=axis), n_exp, 1)
    return jnp.concatenate([x, far, near], axis=axis)


def gather_prefix_near(mine, n_req):
    along_x = jnp.stack(
        [mine] + [lax.ppermute(mine, "req", req_shift_pairs(n_req, "x", d)) for d in (1, 2, 3)]
    )
    return jnp.stack([along_x, lax.ppermute(along_x, "req", req_shift_pairs(n_req, "z", 1))])


def gather_prefix_halves(along_z, n_req):
    along_y = jnp.stack(
        [along_z] + [lax.ppermute(along_z, "req", req_shift_pairs(n_req, "y", d)) for d in (1, 2, 3)]
    )
    return along_y.reshape((n_req,) + along_z.shape[2:])


def body(
    activations,
    attn_gain,
    w_query,
    key_value_weight,
    w_output,
    group_prefix_cache,
    lengths,
    groups,
    owners,
    moe_gain,
    w_gate,
    w_up,
    w_down,
    picks,
    pick_weight,
):
    req_index = lax.axis_index("req")
    expert_index = lax.axis_index("exp")
    n_req = lax.axis_size("req")
    n_exp = lax.axis_size("exp")
    tok = activations.shape[0]
    width_model = activations.shape[1]
    heads_per_shard = w_query.shape[1] // HEAD_SIZE
    key_value_head = expert_index * heads_per_shard // (QUERY_HEADS // KEY_VALUE_HEADS)

    own_piece = lax.dynamic_index_in_dim(group_prefix_cache, key_value_head, 2, keepdims=False)
    core = expert_index % 2
    far_half = expert_index // 2
    half_rows = own_piece.shape[0] // 2
    mine = lax.dynamic_slice_in_dim(own_piece, core * half_rows, half_rows, 0)
    along_z = gather_prefix_near(mine, n_req)
    ff_shard = w_gate.shape[2]
    packed = jnp.concatenate([w_gate[0].T, w_up[0].T, w_down[0]], axis=0)
    w_output_late, packed_late, along_z = lax.optimization_barrier((w_output, packed, along_z))
    halves_mine = gather_prefix_halves(along_z, n_req)
    halves_other = exp_flip(halves_mine, n_exp, 1)
    w_output_far = far_relay(w_output_late, n_req, n_exp)
    w_output_far, halves_other = lax.optimization_barrier((w_output_far, halves_other))
    w_output_near = exp_flip(jnp.concatenate([w_output, w_output_far], axis=0), n_exp, 1)
    w_output_full = jnp.concatenate([w_output, w_output_far, w_output_near], axis=0)
    packed_hop = far_relay_first(packed_late.reshape(1, 3 * ff_shard, -1), n_req, n_exp)

    normalized_input = rms_scale(activations, attn_gain)
    query_rows = (
        jnp.dot(normalized_input, w_query, preferred_element_type=jnp.float32) * HEAD_SIZE ** (-0.5)
    ).astype(jnp.bfloat16)
    query_rows = query_rows.reshape(tok, heads_per_shard, HEAD_SIZE)
    kv_weight = lax.dynamic_slice_in_dim(key_value_weight, key_value_head * HEAD_SIZE, HEAD_SIZE, 2)
    local_key_value = jnp.einsum(
        "td,dcf->tcf", normalized_input, kv_weight, preferred_element_type=jnp.float32
    ).astype(jnp.bfloat16)

    pair = lax.dynamic_slice_in_dim(lengths, req_index * REQ_DEV, REQ_DEV, 0)
    pair_groups = lax.dynamic_slice_in_dim(groups, req_index * REQ_DEV, REQ_DEV, 0)
    per_group = n_req // GROUPS
    positions = jnp.arange(tok)
    in_first = positions < pair[0]
    my_y, my_z, my_x = req_index // 8, (req_index // 4) % 2, req_index % 4

    owner = jnp.stack(
        [lax.dynamic_slice_in_dim(owners, pair_groups[i] * per_group, per_group, 0) for i in range(2)]
    )
    where = ((my_y - owner // 8) % 4) * 8 + ((my_z - (owner // 4) % 2) % 2) * 4 + (my_x - owner % 4) % 4
    pick = (where[:, :, None] == jnp.arange(n_req, dtype=jnp.int32)[None, None, :]).astype(jnp.bfloat16)
    rows_mine = jnp.einsum("gjp,prcd->gcjrd", pick, halves_mine, preferred_element_type=jnp.float32)
    rows_other = jnp.einsum("gjp,prcd->gcjrd", pick, halves_other, preferred_element_type=jnp.float32)
    rows_both = jnp.stack([rows_mine, rows_other], axis=2).astype(jnp.bfloat16)
    prefix_rows = rows_both.reshape(2, 2, per_group * 2 * half_rows, HEAD_SIZE)
    zero_q = jnp.zeros_like(query_rows)
    first3 = in_first[:, None, None]
    query_ab = jnp.concatenate(
        [jnp.where(first3, query_rows, zero_q), jnp.where(first3, zero_q, query_rows)], axis=-1
    )
    keys_ab = jnp.concatenate([prefix_rows[0, 0], prefix_rows[1, 0]], axis=-1)
    values_ab = jnp.concatenate([prefix_rows[0, 1], prefix_rows[1, 1]], axis=-1)
    pre_scores = jnp.einsum("thd,pd->htp", query_ab, keys_ab, preferred_element_type=jnp.float32)
    suf_scores = jnp.einsum(
        "thd,sd->hts", query_rows, local_key_value[:, 0], preferred_element_type=jnp.float32
    )
    allowed = (positions[None, :] <= positions[:, None]) & (in_first[:, None] == in_first[None, :])
    suf_scores = jnp.where(allowed[None], suf_scores, -jnp.inf)
    top = jnp.maximum(
        jnp.max(pre_scores, axis=-1, keepdims=True), jnp.max(suf_scores, axis=-1, keepdims=True)
    )
    pre_exp = jnp.exp(pre_scores - top)
    suf_exp = jnp.exp(suf_scores - top)
    denom = jnp.sum(pre_exp, axis=-1, keepdims=True) + jnp.sum(suf_exp, axis=-1, keepdims=True)
    pre_w = (pre_exp / denom).astype(jnp.bfloat16)
    packed_hop, pre_w = lax.optimization_barrier((packed_hop, pre_w))
    packed_far = far_relay_second(packed_hop, n_req, n_exp)
    suf_w = (suf_exp / denom).astype(jnp.bfloat16)
    pre_ctx_ab = jnp.einsum("htp,pd->thd", pre_w, values_ab, preferred_element_type=jnp.float32)
    pre_ctx = jnp.where(first3, pre_ctx_ab[..., :HEAD_SIZE], pre_ctx_ab[..., HEAD_SIZE:])
    suf_ctx = jnp.einsum(
        "hts,sd->thd", suf_w, local_key_value[:, 1], preferred_element_type=jnp.float32
    )
    context = (pre_ctx + suf_ctx).astype(jnp.bfloat16)
    context = context.reshape(tok, heads_per_shard * HEAD_SIZE)
    context_full = gather_exp(context, 1, n_exp)
    attn = jnp.dot(context_full, w_output_full, preferred_element_type=jnp.float32)
    resid = (activations.astype(jnp.float32) + attn).astype(jnp.bfloat16)
    normed_moe = rms_scale(resid, moe_gain)
    packed_far, normed_moe = lax.optimization_barrier((packed_far, normed_moe))
    packed_own = packed.reshape(1, 3 * ff_shard, -1)
    packed_near = exp_flip(jnp.concatenate([packed_own, packed_far], axis=0), n_exp, 1)
    packed_full = jnp.concatenate([packed_own, packed_far, packed_near], axis=0)
    gate_full = packed_full[:, :ff_shard].reshape(-1, packed.shape[1]).T
    up_full = packed_full[:, ff_shard : 2 * ff_shard].reshape(-1, packed.shape[1]).T
    down_full = packed_full[:, 2 * ff_shard :].reshape(-1, packed.shape[1])

    n_experts = n_req
    cap = min(tok, 2 * tok * TOP // n_req)
    quarter = cap // n_exp
    expert_ids = jnp.arange(n_experts, dtype=jnp.int32)
    chose = jnp.any(picks[:, :, None] == expert_ids[None, None, :], axis=1).astype(jnp.bfloat16)
    earlier = (positions[None, :] < positions[:, None]).astype(jnp.bfloat16)
    before = jnp.dot(earlier, chose, preferred_element_type=jnp.float32).astype(jnp.int32)
    pick_hot = picks[:, :, None] == expert_ids[None, None, :]
    slot = jnp.sum(jnp.where(pick_hot, before[:, None, :], 0), axis=2)
    local = slot - expert_index * quarter
    keep = (local >= 0) & (local < quarter)
    target = jnp.where(keep, picks * quarter + local, -1)
    columns = jnp.arange(n_experts * quarter, dtype=jnp.int32)
    hits = target[:, :, None] == columns[None, None, :]
    dispatch = jnp.any(hits, axis=1).astype(jnp.bfloat16)
    send = jnp.einsum("tq,td->qd", dispatch, normed_moe, preferred_element_type=jnp.float32)
    send = send.astype(jnp.bfloat16).reshape(n_experts, quarter, width_model)
    combine = jnp.sum(jnp.where(hits, pick_weight[:, :, None], 0.0), axis=1)
    combine = combine.reshape(tok, n_experts, quarter)
    chunks = 1
    step = quarter // chunks
    mix = None
    for k in range(chunks):
        received = lax.all_to_all(
            send[:, k * step : (k + 1) * step], "req", split_axis=0, concat_axis=0, tiled=True
        )
        rows = received.reshape(-1, width_model)
        gate = jnp.dot(rows, gate_full, preferred_element_type=jnp.float32)
        up = jnp.dot(rows, up_full, preferred_element_type=jnp.float32)
        hidden = (jnp.maximum(gate, 0.0) * up).astype(jnp.bfloat16)
        part = jnp.dot(hidden, down_full, preferred_element_type=jnp.float32).astype(jnp.bfloat16)
        part = part.reshape(n_experts, step, width_model)
        back = lax.all_to_all(part, "req", split_axis=0, concat_axis=0, tiled=True)
        back = back.reshape(-1, width_model)
        weights_k = combine[:, :, k * step : (k + 1) * step].reshape(tok, -1)
        weights_hi = weights_k.astype(jnp.bfloat16)
        weights_lo = (weights_k - weights_hi.astype(jnp.float32)).astype(jnp.bfloat16)
        mix_k = jnp.dot(weights_hi, back, preferred_element_type=jnp.float32) + jnp.dot(
            weights_lo, back, preferred_element_type=jnp.float32
        )
        mix = mix_k if mix is None else mix + mix_k
    half_tok = tok // 2
    quarter_tok = tok // 4
    keep_half = lax.dynamic_slice_in_dim(mix, core * half_tok, half_tok, 0)
    give_half = lax.dynamic_slice_in_dim(mix, (1 - core) * half_tok, half_tok, 0)
    half_sum = keep_half + exp_flip(give_half, n_exp, 1)
    keep_q = lax.dynamic_slice_in_dim(half_sum, far_half * quarter_tok, quarter_tok, 0)
    give_q = lax.dynamic_slice_in_dim(half_sum, (1 - far_half) * quarter_tok, quarter_tok, 0)
    quarter_sum = keep_q + exp_flip(give_q, n_exp, 2)
    my_rows = core * half_tok + far_half * quarter_tok
    resid_rows = lax.dynamic_slice_in_dim(resid, my_rows, quarter_tok, 0)
    out_q = (resid_rows.astype(jnp.float32) + quarter_sum).astype(jnp.bfloat16)
    other_q = exp_flip(out_q, n_exp, 2)
    out_half = jnp.where(
        far_half == 0,
        jnp.concatenate([out_q, other_q], axis=0),
        jnp.concatenate([other_q, out_q], axis=0),
    )
    other_half = exp_flip(out_half, n_exp, 1)
    return jnp.where(
        core == 0,
        jnp.concatenate([out_half, other_half], axis=0),
        jnp.concatenate([other_half, out_half], axis=0),
    )


def solution(mesh):
    return jax.shard_map(
        body,
        mesh=mesh,
        in_specs=(
            P("req", None),
            P(),
            P(None, "exp"),
            P(),
            P("exp", None),
            P("req", None, None, None),
            P(),
            P(),
            P(),
            P(),
            P("req", None, "exp"),
            P("req", None, "exp"),
            P("req", "exp", None),
            P("req", None),
            P("req", None),
        ),
        out_specs=P("req", None),
        check_vma=False,
    )
```

```python
import jax
import jax.numpy as jnp
from jax import lax
from jax.sharding import PartitionSpec as P

QUERY_HEADS = 12
KEY_VALUE_HEADS = 2
HEAD_SIZE = 128
TOP = 4
GROUPS = 4
REQ_DEV = 2
LMIN = 64


EPS = 1e-06


def rms_scale(rows, gain):
    rows32 = rows.astype(jnp.float32)
    inverse = lax.rsqrt(jnp.mean(rows32 * rows32, axis=-1, keepdims=True) + EPS)
    return (rows32 * inverse * gain).astype(jnp.bfloat16)


def prefix_for(gathered, owners, group, per_group):
    prefix_segments = lax.dynamic_slice_in_dim(owners, group * per_group, per_group, 0)
    return gathered[prefix_segments].reshape(per_group * gathered.shape[1], 2, gathered.shape[3])


def req_shift_pairs(n_req, kind, d):
    pairs = []
    for r in range(n_req):
        if kind == "x":
            dest = (r // 4) * 4 + (r % 4 + d) % 4
        elif kind == "z":
            dest = r ^ 4
        else:
            dest = (r + 8 * d) % n_req
        pairs.append((r, dest))
    return pairs


def exp_flip(x, n_exp, bit):
    return lax.ppermute(x, "exp", [(e, e ^ bit) for e in range(n_exp)])


def gather_exp(x, axis, n_exp):
    far = exp_flip(x, n_exp, 2)
    near = exp_flip(jnp.concatenate([x, far], axis=axis), n_exp, 1)
    return jnp.concatenate([x, far, near], axis=axis)


def far_relay(x, n_req, n_exp):
    def index(r, e):
        return r * n_exp + e

    first = []
    second = []
    for r in range(n_req):
        for e in range(n_exp):
            if e % 2 == 0:
                first.append((index(r, e), index(r ^ 4, e)))
                second.append((index(r, e), index(r ^ 4, e ^ 2)))
            else:
                first.append((index(r, e), index(r ^ 4, e ^ 2)))
                second.append((index(r, e), index(r ^ 4, e)))
    hop = lax.ppermute(x, ("req", "exp"), first)
    return lax.ppermute(hop, ("req", "exp"), second)


def gather_exp_relay(x, axis, n_req, n_exp):
    far = far_relay(x, n_req, n_exp)
    near = exp_flip(jnp.concatenate([x, far], axis=axis), n_exp, 1)
    return jnp.concatenate([x, far, near], axis=axis)


def gather_prefix_near(mine, n_req):
    along_x = jnp.stack(
        [mine] + [lax.ppermute(mine, "req", req_shift_pairs(n_req, "x", d)) for d in (1, 2, 3)]
    )
    return jnp.stack([along_x, lax.ppermute(along_x, "req", req_shift_pairs(n_req, "z", 1))])


def gather_prefix_halves(along_z, n_req):
    along_y = jnp.stack(
        [along_z] + [lax.ppermute(along_z, "req", req_shift_pairs(n_req, "y", d)) for d in (1, 2, 3)]
    )
    return along_y.reshape((n_req,) + along_z.shape[2:])


def body(
    activations,
    attn_gain,
    w_query,
    key_value_weight,
    w_output,
    group_prefix_cache,
    lengths,
    groups,
    owners,
    moe_gain,
    w_gate,
    w_up,
    w_down,
    picks,
    pick_weight,
):
    req_index = lax.axis_index("req")
    expert_index = lax.axis_index("exp")
    n_req = lax.axis_size("req")
    n_exp = lax.axis_size("exp")
    tok = activations.shape[0]
    width_model = activations.shape[1]
    heads_per_shard = w_query.shape[1] // HEAD_SIZE
    key_value_head = expert_index * heads_per_shard // (QUERY_HEADS // KEY_VALUE_HEADS)

    own_piece = lax.dynamic_index_in_dim(group_prefix_cache, key_value_head, 2, keepdims=False)
    core = expert_index % 2
    far_half = expert_index // 2
    half_rows = own_piece.shape[0] // 2
    mine = lax.dynamic_slice_in_dim(own_piece, core * half_rows, half_rows, 0)
    along_z = gather_prefix_near(mine, n_req)
    ff_shard = w_gate.shape[2]
    packed = jnp.concatenate([w_gate[0].T, w_up[0].T, w_down[0]], axis=0)
    w_output_late, packed_late, along_z = lax.optimization_barrier((w_output, packed, along_z))
    halves_mine = gather_prefix_halves(along_z, n_req)
    halves_other = exp_flip(halves_mine, n_exp, 1)
    w_output_full = gather_exp_relay(w_output_late, 0, n_req, n_exp)
    packed_full = gather_exp_relay(packed_late.reshape(1, 3 * ff_shard, -1), 0, n_req, n_exp)
    gate_full = packed_full[:, :ff_shard].reshape(-1, packed.shape[1]).T
    up_full = packed_full[:, ff_shard : 2 * ff_shard].reshape(-1, packed.shape[1]).T
    down_full = packed_full[:, 2 * ff_shard :].reshape(-1, packed.shape[1])

    normalized_input = rms_scale(activations, attn_gain)
    query_rows = (
        jnp.dot(normalized_input, w_query, preferred_element_type=jnp.float32) * HEAD_SIZE ** (-0.5)
    ).astype(jnp.bfloat16)
    query_rows = query_rows.reshape(tok, heads_per_shard, HEAD_SIZE)
    kv_weight = lax.dynamic_slice_in_dim(key_value_weight, key_value_head * HEAD_SIZE, HEAD_SIZE, 2)
    local_key_value = jnp.einsum(
        "td,dcf->tcf", normalized_input, kv_weight, preferred_element_type=jnp.float32
    ).astype(jnp.bfloat16)

    pair = lax.dynamic_slice_in_dim(lengths, req_index * REQ_DEV, REQ_DEV, 0)
    pair_groups = lax.dynamic_slice_in_dim(groups, req_index * REQ_DEV, REQ_DEV, 0)
    per_group = n_req // GROUPS
    positions = jnp.arange(tok)
    in_first = positions < pair[0]
    my_y, my_z, my_x = req_index // 8, (req_index // 4) % 2, req_index % 4

    owner = jnp.stack(
        [lax.dynamic_slice_in_dim(owners, pair_groups[i] * per_group, per_group, 0) for i in range(2)]
    )
    where = ((my_y - owner // 8) % 4) * 8 + ((my_z - (owner // 4) % 2) % 2) * 4 + (my_x - owner % 4) % 4
    pick = (where[:, :, None] == jnp.arange(n_req, dtype=jnp.int32)[None, None, :]).astype(jnp.bfloat16)
    rows_mine = jnp.einsum("gjp,prcd->gcjrd", pick, halves_mine, preferred_element_type=jnp.float32)
    rows_other = jnp.einsum("gjp,prcd->gcjrd", pick, halves_other, preferred_element_type=jnp.float32)
    rows_both = jnp.stack([rows_mine, rows_other], axis=2).astype(jnp.bfloat16)
    prefix_rows = rows_both.reshape(2, 2, per_group * 2 * half_rows, HEAD_SIZE)
    zero_q = jnp.zeros_like(query_rows)
    first3 = in_first[:, None, None]
    query_ab = jnp.concatenate(
        [jnp.where(first3, query_rows, zero_q), jnp.where(first3, zero_q, query_rows)], axis=-1
    )
    keys_ab = jnp.concatenate([prefix_rows[0, 0], prefix_rows[1, 0]], axis=-1)
    values_ab = jnp.concatenate([prefix_rows[0, 1], prefix_rows[1, 1]], axis=-1)
    pre_scores = jnp.einsum("thd,pd->htp", query_ab, keys_ab, preferred_element_type=jnp.float32)
    suf_scores = jnp.einsum(
        "thd,sd->hts", query_rows, local_key_value[:, 0], preferred_element_type=jnp.float32
    )
    allowed = (positions[None, :] <= positions[:, None]) & (in_first[:, None] == in_first[None, :])
    suf_scores = jnp.where(allowed[None], suf_scores, -jnp.inf)
    top = jnp.maximum(
        jnp.max(pre_scores, axis=-1, keepdims=True), jnp.max(suf_scores, axis=-1, keepdims=True)
    )
    pre_exp = jnp.exp(pre_scores - top)
    suf_exp = jnp.exp(suf_scores - top)
    denom = jnp.sum(pre_exp, axis=-1, keepdims=True) + jnp.sum(suf_exp, axis=-1, keepdims=True)
    pre_w = (pre_exp / denom).astype(jnp.bfloat16)
    suf_w = (suf_exp / denom).astype(jnp.bfloat16)
    pre_ctx_ab = jnp.einsum("htp,pd->thd", pre_w, values_ab, preferred_element_type=jnp.float32)
    pre_ctx = jnp.where(first3, pre_ctx_ab[..., :HEAD_SIZE], pre_ctx_ab[..., HEAD_SIZE:])
    suf_ctx = jnp.einsum(
        "hts,sd->thd", suf_w, local_key_value[:, 1], preferred_element_type=jnp.float32
    )
    context = (pre_ctx + suf_ctx).astype(jnp.bfloat16)
    context = context.reshape(tok, heads_per_shard * HEAD_SIZE)
    context_full = gather_exp(context, 1, n_exp)
    attn = jnp.dot(context_full, w_output_full, preferred_element_type=jnp.float32)
    resid = (activations.astype(jnp.float32) + attn).astype(jnp.bfloat16)
    normed_moe = rms_scale(resid, moe_gain)

    n_experts = n_req
    cap = min(tok, 2 * tok * TOP // n_req)
    quarter = cap // n_exp
    expert_ids = jnp.arange(n_experts, dtype=jnp.int32)
    chose = jnp.any(picks[:, :, None] == expert_ids[None, None, :], axis=1).astype(jnp.bfloat16)
    earlier = (positions[None, :] < positions[:, None]).astype(jnp.bfloat16)
    before = jnp.dot(earlier, chose, preferred_element_type=jnp.float32).astype(jnp.int32)
    pick_hot = picks[:, :, None] == expert_ids[None, None, :]
    slot = jnp.sum(jnp.where(pick_hot, before[:, None, :], 0), axis=2)
    local = slot - expert_index * quarter
    keep = (local >= 0) & (local < quarter)
    target = jnp.where(keep, picks * quarter + local, -1)
    columns = jnp.arange(n_experts * quarter, dtype=jnp.int32)
    hits = target[:, :, None] == columns[None, None, :]
    dispatch = jnp.any(hits, axis=1).astype(jnp.bfloat16)
    send = jnp.einsum("tq,td->qd", dispatch, normed_moe, preferred_element_type=jnp.float32)
    send = send.astype(jnp.bfloat16).reshape(n_experts, quarter, width_model)
    received = lax.all_to_all(send, "req", split_axis=0, concat_axis=0, tiled=True)
    rows = received.reshape(-1, width_model)
    gate = jnp.dot(rows, gate_full, preferred_element_type=jnp.float32)
    up = jnp.dot(rows, up_full, preferred_element_type=jnp.float32)
    hidden = (jnp.maximum(gate, 0.0) * up).astype(jnp.bfloat16)
    part = jnp.dot(hidden, down_full, preferred_element_type=jnp.float32).astype(jnp.bfloat16)
    part = part.reshape(n_experts, quarter, width_model)
    back = lax.all_to_all(part, "req", split_axis=0, concat_axis=0, tiled=True)
    back = back.reshape(-1, width_model)
    combine = jnp.sum(jnp.where(hits, pick_weight[:, :, None], 0.0), axis=1)
    combine_hi = combine.astype(jnp.bfloat16)
    combine_lo = (combine - combine_hi.astype(jnp.float32)).astype(jnp.bfloat16)
    mix = jnp.dot(combine_hi, back, preferred_element_type=jnp.float32) + jnp.dot(
        combine_lo, back, preferred_element_type=jnp.float32
    )
    half_tok = tok // 2
    quarter_tok = tok // 4
    keep_half = lax.dynamic_slice_in_dim(mix, core * half_tok, half_tok, 0)
    give_half = lax.dynamic_slice_in_dim(mix, (1 - core) * half_tok, half_tok, 0)
    half_sum = keep_half + exp_flip(give_half, n_exp, 1)
    keep_q = lax.dynamic_slice_in_dim(half_sum, far_half * quarter_tok, quarter_tok, 0)
    give_q = lax.dynamic_slice_in_dim(half_sum, (1 - far_half) * quarter_tok, quarter_tok, 0)
    quarter_sum = keep_q + exp_flip(give_q, n_exp, 2)
    my_rows = core * half_tok + far_half * quarter_tok
    resid_rows = lax.dynamic_slice_in_dim(resid, my_rows, quarter_tok, 0)
    out_q = (resid_rows.astype(jnp.float32) + quarter_sum).astype(jnp.bfloat16)
    other_q = exp_flip(out_q, n_exp, 2)
    out_half = jnp.where(
        far_half == 0,
        jnp.concatenate([out_q, other_q], axis=0),
        jnp.concatenate([other_q, out_q], axis=0),
    )
    other_half = exp_flip(out_half, n_exp, 1)
    return jnp.where(
        core == 0,
        jnp.concatenate([out_half, other_half], axis=0),
        jnp.concatenate([other_half, out_half], axis=0),
    )


def solution(mesh):
    return jax.shard_map(
        body,
        mesh=mesh,
        in_specs=(
            P("req", None),
            P(),
            P(None, "exp"),
            P(),
            P("exp", None),
            P("req", None, None, None),
            P(),
            P(),
            P(),
            P(),
            P("req", None, "exp"),
            P("req", None, "exp"),
            P("req", "exp", None),
            P("req", None),
            P("req", None),
        ),
        out_specs=P("req", None),
        check_vma=False,
    )
```

```python
import jax
import jax.numpy as jnp
from jax import lax
from jax.sharding import PartitionSpec as P

QUERY_HEADS = 12
KEY_VALUE_HEADS = 2
HEAD_SIZE = 128
TOP = 4
GROUPS = 4
REQ_DEV = 2
LMIN = 64


EPS = 1e-06


def rms_scale(rows, gain):
    rows32 = rows.astype(jnp.float32)
    inverse = lax.rsqrt(jnp.mean(rows32 * rows32, axis=-1, keepdims=True) + EPS)
    return (rows32 * inverse * gain).astype(jnp.bfloat16)


def prefix_for(gathered, owners, group, per_group):
    prefix_segments = lax.dynamic_slice_in_dim(owners, group * per_group, per_group, 0)
    return gathered[prefix_segments].reshape(per_group * gathered.shape[1], 2, gathered.shape[3])


def req_shift_pairs(n_req, kind, d):
    pairs = []
    for r in range(n_req):
        if kind == "x":
            dest = (r // 4) * 4 + (r % 4 + d) % 4
        elif kind == "z":
            dest = r ^ 4
        else:
            dest = (r + 8 * d) % n_req
        pairs.append((r, dest))
    return pairs


def exp_flip(x, n_exp, bit):
    return lax.ppermute(x, "exp", [(e, e ^ bit) for e in range(n_exp)])


def gather_exp(x, axis, n_exp):
    far = exp_flip(x, n_exp, 2)
    near = exp_flip(jnp.concatenate([x, far], axis=axis), n_exp, 1)
    return jnp.concatenate([x, far, near], axis=axis)


def far_relay(x, n_req, n_exp):
    def index(r, e):
        return r * n_exp + e

    first = []
    second = []
    for r in range(n_req):
        for e in range(n_exp):
            if e % 2 == 0:
                first.append((index(r, e), index(r ^ 4, e)))
                second.append((index(r, e), index(r ^ 4, e ^ 2)))
            else:
                first.append((index(r, e), index(r ^ 4, e ^ 2)))
                second.append((index(r, e), index(r ^ 4, e)))
    hop = lax.ppermute(x, ("req", "exp"), first)
    return lax.ppermute(hop, ("req", "exp"), second)


def gather_exp_relay(x, axis, n_req, n_exp):
    far = far_relay(x, n_req, n_exp)
    near = exp_flip(jnp.concatenate([x, far], axis=axis), n_exp, 1)
    return jnp.concatenate([x, far, near], axis=axis)


def gather_prefix_near(mine, n_req):
    return jnp.stack([mine, lax.ppermute(mine, "req", req_shift_pairs(n_req, "z", 1))])


def gather_prefix_halves(along_z, n_req):
    along_x = jnp.stack(
        [along_z] + [lax.ppermute(along_z, "req", req_shift_pairs(n_req, "x", d)) for d in (1, 2, 3)]
    )
    along_y = jnp.stack(
        [along_x] + [lax.ppermute(along_x, "req", req_shift_pairs(n_req, "y", d)) for d in (1, 2, 3)]
    )
    return along_y.reshape((n_req,) + along_z.shape[1:])


def body(
    activations,
    attn_gain,
    w_query,
    key_value_weight,
    w_output,
    group_prefix_cache,
    lengths,
    groups,
    owners,
    moe_gain,
    w_gate,
    w_up,
    w_down,
    picks,
    pick_weight,
):
    req_index = lax.axis_index("req")
    expert_index = lax.axis_index("exp")
    n_req = lax.axis_size("req")
    n_exp = lax.axis_size("exp")
    tok = activations.shape[0]
    width_model = activations.shape[1]
    heads_per_shard = w_query.shape[1] // HEAD_SIZE
    key_value_head = expert_index * heads_per_shard // (QUERY_HEADS // KEY_VALUE_HEADS)

    own_piece = lax.dynamic_index_in_dim(group_prefix_cache, key_value_head, 2, keepdims=False)
    core = expert_index % 2
    far_half = expert_index // 2
    half_rows = own_piece.shape[0] // 2
    mine = lax.dynamic_slice_in_dim(own_piece, core * half_rows, half_rows, 0)
    along_z = gather_prefix_near(mine, n_req)
    ff_shard = w_gate.shape[2]
    packed = jnp.concatenate([w_gate[0].T, w_up[0].T, w_down[0]], axis=0)
    w_output_late, packed_late, along_z = lax.optimization_barrier((w_output, packed, along_z))
    halves_mine = gather_prefix_halves(along_z, n_req)
    halves_other = exp_flip(halves_mine, n_exp, 1)
    w_output_full = gather_exp_relay(w_output_late, 0, n_req, n_exp)
    packed_full = gather_exp_relay(packed_late.reshape(1, 3 * ff_shard, -1), 0, n_req, n_exp)
    gate_full = packed_full[:, :ff_shard].reshape(-1, packed.shape[1]).T
    up_full = packed_full[:, ff_shard : 2 * ff_shard].reshape(-1, packed.shape[1]).T
    down_full = packed_full[:, 2 * ff_shard :].reshape(-1, packed.shape[1])

    normalized_input = rms_scale(activations, attn_gain)
    query_rows = (
        jnp.dot(normalized_input, w_query, preferred_element_type=jnp.float32) * HEAD_SIZE ** (-0.5)
    ).astype(jnp.bfloat16)
    query_rows = query_rows.reshape(tok, heads_per_shard, HEAD_SIZE)
    kv_weight = lax.dynamic_slice_in_dim(key_value_weight, key_value_head * HEAD_SIZE, HEAD_SIZE, 2)
    local_key_value = jnp.einsum(
        "td,dcf->tcf", normalized_input, kv_weight, preferred_element_type=jnp.float32
    ).astype(jnp.bfloat16)

    pair = lax.dynamic_slice_in_dim(lengths, req_index * REQ_DEV, REQ_DEV, 0)
    pair_groups = lax.dynamic_slice_in_dim(groups, req_index * REQ_DEV, REQ_DEV, 0)
    per_group = n_req // GROUPS
    positions = jnp.arange(tok)
    in_first = positions < pair[0]
    my_y, my_z, my_x = req_index // 8, (req_index // 4) % 2, req_index % 4

    def prefix_of(group):
        owner = lax.dynamic_slice_in_dim(owners, group * per_group, per_group, 0)
        where = ((my_y - owner // 8) % 4) * 8 + ((my_x - owner % 4) % 4) * 2 + (my_z - (owner // 4) % 2) % 2
        part_mine = halves_mine[where]
        part_other = halves_other[where]
        rows = jnp.where(
            core == 0,
            jnp.concatenate([part_mine, part_other], axis=1),
            jnp.concatenate([part_other, part_mine], axis=1),
        )
        return rows.reshape(per_group * 2 * half_rows, 2, HEAD_SIZE)

    prefix_a = prefix_of(pair_groups[0])
    prefix_b = prefix_of(pair_groups[1])
    zero_q = jnp.zeros_like(query_rows)
    first3 = in_first[:, None, None]
    query_ab = jnp.concatenate(
        [jnp.where(first3, query_rows, zero_q), jnp.where(first3, zero_q, query_rows)], axis=-1
    )
    keys_ab = jnp.concatenate([prefix_a[:, 0], prefix_b[:, 0]], axis=-1)
    values_ab = jnp.concatenate([prefix_a[:, 1], prefix_b[:, 1]], axis=-1)
    pre_scores = jnp.einsum("thd,pd->htp", query_ab, keys_ab, preferred_element_type=jnp.float32)
    suf_scores = jnp.einsum(
        "thd,sd->hts", query_rows, local_key_value[:, 0], preferred_element_type=jnp.float32
    )
    allowed = (positions[None, :] <= positions[:, None]) & (in_first[:, None] == in_first[None, :])
    suf_scores = jnp.where(allowed[None], suf_scores, -jnp.inf)
    top = jnp.maximum(
        jnp.max(pre_scores, axis=-1, keepdims=True), jnp.max(suf_scores, axis=-1, keepdims=True)
    )
    pre_exp = jnp.exp(pre_scores - top)
    suf_exp = jnp.exp(suf_scores - top)
    denom = jnp.sum(pre_exp, axis=-1, keepdims=True) + jnp.sum(suf_exp, axis=-1, keepdims=True)
    pre_w = (pre_exp / denom).astype(jnp.bfloat16)
    suf_w = (suf_exp / denom).astype(jnp.bfloat16)
    pre_ctx_ab = jnp.einsum("htp,pd->thd", pre_w, values_ab, preferred_element_type=jnp.float32)
    pre_ctx = jnp.where(first3, pre_ctx_ab[..., :HEAD_SIZE], pre_ctx_ab[..., HEAD_SIZE:])
    suf_ctx = jnp.einsum(
        "hts,sd->thd", suf_w, local_key_value[:, 1], preferred_element_type=jnp.float32
    )
    context = (pre_ctx + suf_ctx).astype(jnp.bfloat16)
    context = context.reshape(tok, heads_per_shard * HEAD_SIZE)
    context_full = gather_exp(context, 1, n_exp)
    attn = jnp.dot(context_full, w_output_full, preferred_element_type=jnp.float32)
    resid = (activations.astype(jnp.float32) + attn).astype(jnp.bfloat16)
    normed_moe = rms_scale(resid, moe_gain)

    n_experts = n_req
    cap = min(tok, 2 * tok * TOP // n_req)
    quarter = cap // n_exp
    expert_ids = jnp.arange(n_experts, dtype=jnp.int32)
    chose = jnp.any(picks[:, :, None] == expert_ids[None, None, :], axis=1).astype(jnp.bfloat16)
    earlier = (positions[None, :] < positions[:, None]).astype(jnp.bfloat16)
    before = jnp.dot(earlier, chose, preferred_element_type=jnp.float32).astype(jnp.int32)
    pick_hot = picks[:, :, None] == expert_ids[None, None, :]
    slot = jnp.sum(jnp.where(pick_hot, before[:, None, :], 0), axis=2)
    local = slot - expert_index * quarter
    keep = (local >= 0) & (local < quarter)
    target = jnp.where(keep, picks * quarter + local, -1)
    columns = jnp.arange(n_experts * quarter, dtype=jnp.int32)
    hits = target[:, :, None] == columns[None, None, :]
    dispatch = jnp.any(hits, axis=1).astype(jnp.bfloat16)
    send = jnp.einsum("tq,td->qd", dispatch, normed_moe, preferred_element_type=jnp.float32)
    send = send.astype(jnp.bfloat16).reshape(n_experts, quarter, width_model)
    received = lax.all_to_all(send, "req", split_axis=0, concat_axis=0, tiled=True)
    rows = received.reshape(-1, width_model)
    gate = jnp.dot(rows, gate_full, preferred_element_type=jnp.float32)
    up = jnp.dot(rows, up_full, preferred_element_type=jnp.float32)
    hidden = (jnp.maximum(gate, 0.0) * up).astype(jnp.bfloat16)
    part = jnp.dot(hidden, down_full, preferred_element_type=jnp.float32).astype(jnp.bfloat16)
    part = part.reshape(n_experts, quarter, width_model)
    back = lax.all_to_all(part, "req", split_axis=0, concat_axis=0, tiled=True)
    back = back.reshape(-1, width_model)
    combine = jnp.sum(jnp.where(hits, pick_weight[:, :, None], 0.0), axis=1)
    combine_hi = combine.astype(jnp.bfloat16)
    combine_lo = (combine - combine_hi.astype(jnp.float32)).astype(jnp.bfloat16)
    mix = jnp.dot(combine_hi, back, preferred_element_type=jnp.float32) + jnp.dot(
        combine_lo, back, preferred_element_type=jnp.float32
    )
    half_tok = tok // 2
    quarter_tok = tok // 4
    keep_half = lax.dynamic_slice_in_dim(mix, core * half_tok, half_tok, 0)
    give_half = lax.dynamic_slice_in_dim(mix, (1 - core) * half_tok, half_tok, 0)
    half_sum = keep_half + exp_flip(give_half, n_exp, 1)
    keep_q = lax.dynamic_slice_in_dim(half_sum, far_half * quarter_tok, quarter_tok, 0)
    give_q = lax.dynamic_slice_in_dim(half_sum, (1 - far_half) * quarter_tok, quarter_tok, 0)
    quarter_sum = keep_q + exp_flip(give_q, n_exp, 2)
    my_rows = core * half_tok + far_half * quarter_tok
    resid_rows = lax.dynamic_slice_in_dim(resid, my_rows, quarter_tok, 0)
    out_q = (resid_rows.astype(jnp.float32) + quarter_sum).astype(jnp.bfloat16)
    other_q = exp_flip(out_q, n_exp, 2)
    out_half = jnp.where(
        far_half == 0,
        jnp.concatenate([out_q, other_q], axis=0),
        jnp.concatenate([other_q, out_q], axis=0),
    )
    other_half = exp_flip(out_half, n_exp, 1)
    return jnp.where(
        core == 0,
        jnp.concatenate([out_half, other_half], axis=0),
        jnp.concatenate([other_half, out_half], axis=0),
    )


def solution(mesh):
    return jax.shard_map(
        body,
        mesh=mesh,
        in_specs=(
            P("req", None),
            P(),
            P(None, "exp"),
            P(),
            P("exp", None),
            P("req", None, None, None),
            P(),
            P(),
            P(),
            P(),
            P("req", None, "exp"),
            P("req", None, "exp"),
            P("req", "exp", None),
            P("req", None),
            P("req", None),
        ),
        out_specs=P("req", None),
        check_vma=False,
    )
```

```python
import jax
import jax.numpy as jnp
from jax import lax
from jax.sharding import PartitionSpec as P

QUERY_HEADS = 12
KEY_VALUE_HEADS = 2
HEAD_SIZE = 128
TOP = 4
GROUPS = 4
REQ_DEV = 2
LMIN = 64


EPS = 1e-06


def rms_scale(rows, gain):
    rows32 = rows.astype(jnp.float32)
    inverse = lax.rsqrt(jnp.mean(rows32 * rows32, axis=-1, keepdims=True) + EPS)
    return (rows32 * inverse * gain).astype(jnp.bfloat16)


def prefix_for(gathered, owners, group, per_group):
    prefix_segments = lax.dynamic_slice_in_dim(owners, group * per_group, per_group, 0)
    return gathered[prefix_segments].reshape(per_group * gathered.shape[1], 2, gathered.shape[3])


def req_shift_pairs(n_req, kind, d):
    pairs = []
    for r in range(n_req):
        if kind == "x":
            dest = (r // 4) * 4 + (r % 4 + d) % 4
        elif kind == "z":
            dest = r ^ 4
        else:
            dest = (r + 8 * d) % n_req
        pairs.append((r, dest))
    return pairs


def exp_flip(x, n_exp, bit):
    return lax.ppermute(x, "exp", [(e, e ^ bit) for e in range(n_exp)])


def gather_exp(x, axis, n_exp):
    far = exp_flip(x, n_exp, 2)
    near = exp_flip(jnp.concatenate([x, far], axis=axis), n_exp, 1)
    return jnp.concatenate([x, far, near], axis=axis)


def far_relay(x, n_req, n_exp):
    def index(r, e):
        return r * n_exp + e

    first = []
    second = []
    for r in range(n_req):
        for e in range(n_exp):
            if e % 2 == 0:
                first.append((index(r, e), index(r ^ 4, e)))
                second.append((index(r, e), index(r ^ 4, e ^ 2)))
            else:
                first.append((index(r, e), index(r ^ 4, e ^ 2)))
                second.append((index(r, e), index(r ^ 4, e)))
    hop = lax.ppermute(x, ("req", "exp"), first)
    return lax.ppermute(hop, ("req", "exp"), second)


def gather_exp_relay(x, axis, n_req, n_exp):
    far = far_relay(x, n_req, n_exp)
    near = exp_flip(jnp.concatenate([x, far], axis=axis), n_exp, 1)
    return jnp.concatenate([x, far, near], axis=axis)


def gather_prefix_near(mine, n_req):
    return jnp.stack([mine, lax.ppermute(mine, "req", req_shift_pairs(n_req, "z", 1))])


def gather_prefix_halves(along_z, n_req, n_exp):
    along_x = jnp.stack(
        [along_z] + [lax.ppermute(along_z, "req", req_shift_pairs(n_req, "x", d)) for d in (1, 2, 3)]
    )
    other_x = exp_flip(along_x, n_exp, 1)
    along_x, other_x = lax.optimization_barrier((along_x, other_x))
    from_y = jnp.stack([lax.ppermute(along_x, "req", req_shift_pairs(n_req, "y", d)) for d in (1, 2, 3)])
    other_y = exp_flip(from_y, n_exp, 1)
    mine = jnp.concatenate([along_x[None], from_y], axis=0)
    other = jnp.concatenate([other_x[None], other_y], axis=0)
    shape = (n_req,) + along_z.shape[1:]
    return mine.reshape(shape), other.reshape(shape)


def body(
    activations,
    attn_gain,
    w_query,
    key_value_weight,
    w_output,
    group_prefix_cache,
    lengths,
    groups,
    owners,
    moe_gain,
    w_gate,
    w_up,
    w_down,
    picks,
    pick_weight,
):
    req_index = lax.axis_index("req")
    expert_index = lax.axis_index("exp")
    n_req = lax.axis_size("req")
    n_exp = lax.axis_size("exp")
    tok = activations.shape[0]
    width_model = activations.shape[1]
    heads_per_shard = w_query.shape[1] // HEAD_SIZE
    key_value_head = expert_index * heads_per_shard // (QUERY_HEADS // KEY_VALUE_HEADS)

    own_piece = lax.dynamic_index_in_dim(group_prefix_cache, key_value_head, 2, keepdims=False)
    core = expert_index % 2
    far_half = expert_index // 2
    half_rows = own_piece.shape[0] // 2
    mine = lax.dynamic_slice_in_dim(own_piece, core * half_rows, half_rows, 0)
    along_z = gather_prefix_near(mine, n_req)
    ff_shard = w_gate.shape[2]
    packed = jnp.concatenate([w_gate[0].T, w_up[0].T, w_down[0]], axis=0)
    w_output_late, packed_late, along_z = lax.optimization_barrier((w_output, packed, along_z))
    halves_mine, halves_other = gather_prefix_halves(along_z, n_req, n_exp)
    w_output_far = far_relay(w_output_late, n_req, n_exp)
    w_output_near = exp_flip(jnp.concatenate([w_output, w_output_far], axis=0), n_exp, 1)
    packed_full = gather_exp_relay(packed_late.reshape(1, 3 * ff_shard, -1), 0, n_req, n_exp)
    gate_full = packed_full[:, :ff_shard].reshape(-1, packed.shape[1]).T
    up_full = packed_full[:, ff_shard : 2 * ff_shard].reshape(-1, packed.shape[1]).T
    down_full = packed_full[:, 2 * ff_shard :].reshape(-1, packed.shape[1])

    normalized_input = rms_scale(activations, attn_gain)
    query_rows = (
        jnp.dot(normalized_input, w_query, preferred_element_type=jnp.float32) * HEAD_SIZE ** (-0.5)
    ).astype(jnp.bfloat16)
    query_rows = query_rows.reshape(tok, heads_per_shard, HEAD_SIZE)
    kv_weight = lax.dynamic_slice_in_dim(key_value_weight, key_value_head * HEAD_SIZE, HEAD_SIZE, 2)
    local_key_value = jnp.einsum(
        "td,dcf->tcf", normalized_input, kv_weight, preferred_element_type=jnp.float32
    ).astype(jnp.bfloat16)

    pair = lax.dynamic_slice_in_dim(lengths, req_index * REQ_DEV, REQ_DEV, 0)
    pair_groups = lax.dynamic_slice_in_dim(groups, req_index * REQ_DEV, REQ_DEV, 0)
    per_group = n_req // GROUPS
    positions = jnp.arange(tok)
    in_first = positions < pair[0]
    my_y, my_z, my_x = req_index // 8, (req_index // 4) % 2, req_index % 4

    def prefix_of(group):
        owner = lax.dynamic_slice_in_dim(owners, group * per_group, per_group, 0)
        where = ((my_y - owner // 8) % 4) * 8 + ((my_x - owner % 4) % 4) * 2 + (my_z - (owner // 4) % 2) % 2
        part_mine = halves_mine[where]
        part_other = halves_other[where]
        rows = jnp.where(
            core == 0,
            jnp.concatenate([part_mine, part_other], axis=1),
            jnp.concatenate([part_other, part_mine], axis=1),
        )
        return rows.reshape(per_group * 2 * half_rows, 2, HEAD_SIZE)

    prefix_a = prefix_of(pair_groups[0])
    prefix_b = prefix_of(pair_groups[1])
    zero_q = jnp.zeros_like(query_rows)
    first3 = in_first[:, None, None]
    query_ab = jnp.concatenate(
        [jnp.where(first3, query_rows, zero_q), jnp.where(first3, zero_q, query_rows)], axis=-1
    )
    keys_ab = jnp.concatenate([prefix_a[:, 0], prefix_b[:, 0]], axis=-1)
    values_ab = jnp.concatenate([prefix_a[:, 1], prefix_b[:, 1]], axis=-1)
    pre_scores = jnp.einsum("thd,pd->htp", query_ab, keys_ab, preferred_element_type=jnp.float32)
    suf_scores = jnp.einsum(
        "thd,sd->hts", query_rows, local_key_value[:, 0], preferred_element_type=jnp.float32
    )
    allowed = (positions[None, :] <= positions[:, None]) & (in_first[:, None] == in_first[None, :])
    suf_scores = jnp.where(allowed[None], suf_scores, -jnp.inf)
    top = jnp.maximum(
        jnp.max(pre_scores, axis=-1, keepdims=True), jnp.max(suf_scores, axis=-1, keepdims=True)
    )
    pre_exp = jnp.exp(pre_scores - top)
    suf_exp = jnp.exp(suf_scores - top)
    denom = jnp.sum(pre_exp, axis=-1, keepdims=True) + jnp.sum(suf_exp, axis=-1, keepdims=True)
    pre_w = (pre_exp / denom).astype(jnp.bfloat16)
    suf_w = (suf_exp / denom).astype(jnp.bfloat16)
    pre_ctx_ab = jnp.einsum("htp,pd->thd", pre_w, values_ab, preferred_element_type=jnp.float32)
    pre_ctx = jnp.where(first3, pre_ctx_ab[..., :HEAD_SIZE], pre_ctx_ab[..., HEAD_SIZE:])
    suf_ctx = jnp.einsum(
        "hts,sd->thd", suf_w, local_key_value[:, 1], preferred_element_type=jnp.float32
    )
    context = (pre_ctx + suf_ctx).astype(jnp.bfloat16)
    context = context.reshape(tok, heads_per_shard * HEAD_SIZE)
    context_far = exp_flip(context, n_exp, 2)
    context_near = exp_flip(jnp.concatenate([context, context_far], axis=1), n_exp, 1)
    attn = jnp.dot(context, w_output, preferred_element_type=jnp.float32)
    attn = attn + jnp.dot(context_far, w_output_far, preferred_element_type=jnp.float32)
    attn = attn + jnp.dot(context_near, w_output_near, preferred_element_type=jnp.float32)
    resid = (activations.astype(jnp.float32) + attn).astype(jnp.bfloat16)
    normed_moe = rms_scale(resid, moe_gain)

    n_experts = n_req
    cap = min(tok, 2 * tok * TOP // n_req)
    quarter = cap // n_exp
    expert_ids = jnp.arange(n_experts, dtype=jnp.int32)
    chose = jnp.any(picks[:, :, None] == expert_ids[None, None, :], axis=1).astype(jnp.bfloat16)
    earlier = (positions[None, :] < positions[:, None]).astype(jnp.bfloat16)
    before = jnp.dot(earlier, chose, preferred_element_type=jnp.float32).astype(jnp.int32)
    pick_hot = picks[:, :, None] == expert_ids[None, None, :]
    slot = jnp.sum(jnp.where(pick_hot, before[:, None, :], 0), axis=2)
    local = slot - expert_index * quarter
    keep = (local >= 0) & (local < quarter)
    target = jnp.where(keep, picks * quarter + local, -1)
    columns = jnp.arange(n_experts * quarter, dtype=jnp.int32)
    hits = target[:, :, None] == columns[None, None, :]
    dispatch = jnp.any(hits, axis=1).astype(jnp.bfloat16)
    send = jnp.einsum("tq,td->qd", dispatch, normed_moe, preferred_element_type=jnp.float32)
    send = send.astype(jnp.bfloat16).reshape(n_experts, quarter, width_model)
    received = lax.all_to_all(send, "req", split_axis=0, concat_axis=0, tiled=True)
    rows = received.reshape(-1, width_model)
    gate = jnp.dot(rows, gate_full, preferred_element_type=jnp.float32)
    up = jnp.dot(rows, up_full, preferred_element_type=jnp.float32)
    hidden = (jnp.maximum(gate, 0.0) * up).astype(jnp.bfloat16)
    part = jnp.dot(hidden, down_full, preferred_element_type=jnp.float32).astype(jnp.bfloat16)
    part = part.reshape(n_experts, quarter, width_model)
    back = lax.all_to_all(part, "req", split_axis=0, concat_axis=0, tiled=True)
    back = back.reshape(-1, width_model)
    combine = jnp.sum(jnp.where(hits, pick_weight[:, :, None], 0.0), axis=1)
    combine_hi = combine.astype(jnp.bfloat16)
    combine_lo = (combine - combine_hi.astype(jnp.float32)).astype(jnp.bfloat16)
    mix = jnp.dot(combine_hi, back, preferred_element_type=jnp.float32) + jnp.dot(
        combine_lo, back, preferred_element_type=jnp.float32
    )
    half_tok = tok // 2
    quarter_tok = tok // 4
    keep_half = lax.dynamic_slice_in_dim(mix, core * half_tok, half_tok, 0)
    give_half = lax.dynamic_slice_in_dim(mix, (1 - core) * half_tok, half_tok, 0)
    half_sum = keep_half + exp_flip(give_half, n_exp, 1)
    keep_q = lax.dynamic_slice_in_dim(half_sum, far_half * quarter_tok, quarter_tok, 0)
    give_q = lax.dynamic_slice_in_dim(half_sum, (1 - far_half) * quarter_tok, quarter_tok, 0)
    quarter_sum = keep_q + exp_flip(give_q, n_exp, 2)
    my_rows = core * half_tok + far_half * quarter_tok
    resid_rows = lax.dynamic_slice_in_dim(resid, my_rows, quarter_tok, 0)
    out_q = (resid_rows.astype(jnp.float32) + quarter_sum).astype(jnp.bfloat16)
    other_q = exp_flip(out_q, n_exp, 2)
    out_half = jnp.where(
        far_half == 0,
        jnp.concatenate([out_q, other_q], axis=0),
        jnp.concatenate([other_q, out_q], axis=0),
    )
    other_half = exp_flip(out_half, n_exp, 1)
    return jnp.where(
        core == 0,
        jnp.concatenate([out_half, other_half], axis=0),
        jnp.concatenate([other_half, out_half], axis=0),
    )


def solution(mesh):
    return jax.shard_map(
        body,
        mesh=mesh,
        in_specs=(
            P("req", None),
            P(),
            P(None, "exp"),
            P(),
            P("exp", None),
            P("req", None, None, None),
            P(),
            P(),
            P(),
            P(),
            P("req", None, "exp"),
            P("req", None, "exp"),
            P("req", "exp", None),
            P("req", None),
            P("req", None),
        ),
        out_specs=P("req", None),
        check_vma=False,
    )
```

```python
import jax
import jax.numpy as jnp
from jax import lax
from jax.sharding import PartitionSpec as P

QUERY_HEADS = 12
KEY_VALUE_HEADS = 2
HEAD_SIZE = 128
TOP = 4
GROUPS = 4
REQ_DEV = 2
LMIN = 64


EPS = 1e-06


def rms_scale(rows, gain):
    rows32 = rows.astype(jnp.float32)
    inverse = lax.rsqrt(jnp.mean(rows32 * rows32, axis=-1, keepdims=True) + EPS)
    return (rows32 * inverse * gain).astype(jnp.bfloat16)


def prefix_for(gathered, owners, group, per_group):
    prefix_segments = lax.dynamic_slice_in_dim(owners, group * per_group, per_group, 0)
    return gathered[prefix_segments].reshape(per_group * gathered.shape[1], 2, gathered.shape[3])


def req_shift_pairs(n_req, kind, d):
    pairs = []
    for r in range(n_req):
        if kind == "x":
            dest = (r // 4) * 4 + (r % 4 + d) % 4
        elif kind == "z":
            dest = r ^ 4
        else:
            dest = (r + 8 * d) % n_req
        pairs.append((r, dest))
    return pairs


def exp_flip(x, n_exp, bit):
    return lax.ppermute(x, "exp", [(e, e ^ bit) for e in range(n_exp)])


def gather_exp(x, axis, n_exp):
    far = exp_flip(x, n_exp, 2)
    near = exp_flip(jnp.concatenate([x, far], axis=axis), n_exp, 1)
    return jnp.concatenate([x, far, near], axis=axis)


def far_relay(x, n_req, n_exp):
    def index(r, e):
        return r * n_exp + e

    first = []
    second = []
    for r in range(n_req):
        for e in range(n_exp):
            if e % 2 == 0:
                first.append((index(r, e), index(r ^ 4, e)))
                second.append((index(r, e), index(r ^ 4, e ^ 2)))
            else:
                first.append((index(r, e), index(r ^ 4, e ^ 2)))
                second.append((index(r, e), index(r ^ 4, e)))
    hop = lax.ppermute(x, ("req", "exp"), first)
    return lax.ppermute(hop, ("req", "exp"), second)


def gather_exp_relay(x, axis, n_req, n_exp):
    far = far_relay(x, n_req, n_exp)
    near = exp_flip(jnp.concatenate([x, far], axis=axis), n_exp, 1)
    return jnp.concatenate([x, far, near], axis=axis)


def gather_prefix_near(mine, n_req):
    return jnp.stack([mine, lax.ppermute(mine, "req", req_shift_pairs(n_req, "z", 1))])


def gather_prefix_halves(along_z, n_req):
    along_x = jnp.stack(
        [along_z] + [lax.ppermute(along_z, "req", req_shift_pairs(n_req, "x", d)) for d in (1, 2, 3)]
    )
    along_y = jnp.stack(
        [along_x] + [lax.ppermute(along_x, "req", req_shift_pairs(n_req, "y", d)) for d in (1, 2, 3)]
    )
    return along_y.reshape((n_req,) + along_z.shape[1:])


def body(
    activations,
    attn_gain,
    w_query,
    key_value_weight,
    w_output,
    group_prefix_cache,
    lengths,
    groups,
    owners,
    moe_gain,
    w_gate,
    w_up,
    w_down,
    picks,
    pick_weight,
):
    req_index = lax.axis_index("req")
    expert_index = lax.axis_index("exp")
    n_req = lax.axis_size("req")
    n_exp = lax.axis_size("exp")
    tok = activations.shape[0]
    width_model = activations.shape[1]
    heads_per_shard = w_query.shape[1] // HEAD_SIZE
    key_value_head = expert_index * heads_per_shard // (QUERY_HEADS // KEY_VALUE_HEADS)

    own_piece = lax.dynamic_index_in_dim(group_prefix_cache, key_value_head, 2, keepdims=False)
    core = expert_index % 2
    far_half = expert_index // 2
    half_rows = own_piece.shape[0] // 2
    mine = lax.dynamic_slice_in_dim(own_piece, core * half_rows, half_rows, 0)
    along_z = gather_prefix_near(mine, n_req)
    ff_shard = w_gate.shape[2]
    packed = jnp.concatenate([w_gate[0].T, w_up[0].T, w_down[0]], axis=0)
    w_output_late, packed_late, along_z = lax.optimization_barrier((w_output, packed, along_z))
    halves_mine = gather_prefix_halves(along_z, n_req)
    halves_other = exp_flip(halves_mine, n_exp, 1)
    w_output_full = gather_exp_relay(w_output_late, 0, n_req, n_exp)
    packed_full = gather_exp(packed_late.reshape(1, 3 * ff_shard, -1), 0, n_exp)
    gate_full = packed_full[:, :ff_shard].reshape(-1, packed.shape[1]).T
    up_full = packed_full[:, ff_shard : 2 * ff_shard].reshape(-1, packed.shape[1]).T
    down_full = packed_full[:, 2 * ff_shard :].reshape(-1, packed.shape[1])

    normalized_input = rms_scale(activations, attn_gain)
    query_rows = (
        jnp.dot(normalized_input, w_query, preferred_element_type=jnp.float32) * HEAD_SIZE ** (-0.5)
    ).astype(jnp.bfloat16)
    query_rows = query_rows.reshape(tok, heads_per_shard, HEAD_SIZE)
    kv_weight = lax.dynamic_slice_in_dim(key_value_weight, key_value_head * HEAD_SIZE, HEAD_SIZE, 2)
    local_key_value = jnp.einsum(
        "td,dcf->tcf", normalized_input, kv_weight, preferred_element_type=jnp.float32
    ).astype(jnp.bfloat16)

    pair = lax.dynamic_slice_in_dim(lengths, req_index * REQ_DEV, REQ_DEV, 0)
    pair_groups = lax.dynamic_slice_in_dim(groups, req_index * REQ_DEV, REQ_DEV, 0)
    per_group = n_req // GROUPS
    positions = jnp.arange(tok)
    in_first = positions < pair[0]
    my_y, my_z, my_x = req_index // 8, (req_index // 4) % 2, req_index % 4

    def prefix_of(group):
        owner = lax.dynamic_slice_in_dim(owners, group * per_group, per_group, 0)
        where = ((my_y - owner // 8) % 4) * 8 + ((my_x - owner % 4) % 4) * 2 + (my_z - (owner // 4) % 2) % 2
        part_mine = halves_mine[where]
        part_other = halves_other[where]
        rows = jnp.where(
            core == 0,
            jnp.concatenate([part_mine, part_other], axis=1),
            jnp.concatenate([part_other, part_mine], axis=1),
        )
        return rows.reshape(per_group * 2 * half_rows, 2, HEAD_SIZE)

    prefix_a = prefix_of(pair_groups[0])
    prefix_b = prefix_of(pair_groups[1])
    zero_q = jnp.zeros_like(query_rows)
    first3 = in_first[:, None, None]
    query_ab = jnp.concatenate(
        [jnp.where(first3, query_rows, zero_q), jnp.where(first3, zero_q, query_rows)], axis=-1
    )
    keys_ab = jnp.concatenate([prefix_a[:, 0], prefix_b[:, 0]], axis=-1)
    values_ab = jnp.concatenate([prefix_a[:, 1], prefix_b[:, 1]], axis=-1)
    pre_scores = jnp.einsum("thd,pd->htp", query_ab, keys_ab, preferred_element_type=jnp.float32)
    suf_scores = jnp.einsum(
        "thd,sd->hts", query_rows, local_key_value[:, 0], preferred_element_type=jnp.float32
    )
    allowed = (positions[None, :] <= positions[:, None]) & (in_first[:, None] == in_first[None, :])
    suf_scores = jnp.where(allowed[None], suf_scores, -jnp.inf)
    top = jnp.maximum(
        jnp.max(pre_scores, axis=-1, keepdims=True), jnp.max(suf_scores, axis=-1, keepdims=True)
    )
    pre_exp = jnp.exp(pre_scores - top)
    suf_exp = jnp.exp(suf_scores - top)
    denom = jnp.sum(pre_exp, axis=-1, keepdims=True) + jnp.sum(suf_exp, axis=-1, keepdims=True)
    pre_w = (pre_exp / denom).astype(jnp.bfloat16)
    suf_w = (suf_exp / denom).astype(jnp.bfloat16)
    pre_ctx_ab = jnp.einsum("htp,pd->thd", pre_w, values_ab, preferred_element_type=jnp.float32)
    pre_ctx = jnp.where(first3, pre_ctx_ab[..., :HEAD_SIZE], pre_ctx_ab[..., HEAD_SIZE:])
    suf_ctx = jnp.einsum(
        "hts,sd->thd", suf_w, local_key_value[:, 1], preferred_element_type=jnp.float32
    )
    context = (pre_ctx + suf_ctx).astype(jnp.bfloat16)
    context = context.reshape(tok, heads_per_shard * HEAD_SIZE)
    context_full = gather_exp(context, 1, n_exp)
    attn = jnp.dot(context_full, w_output_full, preferred_element_type=jnp.float32)
    resid = (activations.astype(jnp.float32) + attn).astype(jnp.bfloat16)
    normed_moe = rms_scale(resid, moe_gain)

    n_experts = n_req
    cap = min(tok, 2 * tok * TOP // n_req)
    quarter = cap // n_exp
    expert_ids = jnp.arange(n_experts, dtype=jnp.int32)
    chose = jnp.any(picks[:, :, None] == expert_ids[None, None, :], axis=1).astype(jnp.bfloat16)
    earlier = (positions[None, :] < positions[:, None]).astype(jnp.bfloat16)
    before = jnp.dot(earlier, chose, preferred_element_type=jnp.float32).astype(jnp.int32)
    pick_hot = picks[:, :, None] == expert_ids[None, None, :]
    slot = jnp.sum(jnp.where(pick_hot, before[:, None, :], 0), axis=2)
    local = slot - expert_index * quarter
    keep = (local >= 0) & (local < quarter)
    target = jnp.where(keep, picks * quarter + local, -1)
    columns = jnp.arange(n_experts * quarter, dtype=jnp.int32)
    hits = target[:, :, None] == columns[None, None, :]
    dispatch = jnp.any(hits, axis=1).astype(jnp.bfloat16)
    send = jnp.einsum("tq,td->qd", dispatch, normed_moe, preferred_element_type=jnp.float32)
    send = send.astype(jnp.bfloat16).reshape(n_experts, quarter, width_model)
    received = lax.all_to_all(send, "req", split_axis=0, concat_axis=0, tiled=True)
    rows = received.reshape(-1, width_model)
    gate = jnp.dot(rows, gate_full, preferred_element_type=jnp.float32)
    up = jnp.dot(rows, up_full, preferred_element_type=jnp.float32)
    hidden = (jnp.maximum(gate, 0.0) * up).astype(jnp.bfloat16)
    part = jnp.dot(hidden, down_full, preferred_element_type=jnp.float32).astype(jnp.bfloat16)
    part = part.reshape(n_experts, quarter, width_model)
    back = lax.all_to_all(part, "req", split_axis=0, concat_axis=0, tiled=True)
    back = back.reshape(-1, width_model)
    combine = jnp.sum(jnp.where(hits, pick_weight[:, :, None], 0.0), axis=1)
    combine_hi = combine.astype(jnp.bfloat16)
    combine_lo = (combine - combine_hi.astype(jnp.float32)).astype(jnp.bfloat16)
    mix = jnp.dot(combine_hi, back, preferred_element_type=jnp.float32) + jnp.dot(
        combine_lo, back, preferred_element_type=jnp.float32
    )
    half_tok = tok // 2
    quarter_tok = tok // 4
    keep_half = lax.dynamic_slice_in_dim(mix, core * half_tok, half_tok, 0)
    give_half = lax.dynamic_slice_in_dim(mix, (1 - core) * half_tok, half_tok, 0)
    half_sum = keep_half + exp_flip(give_half, n_exp, 1)
    keep_q = lax.dynamic_slice_in_dim(half_sum, far_half * quarter_tok, quarter_tok, 0)
    give_q = lax.dynamic_slice_in_dim(half_sum, (1 - far_half) * quarter_tok, quarter_tok, 0)
    quarter_sum = keep_q + exp_flip(give_q, n_exp, 2)
    my_rows = core * half_tok + far_half * quarter_tok
    resid_rows = lax.dynamic_slice_in_dim(resid, my_rows, quarter_tok, 0)
    out_q = (resid_rows.astype(jnp.float32) + quarter_sum).astype(jnp.bfloat16)
    other_q = exp_flip(out_q, n_exp, 2)
    out_half = jnp.where(
        far_half == 0,
        jnp.concatenate([out_q, other_q], axis=0),
        jnp.concatenate([other_q, out_q], axis=0),
    )
    other_half = exp_flip(out_half, n_exp, 1)
    return jnp.where(
        core == 0,
        jnp.concatenate([out_half, other_half], axis=0),
        jnp.concatenate([other_half, out_half], axis=0),
    )


def solution(mesh):
    return jax.shard_map(
        body,
        mesh=mesh,
        in_specs=(
            P("req", None),
            P(),
            P(None, "exp"),
            P(),
            P("exp", None),
            P("req", None, None, None),
            P(),
            P(),
            P(),
            P(),
            P("req", None, "exp"),
            P("req", None, "exp"),
            P("req", "exp", None),
            P("req", None),
            P("req", None),
        ),
        out_specs=P("req", None),
        check_vma=False,
    )
```

```python
import jax
import jax.numpy as jnp
from jax import lax
from jax.sharding import PartitionSpec as P

QUERY_HEADS = 12
KEY_VALUE_HEADS = 2
HEAD_SIZE = 128
TOP = 4
GROUPS = 4
REQ_DEV = 2
LMIN = 64


EPS = 1e-06


def rms_scale(rows, gain):
    rows32 = rows.astype(jnp.float32)
    inverse = lax.rsqrt(jnp.mean(rows32 * rows32, axis=-1, keepdims=True) + EPS)
    return (rows32 * inverse * gain).astype(jnp.bfloat16)


def prefix_for(gathered, owners, group, per_group):
    prefix_segments = lax.dynamic_slice_in_dim(owners, group * per_group, per_group, 0)
    return gathered[prefix_segments].reshape(per_group * gathered.shape[1], 2, gathered.shape[3])


def req_shift_pairs(n_req, kind, d):
    pairs = []
    for r in range(n_req):
        if kind == "x":
            dest = (r // 4) * 4 + (r % 4 + d) % 4
        elif kind == "z":
            dest = r ^ 4
        else:
            dest = (r + 8 * d) % n_req
        pairs.append((r, dest))
    return pairs


def exp_flip(x, n_exp, bit):
    return lax.ppermute(x, "exp", [(e, e ^ bit) for e in range(n_exp)])


def gather_exp(x, axis, n_exp):
    far = exp_flip(x, n_exp, 2)
    near = exp_flip(jnp.concatenate([x, far], axis=axis), n_exp, 1)
    return jnp.concatenate([x, far, near], axis=axis)


def far_relay(x, n_req, n_exp):
    def index(r, e):
        return r * n_exp + e

    first = []
    second = []
    for r in range(n_req):
        for e in range(n_exp):
            if e % 2 == 0:
                first.append((index(r, e), index(r ^ 4, e)))
                second.append((index(r, e), index(r ^ 4, e ^ 2)))
            else:
                first.append((index(r, e), index(r ^ 4, e ^ 2)))
                second.append((index(r, e), index(r ^ 4, e)))
    hop = lax.ppermute(x, ("req", "exp"), first)
    return lax.ppermute(hop, ("req", "exp"), second)


def gather_exp_relay(x, axis, n_req, n_exp):
    far = far_relay(x, n_req, n_exp)
    near = exp_flip(jnp.concatenate([x, far], axis=axis), n_exp, 1)
    return jnp.concatenate([x, far, near], axis=axis)


def gather_prefix_near(mine, n_req):
    return jnp.stack([mine, lax.ppermute(mine, "req", req_shift_pairs(n_req, "z", 1))])


def gather_prefix_halves(along_z, n_req):
    along_x = jnp.stack(
        [along_z] + [lax.ppermute(along_z, "req", req_shift_pairs(n_req, "x", d)) for d in (1, 2, 3)]
    )
    along_y = jnp.stack(
        [along_x] + [lax.ppermute(along_x, "req", req_shift_pairs(n_req, "y", d)) for d in (1, 2, 3)]
    )
    return along_y.reshape((n_req,) + along_z.shape[1:])


def body(
    activations,
    attn_gain,
    w_query,
    key_value_weight,
    w_output,
    group_prefix_cache,
    lengths,
    groups,
    owners,
    moe_gain,
    w_gate,
    w_up,
    w_down,
    picks,
    pick_weight,
):
    req_index = lax.axis_index("req")
    expert_index = lax.axis_index("exp")
    n_req = lax.axis_size("req")
    n_exp = lax.axis_size("exp")
    tok = activations.shape[0]
    width_model = activations.shape[1]
    heads_per_shard = w_query.shape[1] // HEAD_SIZE
    key_value_head = expert_index * heads_per_shard // (QUERY_HEADS // KEY_VALUE_HEADS)

    own_piece = lax.dynamic_index_in_dim(group_prefix_cache, key_value_head, 2, keepdims=False)
    core = expert_index % 2
    far_half = expert_index // 2
    half_rows = own_piece.shape[0] // 2
    mine = lax.dynamic_slice_in_dim(own_piece, core * half_rows, half_rows, 0)
    along_z = gather_prefix_near(mine, n_req)
    ff_shard = w_gate.shape[2]
    packed = jnp.concatenate([w_gate[0].T, w_up[0].T, w_down[0]], axis=0)
    w_output_late, packed_late, along_z = lax.optimization_barrier((w_output, packed, along_z))
    halves_mine = gather_prefix_halves(along_z, n_req)
    halves_other = exp_flip(halves_mine, n_exp, 1)
    w_output_full = gather_exp_relay(w_output_late, 0, n_req, n_exp)
    packed_full = gather_exp_relay(packed_late.reshape(1, 3 * ff_shard, -1), 0, n_req, n_exp)
    gate_full = packed_full[:, :ff_shard].reshape(-1, packed.shape[1]).T
    up_full = packed_full[:, ff_shard : 2 * ff_shard].reshape(-1, packed.shape[1]).T
    down_full = packed_full[:, 2 * ff_shard :].reshape(-1, packed.shape[1])

    normalized_input = rms_scale(activations, attn_gain)
    query_rows = (
        jnp.dot(normalized_input, w_query, preferred_element_type=jnp.float32) * HEAD_SIZE ** (-0.5)
    ).astype(jnp.bfloat16)
    query_rows = query_rows.reshape(tok, heads_per_shard, HEAD_SIZE)
    kv_weight = lax.dynamic_slice_in_dim(key_value_weight, key_value_head * HEAD_SIZE, HEAD_SIZE, 2)
    local_key_value = jnp.einsum(
        "td,dcf->tcf", normalized_input, kv_weight, preferred_element_type=jnp.float32
    ).astype(jnp.bfloat16)

    pair = lax.dynamic_slice_in_dim(lengths, req_index * REQ_DEV, REQ_DEV, 0)
    pair_groups = lax.dynamic_slice_in_dim(groups, req_index * REQ_DEV, REQ_DEV, 0)
    per_group = n_req // GROUPS
    positions = jnp.arange(tok)
    in_first = positions < pair[0]
    my_y, my_z, my_x = req_index // 8, (req_index // 4) % 2, req_index % 4

    def prefix_of(group):
        owner = lax.dynamic_slice_in_dim(owners, group * per_group, per_group, 0)
        where = ((my_y - owner // 8) % 4) * 8 + ((my_x - owner % 4) % 4) * 2 + (my_z - (owner // 4) % 2) % 2
        part_mine = halves_mine[where]
        part_other = halves_other[where]
        rows = jnp.where(
            core == 0,
            jnp.concatenate([part_mine, part_other], axis=1),
            jnp.concatenate([part_other, part_mine], axis=1),
        )
        return rows.reshape(per_group * 2 * half_rows, 2, HEAD_SIZE)

    prefix_a = prefix_of(pair_groups[0])
    prefix_b = prefix_of(pair_groups[1])
    zero_q = jnp.zeros_like(query_rows)
    first3 = in_first[:, None, None]
    query_ab = jnp.concatenate(
        [jnp.where(first3, query_rows, zero_q), jnp.where(first3, zero_q, query_rows)], axis=-1
    )
    keys_ab = jnp.concatenate([prefix_a[:, 0], prefix_b[:, 0]], axis=-1)
    values_ab = jnp.concatenate([prefix_a[:, 1], prefix_b[:, 1]], axis=-1)
    pre_scores = jnp.einsum("thd,pd->htp", query_ab, keys_ab, preferred_element_type=jnp.float32)
    suf_scores = jnp.einsum(
        "thd,sd->hts", query_rows, local_key_value[:, 0], preferred_element_type=jnp.float32
    )
    allowed = (positions[None, :] <= positions[:, None]) & (in_first[:, None] == in_first[None, :])
    suf_scores = jnp.where(allowed[None], suf_scores, -jnp.inf)
    top = jnp.maximum(
        jnp.max(pre_scores, axis=-1, keepdims=True), jnp.max(suf_scores, axis=-1, keepdims=True)
    )
    pre_exp = jnp.exp(pre_scores - top)
    suf_exp = jnp.exp(suf_scores - top)
    denom = jnp.sum(pre_exp, axis=-1, keepdims=True) + jnp.sum(suf_exp, axis=-1, keepdims=True)
    pre_w = (pre_exp / denom).astype(jnp.bfloat16)
    suf_w = (suf_exp / denom).astype(jnp.bfloat16)
    pre_ctx_ab = jnp.einsum("htp,pd->thd", pre_w, values_ab, preferred_element_type=jnp.float32)
    pre_ctx = jnp.where(first3, pre_ctx_ab[..., :HEAD_SIZE], pre_ctx_ab[..., HEAD_SIZE:])
    suf_ctx = jnp.einsum(
        "hts,sd->thd", suf_w, local_key_value[:, 1], preferred_element_type=jnp.float32
    )
    context = (pre_ctx + suf_ctx).astype(jnp.bfloat16)
    context = context.reshape(tok, heads_per_shard * HEAD_SIZE)
    context_full = gather_exp(context, 1, n_exp)
    attn = jnp.dot(context_full, w_output_full, preferred_element_type=jnp.float32)
    resid = (activations.astype(jnp.float32) + attn).astype(jnp.bfloat16)
    normed_moe = rms_scale(resid, moe_gain)

    n_experts = n_req
    cap = min(tok, 2 * tok * TOP // n_req)
    quarter = cap // n_exp
    expert_ids = jnp.arange(n_experts, dtype=jnp.int32)
    chose = jnp.any(picks[:, :, None] == expert_ids[None, None, :], axis=1).astype(jnp.bfloat16)
    earlier = (positions[None, :] < positions[:, None]).astype(jnp.bfloat16)
    before = jnp.dot(earlier, chose, preferred_element_type=jnp.float32).astype(jnp.int32)
    pick_hot = picks[:, :, None] == expert_ids[None, None, :]
    slot = jnp.sum(jnp.where(pick_hot, before[:, None, :], 0), axis=2)
    local = slot - expert_index * quarter
    keep = (local >= 0) & (local < quarter)
    target = jnp.where(keep, picks * quarter + local, -1)
    columns = jnp.arange(n_experts * quarter, dtype=jnp.int32)
    hits = target[:, :, None] == columns[None, None, :]
    dispatch = jnp.any(hits, axis=1).astype(jnp.bfloat16)
    send = jnp.einsum("tq,td->qd", dispatch, normed_moe, preferred_element_type=jnp.float32)
    send = send.astype(jnp.bfloat16).reshape(n_experts, quarter, width_model)
    received = lax.all_to_all(send, "req", split_axis=0, concat_axis=0, tiled=True)
    rows = received.reshape(-1, width_model)
    gate = jnp.dot(rows, gate_full, preferred_element_type=jnp.float32)
    up = jnp.dot(rows, up_full, preferred_element_type=jnp.float32)
    hidden = (jnp.maximum(gate, 0.0) * up).astype(jnp.bfloat16)
    part = jnp.dot(hidden, down_full, preferred_element_type=jnp.float32).astype(jnp.bfloat16)
    part = part.reshape(n_experts, quarter, width_model)
    back = lax.all_to_all(part, "req", split_axis=0, concat_axis=0, tiled=True)
    back = back.reshape(-1, width_model)
    combine = jnp.sum(jnp.where(hits, pick_weight[:, :, None], 0.0), axis=1)
    half_tok = tok // 2
    quarter_tok = tok // 4

    def mix_rows(first_row, count):
        weights = lax.dynamic_slice_in_dim(combine, first_row, count, 0)
        weights_hi = weights.astype(jnp.bfloat16)
        weights_lo = (weights - weights_hi.astype(jnp.float32)).astype(jnp.bfloat16)
        return jnp.dot(weights_hi, back, preferred_element_type=jnp.float32) + jnp.dot(
            weights_lo, back, preferred_element_type=jnp.float32
        )

    give_half = mix_rows((1 - core) * half_tok, half_tok)
    got_half = exp_flip(give_half, n_exp, 1)
    my_half = core * half_tok
    give_q = mix_rows(my_half + (1 - far_half) * quarter_tok, quarter_tok) + lax.dynamic_slice_in_dim(
        got_half, (1 - far_half) * quarter_tok, quarter_tok, 0
    )
    got_q = exp_flip(give_q, n_exp, 2)
    my_rows = my_half + far_half * quarter_tok
    keep_q = mix_rows(my_rows, quarter_tok) + lax.dynamic_slice_in_dim(
        got_half, far_half * quarter_tok, quarter_tok, 0
    )
    quarter_sum = keep_q + got_q
    resid_rows = lax.dynamic_slice_in_dim(resid, my_rows, quarter_tok, 0)
    out_q = (resid_rows.astype(jnp.float32) + quarter_sum).astype(jnp.bfloat16)
    other_q = exp_flip(out_q, n_exp, 2)
    out_half = jnp.zeros((half_tok, width_model), jnp.bfloat16)
    out_half = lax.dynamic_update_slice_in_dim(out_half, out_q, far_half * quarter_tok, 0)
    out_half = lax.dynamic_update_slice_in_dim(out_half, other_q, (1 - far_half) * quarter_tok, 0)
    other_half = exp_flip(out_half, n_exp, 1)
    out = jnp.zeros((tok, width_model), jnp.bfloat16)
    out = lax.dynamic_update_slice_in_dim(out, out_half, my_half, 0)
    return lax.dynamic_update_slice_in_dim(out, other_half, (1 - core) * half_tok, 0)


def solution(mesh):
    return jax.shard_map(
        body,
        mesh=mesh,
        in_specs=(
            P("req", None),
            P(),
            P(None, "exp"),
            P(),
            P("exp", None),
            P("req", None, None, None),
            P(),
            P(),
            P(),
            P(),
            P("req", None, "exp"),
            P("req", None, "exp"),
            P("req", "exp", None),
            P("req", None),
            P("req", None),
        ),
        out_specs=P("req", None),
        check_vma=False,
    )
```

```python
import jax
import jax.numpy as jnp
from jax import lax
from jax.sharding import PartitionSpec as P

QUERY_HEADS = 12
KEY_VALUE_HEADS = 2
HEAD_SIZE = 128
TOP = 4
GROUPS = 4
REQ_DEV = 2
LMIN = 64


EPS = 1e-06


def rms_scale(rows, gain):
    rows32 = rows.astype(jnp.float32)
    inverse = lax.rsqrt(jnp.mean(rows32 * rows32, axis=-1, keepdims=True) + EPS)
    return (rows32 * inverse * gain).astype(jnp.bfloat16)


def prefix_for(gathered, owners, group, per_group):
    prefix_segments = lax.dynamic_slice_in_dim(owners, group * per_group, per_group, 0)
    return gathered[prefix_segments].reshape(per_group * gathered.shape[1], 2, gathered.shape[3])


def req_shift_pairs(n_req, kind, d):
    pairs = []
    for r in range(n_req):
        if kind == "x":
            dest = (r // 4) * 4 + (r % 4 + d) % 4
        elif kind == "z":
            dest = r ^ 4
        else:
            dest = (r + 8 * d) % n_req
        pairs.append((r, dest))
    return pairs


def exp_flip(x, n_exp, bit):
    return lax.ppermute(x, "exp", [(e, e ^ bit) for e in range(n_exp)])


def gather_exp(x, axis, n_exp):
    far = exp_flip(x, n_exp, 2)
    near = exp_flip(jnp.concatenate([x, far], axis=axis), n_exp, 1)
    return jnp.concatenate([x, far, near], axis=axis)


def far_relay(x, n_req, n_exp):
    def index(r, e):
        return r * n_exp + e

    first = []
    second = []
    for r in range(n_req):
        for e in range(n_exp):
            if e % 2 == 0:
                first.append((index(r, e), index(r ^ 4, e)))
                second.append((index(r, e), index(r ^ 4, e ^ 2)))
            else:
                first.append((index(r, e), index(r ^ 4, e ^ 2)))
                second.append((index(r, e), index(r ^ 4, e)))
    hop = lax.ppermute(x, ("req", "exp"), first)
    return lax.ppermute(hop, ("req", "exp"), second)


def gather_exp_relay(x, axis, n_req, n_exp):
    far = far_relay(x, n_req, n_exp)
    near = exp_flip(jnp.concatenate([x, far], axis=axis), n_exp, 1)
    return jnp.concatenate([x, far, near], axis=axis)


def gather_prefix_near(mine, n_req):
    return jnp.stack([mine, lax.ppermute(mine, "req", req_shift_pairs(n_req, "z", 1))])


def gather_prefix_halves(along_z, n_req):
    along_x = jnp.stack(
        [along_z] + [lax.ppermute(along_z, "req", req_shift_pairs(n_req, "x", d)) for d in (1, 2, 3)]
    )
    along_y = jnp.stack(
        [along_x] + [lax.ppermute(along_x, "req", req_shift_pairs(n_req, "y", d)) for d in (1, 2, 3)]
    )
    return along_y.reshape((n_req,) + along_z.shape[1:])


def body(
    activations,
    attn_gain,
    w_query,
    key_value_weight,
    w_output,
    group_prefix_cache,
    lengths,
    groups,
    owners,
    moe_gain,
    w_gate,
    w_up,
    w_down,
    picks,
    pick_weight,
):
    req_index = lax.axis_index("req")
    expert_index = lax.axis_index("exp")
    n_req = lax.axis_size("req")
    n_exp = lax.axis_size("exp")
    tok = activations.shape[0]
    width_model = activations.shape[1]
    heads_per_shard = w_query.shape[1] // HEAD_SIZE
    key_value_head = expert_index * heads_per_shard // (QUERY_HEADS // KEY_VALUE_HEADS)

    own_piece = lax.dynamic_index_in_dim(group_prefix_cache, key_value_head, 2, keepdims=False)
    core = expert_index % 2
    far_half = expert_index // 2
    half_rows = own_piece.shape[0] // 2
    mine = lax.dynamic_slice_in_dim(own_piece, core * half_rows, half_rows, 0)
    along_z = gather_prefix_near(mine, n_req)
    ff_shard = w_gate.shape[2]
    packed = jnp.concatenate([w_gate[0].T, w_up[0].T, w_down[0]], axis=0)
    w_output_late, packed_late, along_z = lax.optimization_barrier((w_output, packed, along_z))
    halves_mine = gather_prefix_halves(along_z, n_req)
    halves_other = exp_flip(halves_mine, n_exp, 1)
    w_output_full = gather_exp_relay(w_output_late, 0, n_req, n_exp)
    packed_full = gather_exp_relay(packed_late.reshape(1, 3 * ff_shard, -1), 0, n_req, n_exp)
    gate_full = packed_full[:, :ff_shard].reshape(-1, packed.shape[1]).T
    up_full = packed_full[:, ff_shard : 2 * ff_shard].reshape(-1, packed.shape[1]).T
    down_full = packed_full[:, 2 * ff_shard :].reshape(-1, packed.shape[1])

    normalized_input = rms_scale(activations, attn_gain)
    query_rows = (
        jnp.dot(normalized_input, w_query, preferred_element_type=jnp.float32) * HEAD_SIZE ** (-0.5)
    ).astype(jnp.bfloat16)
    query_rows = query_rows.reshape(tok, heads_per_shard, HEAD_SIZE)
    kv_weight = lax.dynamic_slice_in_dim(key_value_weight, key_value_head * HEAD_SIZE, HEAD_SIZE, 2)
    local_key_value = jnp.einsum(
        "td,dcf->tcf", normalized_input, kv_weight, preferred_element_type=jnp.float32
    ).astype(jnp.bfloat16)

    pair = lax.dynamic_slice_in_dim(lengths, req_index * REQ_DEV, REQ_DEV, 0)
    pair_groups = lax.dynamic_slice_in_dim(groups, req_index * REQ_DEV, REQ_DEV, 0)
    per_group = n_req // GROUPS
    positions = jnp.arange(tok)
    in_first = positions < pair[0]
    my_y, my_z, my_x = req_index // 8, (req_index // 4) % 2, req_index % 4

    def prefix_of(group):
        owner = lax.dynamic_slice_in_dim(owners, group * per_group, per_group, 0)
        where = ((my_y - owner // 8) % 4) * 8 + ((my_x - owner % 4) % 4) * 2 + (my_z - (owner // 4) % 2) % 2
        part_mine = halves_mine[where]
        part_other = halves_other[where]
        rows = jnp.concatenate([part_mine, part_other], axis=1)
        return rows.reshape(per_group * 2 * half_rows, 2, HEAD_SIZE)

    prefix_a = prefix_of(pair_groups[0])
    prefix_b = prefix_of(pair_groups[1])
    zero_q = jnp.zeros_like(query_rows)
    first3 = in_first[:, None, None]
    query_ab = jnp.concatenate(
        [jnp.where(first3, query_rows, zero_q), jnp.where(first3, zero_q, query_rows)], axis=-1
    )
    keys_ab = jnp.concatenate([prefix_a[:, 0], prefix_b[:, 0]], axis=-1)
    values_ab = jnp.concatenate([prefix_a[:, 1], prefix_b[:, 1]], axis=-1)
    pre_scores = jnp.einsum("thd,pd->htp", query_ab, keys_ab, preferred_element_type=jnp.float32)
    suf_scores = jnp.einsum(
        "thd,sd->hts", query_rows, local_key_value[:, 0], preferred_element_type=jnp.float32
    )
    allowed = (positions[None, :] <= positions[:, None]) & (in_first[:, None] == in_first[None, :])
    suf_scores = jnp.where(allowed[None], suf_scores, -jnp.inf)
    top = jnp.maximum(
        jnp.max(pre_scores, axis=-1, keepdims=True), jnp.max(suf_scores, axis=-1, keepdims=True)
    )
    pre_exp = jnp.exp(pre_scores - top)
    suf_exp = jnp.exp(suf_scores - top)
    denom = jnp.sum(pre_exp, axis=-1, keepdims=True) + jnp.sum(suf_exp, axis=-1, keepdims=True)
    pre_w = (pre_exp / denom).astype(jnp.bfloat16)
    suf_w = (suf_exp / denom).astype(jnp.bfloat16)
    pre_ctx_ab = jnp.einsum("htp,pd->thd", pre_w, values_ab, preferred_element_type=jnp.float32)
    pre_ctx = jnp.where(first3, pre_ctx_ab[..., :HEAD_SIZE], pre_ctx_ab[..., HEAD_SIZE:])
    suf_ctx = jnp.einsum(
        "hts,sd->thd", suf_w, local_key_value[:, 1], preferred_element_type=jnp.float32
    )
    context = (pre_ctx + suf_ctx).astype(jnp.bfloat16)
    context = context.reshape(tok, heads_per_shard * HEAD_SIZE)
    context_full = gather_exp(context, 1, n_exp)
    attn = jnp.dot(context_full, w_output_full, preferred_element_type=jnp.float32)
    resid = (activations.astype(jnp.float32) + attn).astype(jnp.bfloat16)
    normed_moe = rms_scale(resid, moe_gain)

    n_experts = n_req
    cap = min(tok, 2 * tok * TOP // n_req)
    quarter = cap // n_exp
    expert_ids = jnp.arange(n_experts, dtype=jnp.int32)
    chose = jnp.any(picks[:, :, None] == expert_ids[None, None, :], axis=1).astype(jnp.bfloat16)
    earlier = (positions[None, :] < positions[:, None]).astype(jnp.bfloat16)
    before = jnp.dot(earlier, chose, preferred_element_type=jnp.float32).astype(jnp.int32)
    pick_hot = picks[:, :, None] == expert_ids[None, None, :]
    slot = jnp.sum(jnp.where(pick_hot, before[:, None, :], 0), axis=2)
    local = slot - expert_index * quarter
    keep = (local >= 0) & (local < quarter)
    target = jnp.where(keep, picks * quarter + local, -1)
    columns = jnp.arange(n_experts * quarter, dtype=jnp.int32)
    hits = target[:, :, None] == columns[None, None, :]
    dispatch = jnp.any(hits, axis=1).astype(jnp.bfloat16)
    send = jnp.einsum("tq,td->qd", dispatch, normed_moe, preferred_element_type=jnp.float32)
    send = send.astype(jnp.bfloat16).reshape(n_experts, quarter, width_model)
    received = lax.all_to_all(send, "req", split_axis=0, concat_axis=0, tiled=True)
    rows = received.reshape(-1, width_model)
    gate = jnp.dot(rows, gate_full, preferred_element_type=jnp.float32)
    up = jnp.dot(rows, up_full, preferred_element_type=jnp.float32)
    hidden = (jnp.maximum(gate, 0.0) * up).astype(jnp.bfloat16)
    part = jnp.dot(hidden, down_full, preferred_element_type=jnp.float32).astype(jnp.bfloat16)
    part = part.reshape(n_experts, quarter, width_model)
    back = lax.all_to_all(part, "req", split_axis=0, concat_axis=0, tiled=True)
    back = back.reshape(-1, width_model)
    combine = jnp.sum(jnp.where(hits, pick_weight[:, :, None], 0.0), axis=1)
    half_tok = tok // 2
    quarter_tok = tok // 4

    def mix_rows(first_row, count):
        weights = lax.dynamic_slice_in_dim(combine, first_row, count, 0)
        weights_hi = weights.astype(jnp.bfloat16)
        weights_lo = (weights - weights_hi.astype(jnp.float32)).astype(jnp.bfloat16)
        return jnp.dot(weights_hi, back, preferred_element_type=jnp.float32) + jnp.dot(
            weights_lo, back, preferred_element_type=jnp.float32
        )

    give_half = mix_rows((1 - core) * half_tok, half_tok)
    got_half = exp_flip(give_half, n_exp, 1)
    my_half = core * half_tok
    give_q = mix_rows(my_half + (1 - far_half) * quarter_tok, quarter_tok) + lax.dynamic_slice_in_dim(
        got_half, (1 - far_half) * quarter_tok, quarter_tok, 0
    )
    got_q = exp_flip(give_q, n_exp, 2)
    my_rows = my_half + far_half * quarter_tok
    keep_q = mix_rows(my_rows, quarter_tok) + lax.dynamic_slice_in_dim(
        got_half, far_half * quarter_tok, quarter_tok, 0
    )
    quarter_sum = keep_q + got_q
    resid_rows = lax.dynamic_slice_in_dim(resid, my_rows, quarter_tok, 0)
    out_q = (resid_rows.astype(jnp.float32) + quarter_sum).astype(jnp.bfloat16)
    other_q = exp_flip(out_q, n_exp, 2)
    out_half = jnp.zeros((half_tok, width_model), jnp.bfloat16)
    out_half = lax.dynamic_update_slice_in_dim(out_half, out_q, far_half * quarter_tok, 0)
    out_half = lax.dynamic_update_slice_in_dim(out_half, other_q, (1 - far_half) * quarter_tok, 0)
    other_half = exp_flip(out_half, n_exp, 1)
    out = jnp.zeros((tok, width_model), jnp.bfloat16)
    out = lax.dynamic_update_slice_in_dim(out, out_half, my_half, 0)
    return lax.dynamic_update_slice_in_dim(out, other_half, (1 - core) * half_tok, 0)


def solution(mesh):
    return jax.shard_map(
        body,
        mesh=mesh,
        in_specs=(
            P("req", None),
            P(),
            P(None, "exp"),
            P(),
            P("exp", None),
            P("req", None, None, None),
            P(),
            P(),
            P(),
            P(),
            P("req", None, "exp"),
            P("req", None, "exp"),
            P("req", "exp", None),
            P("req", None),
            P("req", None),
        ),
        out_specs=P("req", None),
        check_vma=False,
    )
```

```python
import jax
import jax.numpy as jnp
from jax import lax
from jax.sharding import PartitionSpec as P

QUERY_HEADS = 12
KEY_VALUE_HEADS = 2
HEAD_SIZE = 128
TOP = 4
GROUPS = 4
REQ_DEV = 2
LMIN = 64


EPS = 1e-06


def rms_scale(rows, gain):
    rows32 = rows.astype(jnp.float32)
    inverse = lax.rsqrt(jnp.mean(rows32 * rows32, axis=-1, keepdims=True) + EPS)
    return (rows32 * inverse * gain).astype(jnp.bfloat16)


def prefix_for(gathered, owners, group, per_group):
    prefix_segments = lax.dynamic_slice_in_dim(owners, group * per_group, per_group, 0)
    return gathered[prefix_segments].reshape(per_group * gathered.shape[1], 2, gathered.shape[3])


def req_shift_pairs(n_req, kind, d):
    pairs = []
    for r in range(n_req):
        if kind == "x":
            dest = (r // 4) * 4 + (r % 4 + d) % 4
        elif kind == "z":
            dest = r ^ 4
        else:
            dest = (r + 8 * d) % n_req
        pairs.append((r, dest))
    return pairs


def exp_flip(x, n_exp, bit):
    return lax.ppermute(x, "exp", [(e, e ^ bit) for e in range(n_exp)])


def gather_exp(x, axis, n_exp):
    far = exp_flip(x, n_exp, 2)
    near = exp_flip(jnp.concatenate([x, far], axis=axis), n_exp, 1)
    return jnp.concatenate([x, far, near], axis=axis)


def far_relay(x, n_req, n_exp):
    def index(r, e):
        return r * n_exp + e

    first = []
    second = []
    for r in range(n_req):
        for e in range(n_exp):
            if e % 2 == 0:
                first.append((index(r, e), index(r ^ 4, e)))
                second.append((index(r, e), index(r ^ 4, e ^ 2)))
            else:
                first.append((index(r, e), index(r ^ 4, e ^ 2)))
                second.append((index(r, e), index(r ^ 4, e)))
    hop = lax.ppermute(x, ("req", "exp"), first)
    return lax.ppermute(hop, ("req", "exp"), second)


def gather_exp_relay(x, axis, n_req, n_exp):
    far = far_relay(x, n_req, n_exp)
    near = exp_flip(jnp.concatenate([x, far], axis=axis), n_exp, 1)
    return jnp.concatenate([x, far, near], axis=axis)


def gather_prefix_near(mine, n_req):
    return jnp.stack([mine, lax.ppermute(mine, "req", req_shift_pairs(n_req, "z", 1))])


def gather_prefix_halves(along_z, n_req):
    along_x = jnp.stack(
        [along_z] + [lax.ppermute(along_z, "req", req_shift_pairs(n_req, "x", d)) for d in (1, 2, 3)]
    )
    along_y = jnp.stack(
        [along_x] + [lax.ppermute(along_x, "req", req_shift_pairs(n_req, "y", d)) for d in (1, 2, 3)]
    )
    return along_y.reshape((n_req,) + along_z.shape[1:])


def body(
    activations,
    attn_gain,
    w_query,
    key_value_weight,
    w_output,
    group_prefix_cache,
    lengths,
    groups,
    owners,
    moe_gain,
    w_gate,
    w_up,
    w_down,
    picks,
    pick_weight,
):
    req_index = lax.axis_index("req")
    expert_index = lax.axis_index("exp")
    n_req = lax.axis_size("req")
    n_exp = lax.axis_size("exp")
    tok = activations.shape[0]
    width_model = activations.shape[1]
    heads_per_shard = w_query.shape[1] // HEAD_SIZE
    key_value_head = expert_index * heads_per_shard // (QUERY_HEADS // KEY_VALUE_HEADS)

    own_piece = lax.dynamic_index_in_dim(group_prefix_cache, key_value_head, 2, keepdims=False)
    core = expert_index % 2
    far_half = expert_index // 2
    half_rows = own_piece.shape[0] // 2
    mine = lax.dynamic_slice_in_dim(own_piece, core * half_rows, half_rows, 0)
    along_z = gather_prefix_near(mine, n_req)
    ff_shard = w_gate.shape[2]
    packed = jnp.concatenate([w_gate[0].T, w_up[0].T, w_down[0]], axis=0)
    w_output_late, packed_late, along_z = lax.optimization_barrier((w_output, packed, along_z))
    halves_mine = gather_prefix_halves(along_z, n_req)
    halves_other = exp_flip(halves_mine, n_exp, 1)
    w_output_far = far_relay(w_output_late, n_req, n_exp)
    w_output_near = exp_flip(jnp.concatenate([w_output, w_output_far], axis=0), n_exp, 1)
    packed_full = gather_exp_relay(packed_late.reshape(1, 3 * ff_shard, -1), 0, n_req, n_exp)
    gate_full = packed_full[:, :ff_shard].reshape(-1, packed.shape[1]).T
    up_full = packed_full[:, ff_shard : 2 * ff_shard].reshape(-1, packed.shape[1]).T
    down_full = packed_full[:, 2 * ff_shard :].reshape(-1, packed.shape[1])

    normalized_input = rms_scale(activations, attn_gain)
    query_rows = (
        jnp.dot(normalized_input, w_query, preferred_element_type=jnp.float32) * HEAD_SIZE ** (-0.5)
    ).astype(jnp.bfloat16)
    query_rows = query_rows.reshape(tok, heads_per_shard, HEAD_SIZE)
    kv_weight = lax.dynamic_slice_in_dim(key_value_weight, key_value_head * HEAD_SIZE, HEAD_SIZE, 2)
    local_key_value = jnp.einsum(
        "td,dcf->tcf", normalized_input, kv_weight, preferred_element_type=jnp.float32
    ).astype(jnp.bfloat16)

    pair = lax.dynamic_slice_in_dim(lengths, req_index * REQ_DEV, REQ_DEV, 0)
    pair_groups = lax.dynamic_slice_in_dim(groups, req_index * REQ_DEV, REQ_DEV, 0)
    per_group = n_req // GROUPS
    positions = jnp.arange(tok)
    in_first = positions < pair[0]
    my_y, my_z, my_x = req_index // 8, (req_index // 4) % 2, req_index % 4

    def prefix_of(group):
        owner = lax.dynamic_slice_in_dim(owners, group * per_group, per_group, 0)
        where = ((my_y - owner // 8) % 4) * 8 + ((my_x - owner % 4) % 4) * 2 + (my_z - (owner // 4) % 2) % 2
        part_mine = halves_mine[where]
        part_other = halves_other[where]
        rows = jnp.concatenate([part_mine, part_other], axis=1)
        return rows.reshape(per_group * 2 * half_rows, 2, HEAD_SIZE)

    prefix_a = prefix_of(pair_groups[0])
    prefix_b = prefix_of(pair_groups[1])
    zero_q = jnp.zeros_like(query_rows)
    first3 = in_first[:, None, None]
    query_ab = jnp.concatenate(
        [jnp.where(first3, query_rows, zero_q), jnp.where(first3, zero_q, query_rows)], axis=-1
    )
    keys_ab = jnp.concatenate([prefix_a[:, 0], prefix_b[:, 0]], axis=-1)
    values_ab = jnp.concatenate([prefix_a[:, 1], prefix_b[:, 1]], axis=-1)
    pre_scores = jnp.einsum("thd,pd->htp", query_ab, keys_ab, preferred_element_type=jnp.float32)
    suf_scores = jnp.einsum(
        "thd,sd->hts", query_rows, local_key_value[:, 0], preferred_element_type=jnp.float32
    )
    allowed = (positions[None, :] <= positions[:, None]) & (in_first[:, None] == in_first[None, :])
    suf_scores = jnp.where(allowed[None], suf_scores, -jnp.inf)
    top = jnp.maximum(
        jnp.max(pre_scores, axis=-1, keepdims=True), jnp.max(suf_scores, axis=-1, keepdims=True)
    )
    pre_exp = jnp.exp(pre_scores - top)
    suf_exp = jnp.exp(suf_scores - top)
    denom = jnp.sum(pre_exp, axis=-1, keepdims=True) + jnp.sum(suf_exp, axis=-1, keepdims=True)
    pre_w = (pre_exp / denom).astype(jnp.bfloat16)
    suf_w = (suf_exp / denom).astype(jnp.bfloat16)
    pre_ctx_ab = jnp.einsum("htp,pd->thd", pre_w, values_ab, preferred_element_type=jnp.float32)
    pre_ctx = jnp.where(first3, pre_ctx_ab[..., :HEAD_SIZE], pre_ctx_ab[..., HEAD_SIZE:])
    suf_ctx = jnp.einsum(
        "hts,sd->thd", suf_w, local_key_value[:, 1], preferred_element_type=jnp.float32
    )
    context = (pre_ctx + suf_ctx).astype(jnp.bfloat16)
    context = context.reshape(tok, heads_per_shard * HEAD_SIZE)
    context_far = exp_flip(context, n_exp, 2)
    context_near = exp_flip(jnp.concatenate([context, context_far], axis=1), n_exp, 1)
    attn = jnp.dot(context, w_output, preferred_element_type=jnp.float32)
    attn = attn + jnp.dot(context_far, w_output_far, preferred_element_type=jnp.float32)
    attn = attn + jnp.dot(context_near, w_output_near, preferred_element_type=jnp.float32)
    resid = (activations.astype(jnp.float32) + attn).astype(jnp.bfloat16)
    normed_moe = rms_scale(resid, moe_gain)

    n_experts = n_req
    cap = min(tok, 2 * tok * TOP // n_req)
    quarter = cap // n_exp
    expert_ids = jnp.arange(n_experts, dtype=jnp.int32)
    chose = jnp.any(picks[:, :, None] == expert_ids[None, None, :], axis=1).astype(jnp.bfloat16)
    earlier = (positions[None, :] < positions[:, None]).astype(jnp.bfloat16)
    before = jnp.dot(earlier, chose, preferred_element_type=jnp.float32).astype(jnp.int32)
    pick_hot = picks[:, :, None] == expert_ids[None, None, :]
    slot = jnp.sum(jnp.where(pick_hot, before[:, None, :], 0), axis=2)
    local = slot - expert_index * quarter
    keep = (local >= 0) & (local < quarter)
    target = jnp.where(keep, picks * quarter + local, -1)
    columns = jnp.arange(n_experts * quarter, dtype=jnp.int32)
    hits = target[:, :, None] == columns[None, None, :]
    dispatch = jnp.any(hits, axis=1).astype(jnp.bfloat16)
    send = jnp.einsum("tq,td->qd", dispatch, normed_moe, preferred_element_type=jnp.float32)
    send = send.astype(jnp.bfloat16).reshape(n_experts, quarter, width_model)
    received = lax.all_to_all(send, "req", split_axis=0, concat_axis=0, tiled=True)
    rows = received.reshape(-1, width_model)
    gate = jnp.dot(rows, gate_full, preferred_element_type=jnp.float32)
    up = jnp.dot(rows, up_full, preferred_element_type=jnp.float32)
    hidden = (jnp.maximum(gate, 0.0) * up).astype(jnp.bfloat16)
    part = jnp.dot(hidden, down_full, preferred_element_type=jnp.float32).astype(jnp.bfloat16)
    part = part.reshape(n_experts, quarter, width_model)
    back = lax.all_to_all(part, "req", split_axis=0, concat_axis=0, tiled=True)
    back = back.reshape(-1, width_model)
    combine = jnp.sum(jnp.where(hits, pick_weight[:, :, None], 0.0), axis=1)
    half_tok = tok // 2
    quarter_tok = tok // 4

    def mix_rows(first_row, count):
        weights = lax.dynamic_slice_in_dim(combine, first_row, count, 0)
        weights_hi = weights.astype(jnp.bfloat16)
        weights_lo = (weights - weights_hi.astype(jnp.float32)).astype(jnp.bfloat16)
        return jnp.dot(weights_hi, back, preferred_element_type=jnp.float32) + jnp.dot(
            weights_lo, back, preferred_element_type=jnp.float32
        )

    give_half = mix_rows((1 - core) * half_tok, half_tok)
    got_half = exp_flip(give_half, n_exp, 1)
    my_half = core * half_tok
    give_q = mix_rows(my_half + (1 - far_half) * quarter_tok, quarter_tok) + lax.dynamic_slice_in_dim(
        got_half, (1 - far_half) * quarter_tok, quarter_tok, 0
    )
    got_q = exp_flip(give_q, n_exp, 2)
    my_rows = my_half + far_half * quarter_tok
    keep_q = mix_rows(my_rows, quarter_tok) + lax.dynamic_slice_in_dim(
        got_half, far_half * quarter_tok, quarter_tok, 0
    )
    quarter_sum = keep_q + got_q
    resid_rows = lax.dynamic_slice_in_dim(resid, my_rows, quarter_tok, 0)
    out_q = (resid_rows.astype(jnp.float32) + quarter_sum).astype(jnp.bfloat16)
    other_q = exp_flip(out_q, n_exp, 2)
    out_half = jnp.zeros((half_tok, width_model), jnp.bfloat16)
    out_half = lax.dynamic_update_slice_in_dim(out_half, out_q, far_half * quarter_tok, 0)
    out_half = lax.dynamic_update_slice_in_dim(out_half, other_q, (1 - far_half) * quarter_tok, 0)
    other_half = exp_flip(out_half, n_exp, 1)
    out = jnp.zeros((tok, width_model), jnp.bfloat16)
    out = lax.dynamic_update_slice_in_dim(out, out_half, my_half, 0)
    return lax.dynamic_update_slice_in_dim(out, other_half, (1 - core) * half_tok, 0)


def solution(mesh):
    return jax.shard_map(
        body,
        mesh=mesh,
        in_specs=(
            P("req", None),
            P(),
            P(None, "exp"),
            P(),
            P("exp", None),
            P("req", None, None, None),
            P(),
            P(),
            P(),
            P(),
            P("req", None, "exp"),
            P("req", None, "exp"),
            P("req", "exp", None),
            P("req", None),
            P("req", None),
        ),
        out_specs=P("req", None),
        check_vma=False,
    )
```

```python
import jax
import jax.numpy as jnp
from jax import lax
from jax.sharding import PartitionSpec as P

QUERY_HEADS = 12
KEY_VALUE_HEADS = 2
HEAD_SIZE = 128
TOP = 4
GROUPS = 4
REQ_DEV = 2
LMIN = 64


EPS = 1e-06


def rms_scale(rows, gain):
    rows32 = rows.astype(jnp.float32)
    inverse = lax.rsqrt(jnp.mean(rows32 * rows32, axis=-1, keepdims=True) + EPS)
    return (rows32 * inverse * gain).astype(jnp.bfloat16)


def prefix_for(gathered, owners, group, per_group):
    prefix_segments = lax.dynamic_slice_in_dim(owners, group * per_group, per_group, 0)
    return gathered[prefix_segments].reshape(per_group * gathered.shape[1], 2, gathered.shape[3])


def req_shift_pairs(n_req, kind, d):
    pairs = []
    for r in range(n_req):
        if kind == "x":
            dest = (r // 4) * 4 + (r % 4 + d) % 4
        elif kind == "z":
            dest = r ^ 4
        else:
            dest = (r + 8 * d) % n_req
        pairs.append((r, dest))
    return pairs


def exp_flip(x, n_exp, bit):
    return lax.ppermute(x, "exp", [(e, e ^ bit) for e in range(n_exp)])


def gather_exp(x, axis, n_exp):
    far = exp_flip(x, n_exp, 2)
    near = exp_flip(jnp.concatenate([x, far], axis=axis), n_exp, 1)
    return jnp.concatenate([x, far, near], axis=axis)


def far_relay(x, n_req, n_exp):
    def index(r, e):
        return r * n_exp + e

    first = []
    second = []
    for r in range(n_req):
        for e in range(n_exp):
            if e % 2 == 0:
                first.append((index(r, e), index(r ^ 4, e)))
                second.append((index(r, e), index(r ^ 4, e ^ 2)))
            else:
                first.append((index(r, e), index(r ^ 4, e ^ 2)))
                second.append((index(r, e), index(r ^ 4, e)))
    hop = lax.ppermute(x, ("req", "exp"), first)
    return lax.ppermute(hop, ("req", "exp"), second)


def gather_exp_relay(x, axis, n_req, n_exp):
    far = far_relay(x, n_req, n_exp)
    near = exp_flip(jnp.concatenate([x, far], axis=axis), n_exp, 1)
    return jnp.concatenate([x, far, near], axis=axis)


def gather_prefix_near(mine, n_req):
    return jnp.stack([mine, lax.ppermute(mine, "req", req_shift_pairs(n_req, "z", 1))])


def gather_prefix_halves(along_z, n_req):
    along_x = jnp.stack(
        [along_z] + [lax.ppermute(along_z, "req", req_shift_pairs(n_req, "x", d)) for d in (1, 2, 3)]
    )
    along_y = jnp.stack(
        [along_x] + [lax.ppermute(along_x, "req", req_shift_pairs(n_req, "y", d)) for d in (1, 2, 3)]
    )
    return along_y.reshape((n_req,) + along_z.shape[1:])


def body(
    activations,
    attn_gain,
    w_query,
    key_value_weight,
    w_output,
    group_prefix_cache,
    lengths,
    groups,
    owners,
    moe_gain,
    w_gate,
    w_up,
    w_down,
    picks,
    pick_weight,
):
    req_index = lax.axis_index("req")
    expert_index = lax.axis_index("exp")
    n_req = lax.axis_size("req")
    n_exp = lax.axis_size("exp")
    tok = activations.shape[0]
    width_model = activations.shape[1]
    heads_per_shard = w_query.shape[1] // HEAD_SIZE
    key_value_head = expert_index * heads_per_shard // (QUERY_HEADS // KEY_VALUE_HEADS)

    own_piece = lax.dynamic_index_in_dim(group_prefix_cache, key_value_head, 2, keepdims=False)
    core = expert_index % 2
    far_half = expert_index // 2
    half_rows = own_piece.shape[0] // 2
    mine = lax.dynamic_slice_in_dim(own_piece, core * half_rows, half_rows, 0)
    along_z = gather_prefix_near(mine, n_req)
    ff_shard = w_gate.shape[2]
    packed = jnp.concatenate([w_gate[0].T, w_up[0].T, w_down[0]], axis=0)
    w_output_late, packed_late, along_z = lax.optimization_barrier((w_output, packed, along_z))
    halves_mine = gather_prefix_halves(along_z, n_req)
    halves_other = exp_flip(halves_mine, n_exp, 1)
    w_output_full = gather_exp_relay(w_output_late, 0, n_req, n_exp)
    packed_full = gather_exp_relay(packed_late.reshape(1, 3 * ff_shard, -1), 0, n_req, n_exp)
    gate_full = packed_full[:, :ff_shard].reshape(-1, packed.shape[1]).T
    up_full = packed_full[:, ff_shard : 2 * ff_shard].reshape(-1, packed.shape[1]).T
    down_full = packed_full[:, 2 * ff_shard :].reshape(-1, packed.shape[1])

    normalized_input = rms_scale(activations, attn_gain)
    query_rows = (
        jnp.dot(normalized_input, w_query, preferred_element_type=jnp.float32) * HEAD_SIZE ** (-0.5)
    ).astype(jnp.bfloat16)
    query_rows = query_rows.reshape(tok, heads_per_shard, HEAD_SIZE)
    kv_weight = lax.dynamic_slice_in_dim(key_value_weight, key_value_head * HEAD_SIZE, HEAD_SIZE, 2)
    local_key_value = jnp.einsum(
        "td,dcf->tcf", normalized_input, kv_weight, preferred_element_type=jnp.float32
    ).astype(jnp.bfloat16)

    pair = lax.dynamic_slice_in_dim(lengths, req_index * REQ_DEV, REQ_DEV, 0)
    pair_groups = lax.dynamic_slice_in_dim(groups, req_index * REQ_DEV, REQ_DEV, 0)
    per_group = n_req // GROUPS
    positions = jnp.arange(tok)
    in_first = positions < pair[0]
    my_y, my_z, my_x = req_index // 8, (req_index // 4) % 2, req_index % 4

    owner = jnp.stack(
        [lax.dynamic_slice_in_dim(owners, pair_groups[i] * per_group, per_group, 0) for i in range(2)]
    )
    where = ((my_y - owner // 8) % 4) * 8 + ((my_x - owner % 4) % 4) * 2 + (my_z - (owner // 4) % 2) % 2
    rows = jnp.concatenate([halves_mine[where], halves_other[where]], axis=2)
    rows = rows.reshape(2, per_group * 2 * half_rows, 2, HEAD_SIZE)
    prefix_a = rows[0]
    prefix_b = rows[1]
    zero_q = jnp.zeros_like(query_rows)
    first3 = in_first[:, None, None]
    query_ab = jnp.concatenate(
        [jnp.where(first3, query_rows, zero_q), jnp.where(first3, zero_q, query_rows)], axis=-1
    )
    keys_ab = jnp.concatenate([prefix_a[:, 0], prefix_b[:, 0]], axis=-1)
    values_ab = jnp.concatenate([prefix_a[:, 1], prefix_b[:, 1]], axis=-1)
    pre_scores = jnp.einsum("thd,pd->htp", query_ab, keys_ab, preferred_element_type=jnp.float32)
    suf_scores = jnp.einsum(
        "thd,sd->hts", query_rows, local_key_value[:, 0], preferred_element_type=jnp.float32
    )
    allowed = (positions[None, :] <= positions[:, None]) & (in_first[:, None] == in_first[None, :])
    suf_scores = jnp.where(allowed[None], suf_scores, -jnp.inf)
    top = jnp.maximum(
        jnp.max(pre_scores, axis=-1, keepdims=True), jnp.max(suf_scores, axis=-1, keepdims=True)
    )
    pre_exp = jnp.exp(pre_scores - top)
    suf_exp = jnp.exp(suf_scores - top)
    denom = jnp.sum(pre_exp, axis=-1, keepdims=True) + jnp.sum(suf_exp, axis=-1, keepdims=True)
    pre_w = (pre_exp / denom).astype(jnp.bfloat16)
    suf_w = (suf_exp / denom).astype(jnp.bfloat16)
    pre_ctx_ab = jnp.einsum("htp,pd->thd", pre_w, values_ab, preferred_element_type=jnp.float32)
    pre_ctx = jnp.where(first3, pre_ctx_ab[..., :HEAD_SIZE], pre_ctx_ab[..., HEAD_SIZE:])
    suf_ctx = jnp.einsum(
        "hts,sd->thd", suf_w, local_key_value[:, 1], preferred_element_type=jnp.float32
    )
    context = (pre_ctx + suf_ctx).astype(jnp.bfloat16)
    context = context.reshape(tok, heads_per_shard * HEAD_SIZE)
    context_full = gather_exp(context, 1, n_exp)
    attn = jnp.dot(context_full, w_output_full, preferred_element_type=jnp.float32)
    resid = (activations.astype(jnp.float32) + attn).astype(jnp.bfloat16)
    normed_moe = rms_scale(resid, moe_gain)

    n_experts = n_req
    cap = min(tok, 2 * tok * TOP // n_req)
    quarter = cap // n_exp
    expert_ids = jnp.arange(n_experts, dtype=jnp.int32)
    chose = jnp.any(picks[:, :, None] == expert_ids[None, None, :], axis=1).astype(jnp.bfloat16)
    earlier = (positions[None, :] < positions[:, None]).astype(jnp.bfloat16)
    before = jnp.dot(earlier, chose, preferred_element_type=jnp.float32).astype(jnp.int32)
    pick_hot = picks[:, :, None] == expert_ids[None, None, :]
    slot = jnp.sum(jnp.where(pick_hot, before[:, None, :], 0), axis=2)
    local = slot - expert_index * quarter
    keep = (local >= 0) & (local < quarter)
    target = jnp.where(keep, picks * quarter + local, -1)
    columns = jnp.arange(n_experts * quarter, dtype=jnp.int32)
    hits = target[:, :, None] == columns[None, None, :]
    dispatch = jnp.any(hits, axis=1).astype(jnp.bfloat16)
    send = jnp.einsum("tq,td->qd", dispatch, normed_moe, preferred_element_type=jnp.float32)
    send = send.astype(jnp.bfloat16).reshape(n_experts, quarter, width_model)
    received = lax.all_to_all(send, "req", split_axis=0, concat_axis=0, tiled=True)
    rows = received.reshape(-1, width_model)
    gate = jnp.dot(rows, gate_full, preferred_element_type=jnp.float32)
    up = jnp.dot(rows, up_full, preferred_element_type=jnp.float32)
    hidden = (jnp.maximum(gate, 0.0) * up).astype(jnp.bfloat16)
    part = jnp.dot(hidden, down_full, preferred_element_type=jnp.float32).astype(jnp.bfloat16)
    part = part.reshape(n_experts, quarter, width_model)
    back = lax.all_to_all(part, "req", split_axis=0, concat_axis=0, tiled=True)
    back = back.reshape(-1, width_model)
    combine = jnp.sum(jnp.where(hits, pick_weight[:, :, None], 0.0), axis=1)
    half_tok = tok // 2
    quarter_tok = tok // 4

    def mix_rows(first_row, count):
        weights = lax.dynamic_slice_in_dim(combine, first_row, count, 0)
        weights_hi = weights.astype(jnp.bfloat16)
        weights_lo = (weights - weights_hi.astype(jnp.float32)).astype(jnp.bfloat16)
        return jnp.dot(weights_hi, back, preferred_element_type=jnp.float32) + jnp.dot(
            weights_lo, back, preferred_element_type=jnp.float32
        )

    give_half = mix_rows((1 - core) * half_tok, half_tok)
    got_half = exp_flip(give_half, n_exp, 1)
    my_half = core * half_tok
    give_q = mix_rows(my_half + (1 - far_half) * quarter_tok, quarter_tok) + lax.dynamic_slice_in_dim(
        got_half, (1 - far_half) * quarter_tok, quarter_tok, 0
    )
    got_q = exp_flip(give_q, n_exp, 2)
    my_rows = my_half + far_half * quarter_tok
    keep_q = mix_rows(my_rows, quarter_tok) + lax.dynamic_slice_in_dim(
        got_half, far_half * quarter_tok, quarter_tok, 0
    )
    quarter_sum = keep_q + got_q
    resid_rows = lax.dynamic_slice_in_dim(resid, my_rows, quarter_tok, 0)
    out_q = (resid_rows.astype(jnp.float32) + quarter_sum).astype(jnp.bfloat16)
    other_q = exp_flip(out_q, n_exp, 2)
    out_half = jnp.zeros((half_tok, width_model), jnp.bfloat16)
    out_half = lax.dynamic_update_slice_in_dim(out_half, out_q, far_half * quarter_tok, 0)
    out_half = lax.dynamic_update_slice_in_dim(out_half, other_q, (1 - far_half) * quarter_tok, 0)
    other_half = exp_flip(out_half, n_exp, 1)
    out = jnp.zeros((tok, width_model), jnp.bfloat16)
    out = lax.dynamic_update_slice_in_dim(out, out_half, my_half, 0)
    return lax.dynamic_update_slice_in_dim(out, other_half, (1 - core) * half_tok, 0)


def solution(mesh):
    return jax.shard_map(
        body,
        mesh=mesh,
        in_specs=(
            P("req", None),
            P(),
            P(None, "exp"),
            P(),
            P("exp", None),
            P("req", None, None, None),
            P(),
            P(),
            P(),
            P(),
            P("req", None, "exp"),
            P("req", None, "exp"),
            P("req", "exp", None),
            P("req", None),
            P("req", None),
        ),
        out_specs=P("req", None),
        check_vma=False,
    )
```

```python
import jax
import jax.numpy as jnp
from jax import lax
from jax.sharding import PartitionSpec as P

QUERY_HEADS = 12
KEY_VALUE_HEADS = 2
HEAD_SIZE = 128
TOP = 4
GROUPS = 4
REQ_DEV = 2
LMIN = 64


EPS = 1e-06


def rms_scale(rows, gain):
    rows32 = rows.astype(jnp.float32)
    inverse = lax.rsqrt(jnp.mean(rows32 * rows32, axis=-1, keepdims=True) + EPS)
    return (rows32 * inverse * gain).astype(jnp.bfloat16)


def prefix_for(gathered, owners, group, per_group):
    prefix_segments = lax.dynamic_slice_in_dim(owners, group * per_group, per_group, 0)
    return gathered[prefix_segments].reshape(per_group * gathered.shape[1], 2, gathered.shape[3])


def req_shift_pairs(n_req, kind, d):
    pairs = []
    for r in range(n_req):
        if kind == "x":
            dest = (r // 4) * 4 + (r % 4 + d) % 4
        elif kind == "z":
            dest = r ^ 4
        else:
            dest = (r + 8 * d) % n_req
        pairs.append((r, dest))
    return pairs


def exp_flip(x, n_exp, bit):
    return lax.ppermute(x, "exp", [(e, e ^ bit) for e in range(n_exp)])


def gather_exp(x, axis, n_exp):
    far = exp_flip(x, n_exp, 2)
    near = exp_flip(jnp.concatenate([x, far], axis=axis), n_exp, 1)
    return jnp.concatenate([x, far, near], axis=axis)


def far_relay(x, n_req, n_exp):
    def index(r, e):
        return r * n_exp + e

    first = []
    second = []
    for r in range(n_req):
        for e in range(n_exp):
            if e % 2 == 0:
                first.append((index(r, e), index(r ^ 4, e)))
                second.append((index(r, e), index(r ^ 4, e ^ 2)))
            else:
                first.append((index(r, e), index(r ^ 4, e ^ 2)))
                second.append((index(r, e), index(r ^ 4, e)))
    hop = lax.ppermute(x, ("req", "exp"), first)
    return lax.ppermute(hop, ("req", "exp"), second)


def gather_exp_relay(x, axis, n_req, n_exp):
    far = far_relay(x, n_req, n_exp)
    near = exp_flip(jnp.concatenate([x, far], axis=axis), n_exp, 1)
    return jnp.concatenate([x, far, near], axis=axis)


def gather_prefix_near(mine, n_req):
    return jnp.stack([mine, lax.ppermute(mine, "req", req_shift_pairs(n_req, "z", 1))])


def gather_prefix_halves(along_z, n_req):
    along_x = jnp.stack(
        [along_z] + [lax.ppermute(along_z, "req", req_shift_pairs(n_req, "x", d)) for d in (1, 2, 3)]
    )
    along_y = jnp.stack(
        [along_x] + [lax.ppermute(along_x, "req", req_shift_pairs(n_req, "y", d)) for d in (1, 2, 3)]
    )
    return along_y.reshape((n_req,) + along_z.shape[1:])


def body(
    activations,
    attn_gain,
    w_query,
    key_value_weight,
    w_output,
    group_prefix_cache,
    lengths,
    groups,
    owners,
    moe_gain,
    w_gate,
    w_up,
    w_down,
    picks,
    pick_weight,
):
    req_index = lax.axis_index("req")
    expert_index = lax.axis_index("exp")
    n_req = lax.axis_size("req")
    n_exp = lax.axis_size("exp")
    tok = activations.shape[0]
    width_model = activations.shape[1]
    heads_per_shard = w_query.shape[1] // HEAD_SIZE
    key_value_head = expert_index * heads_per_shard // (QUERY_HEADS // KEY_VALUE_HEADS)

    own_piece = lax.dynamic_index_in_dim(group_prefix_cache, key_value_head, 2, keepdims=False)
    core = expert_index % 2
    far_half = expert_index // 2
    half_rows = own_piece.shape[0] // 2
    mine = lax.dynamic_slice_in_dim(own_piece, core * half_rows, half_rows, 0)
    along_z = gather_prefix_near(mine, n_req)
    ff_shard = w_gate.shape[2]
    packed = jnp.concatenate([w_gate[0].T, w_up[0].T, w_down[0]], axis=0)
    packed_late, along_z = lax.optimization_barrier((packed, along_z))
    w_output_late = w_output
    halves_mine = gather_prefix_halves(along_z, n_req)
    halves_other = exp_flip(halves_mine, n_exp, 1)
    w_output_full = gather_exp_relay(w_output_late, 0, n_req, n_exp)
    packed_full = gather_exp_relay(packed_late.reshape(1, 3 * ff_shard, -1), 0, n_req, n_exp)
    gate_full = packed_full[:, :ff_shard].reshape(-1, packed.shape[1]).T
    up_full = packed_full[:, ff_shard : 2 * ff_shard].reshape(-1, packed.shape[1]).T
    down_full = packed_full[:, 2 * ff_shard :].reshape(-1, packed.shape[1])

    normalized_input = rms_scale(activations, attn_gain)
    query_rows = (
        jnp.dot(normalized_input, w_query, preferred_element_type=jnp.float32) * HEAD_SIZE ** (-0.5)
    ).astype(jnp.bfloat16)
    query_rows = query_rows.reshape(tok, heads_per_shard, HEAD_SIZE)
    kv_weight = lax.dynamic_slice_in_dim(key_value_weight, key_value_head * HEAD_SIZE, HEAD_SIZE, 2)
    local_key_value = jnp.einsum(
        "td,dcf->tcf", normalized_input, kv_weight, preferred_element_type=jnp.float32
    ).astype(jnp.bfloat16)

    pair = lax.dynamic_slice_in_dim(lengths, req_index * REQ_DEV, REQ_DEV, 0)
    pair_groups = lax.dynamic_slice_in_dim(groups, req_index * REQ_DEV, REQ_DEV, 0)
    per_group = n_req // GROUPS
    positions = jnp.arange(tok)
    in_first = positions < pair[0]
    my_y, my_z, my_x = req_index // 8, (req_index // 4) % 2, req_index % 4

    def prefix_of(group):
        owner = lax.dynamic_slice_in_dim(owners, group * per_group, per_group, 0)
        where = ((my_y - owner // 8) % 4) * 8 + ((my_x - owner % 4) % 4) * 2 + (my_z - (owner // 4) % 2) % 2
        part_mine = halves_mine[where]
        part_other = halves_other[where]
        rows = jnp.concatenate([part_mine, part_other], axis=1)
        return rows.reshape(per_group * 2 * half_rows, 2, HEAD_SIZE)

    prefix_a = prefix_of(pair_groups[0])
    prefix_b = prefix_of(pair_groups[1])
    zero_q = jnp.zeros_like(query_rows)
    first3 = in_first[:, None, None]
    query_ab = jnp.concatenate(
        [jnp.where(first3, query_rows, zero_q), jnp.where(first3, zero_q, query_rows)], axis=-1
    )
    keys_ab = jnp.concatenate([prefix_a[:, 0], prefix_b[:, 0]], axis=-1)
    values_ab = jnp.concatenate([prefix_a[:, 1], prefix_b[:, 1]], axis=-1)
    pre_scores = jnp.einsum("thd,pd->htp", query_ab, keys_ab, preferred_element_type=jnp.float32)
    suf_scores = jnp.einsum(
        "thd,sd->hts", query_rows, local_key_value[:, 0], preferred_element_type=jnp.float32
    )
    allowed = (positions[None, :] <= positions[:, None]) & (in_first[:, None] == in_first[None, :])
    suf_scores = jnp.where(allowed[None], suf_scores, -jnp.inf)
    top = jnp.maximum(
        jnp.max(pre_scores, axis=-1, keepdims=True), jnp.max(suf_scores, axis=-1, keepdims=True)
    )
    pre_exp = jnp.exp(pre_scores - top)
    suf_exp = jnp.exp(suf_scores - top)
    denom = jnp.sum(pre_exp, axis=-1, keepdims=True) + jnp.sum(suf_exp, axis=-1, keepdims=True)
    pre_w = (pre_exp / denom).astype(jnp.bfloat16)
    suf_w = (suf_exp / denom).astype(jnp.bfloat16)
    pre_ctx_ab = jnp.einsum("htp,pd->thd", pre_w, values_ab, preferred_element_type=jnp.float32)
    pre_ctx = jnp.where(first3, pre_ctx_ab[..., :HEAD_SIZE], pre_ctx_ab[..., HEAD_SIZE:])
    suf_ctx = jnp.einsum(
        "hts,sd->thd", suf_w, local_key_value[:, 1], preferred_element_type=jnp.float32
    )
    context = (pre_ctx + suf_ctx).astype(jnp.bfloat16)
    context = context.reshape(tok, heads_per_shard * HEAD_SIZE)
    context_full = gather_exp(context, 1, n_exp)
    attn = jnp.dot(context_full, w_output_full, preferred_element_type=jnp.float32)
    resid = (activations.astype(jnp.float32) + attn).astype(jnp.bfloat16)
    normed_moe = rms_scale(resid, moe_gain)

    n_experts = n_req
    cap = min(tok, 2 * tok * TOP // n_req)
    quarter = cap // n_exp
    expert_ids = jnp.arange(n_experts, dtype=jnp.int32)
    chose = jnp.any(picks[:, :, None] == expert_ids[None, None, :], axis=1).astype(jnp.bfloat16)
    earlier = (positions[None, :] < positions[:, None]).astype(jnp.bfloat16)
    before = jnp.dot(earlier, chose, preferred_element_type=jnp.float32).astype(jnp.int32)
    pick_hot = picks[:, :, None] == expert_ids[None, None, :]
    slot = jnp.sum(jnp.where(pick_hot, before[:, None, :], 0), axis=2)
    local = slot - expert_index * quarter
    keep = (local >= 0) & (local < quarter)
    target = jnp.where(keep, picks * quarter + local, -1)
    columns = jnp.arange(n_experts * quarter, dtype=jnp.int32)
    hits = target[:, :, None] == columns[None, None, :]
    dispatch = jnp.any(hits, axis=1).astype(jnp.bfloat16)
    send = jnp.einsum("tq,td->qd", dispatch, normed_moe, preferred_element_type=jnp.float32)
    send = send.astype(jnp.bfloat16).reshape(n_experts, quarter, width_model)
    received = lax.all_to_all(send, "req", split_axis=0, concat_axis=0, tiled=True)
    rows = received.reshape(-1, width_model)
    gate = jnp.dot(rows, gate_full, preferred_element_type=jnp.float32)
    up = jnp.dot(rows, up_full, preferred_element_type=jnp.float32)
    hidden = (jnp.maximum(gate, 0.0) * up).astype(jnp.bfloat16)
    part = jnp.dot(hidden, down_full, preferred_element_type=jnp.float32).astype(jnp.bfloat16)
    part = part.reshape(n_experts, quarter, width_model)
    back = lax.all_to_all(part, "req", split_axis=0, concat_axis=0, tiled=True)
    back = back.reshape(-1, width_model)
    combine = jnp.sum(jnp.where(hits, pick_weight[:, :, None], 0.0), axis=1)
    half_tok = tok // 2
    quarter_tok = tok // 4

    def mix_rows(first_row, count):
        weights = lax.dynamic_slice_in_dim(combine, first_row, count, 0)
        weights_hi = weights.astype(jnp.bfloat16)
        weights_lo = (weights - weights_hi.astype(jnp.float32)).astype(jnp.bfloat16)
        return jnp.dot(weights_hi, back, preferred_element_type=jnp.float32) + jnp.dot(
            weights_lo, back, preferred_element_type=jnp.float32
        )

    give_half = mix_rows((1 - core) * half_tok, half_tok)
    got_half = exp_flip(give_half, n_exp, 1)
    my_half = core * half_tok
    give_q = mix_rows(my_half + (1 - far_half) * quarter_tok, quarter_tok) + lax.dynamic_slice_in_dim(
        got_half, (1 - far_half) * quarter_tok, quarter_tok, 0
    )
    got_q = exp_flip(give_q, n_exp, 2)
    my_rows = my_half + far_half * quarter_tok
    keep_q = mix_rows(my_rows, quarter_tok) + lax.dynamic_slice_in_dim(
        got_half, far_half * quarter_tok, quarter_tok, 0
    )
    quarter_sum = keep_q + got_q
    resid_rows = lax.dynamic_slice_in_dim(resid, my_rows, quarter_tok, 0)
    out_q = (resid_rows.astype(jnp.float32) + quarter_sum).astype(jnp.bfloat16)
    other_q = exp_flip(out_q, n_exp, 2)
    out_half = jnp.zeros((half_tok, width_model), jnp.bfloat16)
    out_half = lax.dynamic_update_slice_in_dim(out_half, out_q, far_half * quarter_tok, 0)
    out_half = lax.dynamic_update_slice_in_dim(out_half, other_q, (1 - far_half) * quarter_tok, 0)
    other_half = exp_flip(out_half, n_exp, 1)
    out = jnp.zeros((tok, width_model), jnp.bfloat16)
    out = lax.dynamic_update_slice_in_dim(out, out_half, my_half, 0)
    return lax.dynamic_update_slice_in_dim(out, other_half, (1 - core) * half_tok, 0)


def solution(mesh):
    return jax.shard_map(
        body,
        mesh=mesh,
        in_specs=(
            P("req", None),
            P(),
            P(None, "exp"),
            P(),
            P("exp", None),
            P("req", None, None, None),
            P(),
            P(),
            P(),
            P(),
            P("req", None, "exp"),
            P("req", None, "exp"),
            P("req", "exp", None),
            P("req", None),
            P("req", None),
        ),
        out_specs=P("req", None),
        check_vma=False,
    )
```

```python
import jax
import jax.numpy as jnp
from jax import lax
from jax.sharding import PartitionSpec as P

QUERY_HEADS = 12
KEY_VALUE_HEADS = 2
HEAD_SIZE = 128
TOP = 4
GROUPS = 4
REQ_DEV = 2
LMIN = 64


EPS = 1e-06


def rms_scale(rows, gain):
    rows32 = rows.astype(jnp.float32)
    inverse = lax.rsqrt(jnp.mean(rows32 * rows32, axis=-1, keepdims=True) + EPS)
    return (rows32 * inverse * gain).astype(jnp.bfloat16)


def prefix_for(gathered, owners, group, per_group):
    prefix_segments = lax.dynamic_slice_in_dim(owners, group * per_group, per_group, 0)
    return gathered[prefix_segments].reshape(per_group * gathered.shape[1], 2, gathered.shape[3])


def req_shift_pairs(n_req, kind, d):
    pairs = []
    for r in range(n_req):
        if kind == "x":
            dest = (r // 4) * 4 + (r % 4 + d) % 4
        elif kind == "z":
            dest = r ^ 4
        else:
            dest = (r + 8 * d) % n_req
        pairs.append((r, dest))
    return pairs


def exp_flip(x, n_exp, bit):
    return lax.ppermute(x, "exp", [(e, e ^ bit) for e in range(n_exp)])


def gather_exp(x, axis, n_exp):
    far = exp_flip(x, n_exp, 2)
    near = exp_flip(jnp.concatenate([x, far], axis=axis), n_exp, 1)
    return jnp.concatenate([x, far, near], axis=axis)


def far_relay(x, n_req, n_exp):
    def index(r, e):
        return r * n_exp + e

    first = []
    second = []
    for r in range(n_req):
        for e in range(n_exp):
            if e % 2 == 0:
                first.append((index(r, e), index(r ^ 4, e)))
                second.append((index(r, e), index(r ^ 4, e ^ 2)))
            else:
                first.append((index(r, e), index(r ^ 4, e ^ 2)))
                second.append((index(r, e), index(r ^ 4, e)))
    hop = lax.ppermute(x, ("req", "exp"), first)
    return lax.ppermute(hop, ("req", "exp"), second)


def gather_exp_relay(x, axis, n_req, n_exp):
    far = far_relay(x, n_req, n_exp)
    near = exp_flip(jnp.concatenate([x, far], axis=axis), n_exp, 1)
    return jnp.concatenate([x, far, near], axis=axis)


def gather_prefix_near(mine, n_req):
    return jnp.stack([mine, lax.ppermute(mine, "req", req_shift_pairs(n_req, "z", 1))])


def gather_prefix_halves(along_z, n_req):
    along_x = jnp.stack(
        [along_z] + [lax.ppermute(along_z, "req", req_shift_pairs(n_req, "x", d)) for d in (1, 2, 3)]
    )
    along_y = jnp.stack(
        [along_x] + [lax.ppermute(along_x, "req", req_shift_pairs(n_req, "y", d)) for d in (1, 2, 3)]
    )
    return along_y.reshape((n_req,) + along_z.shape[1:])


def body(
    activations,
    attn_gain,
    w_query,
    key_value_weight,
    w_output,
    group_prefix_cache,
    lengths,
    groups,
    owners,
    moe_gain,
    w_gate,
    w_up,
    w_down,
    picks,
    pick_weight,
):
    req_index = lax.axis_index("req")
    expert_index = lax.axis_index("exp")
    n_req = lax.axis_size("req")
    n_exp = lax.axis_size("exp")
    tok = activations.shape[0]
    width_model = activations.shape[1]
    heads_per_shard = w_query.shape[1] // HEAD_SIZE
    key_value_head = expert_index * heads_per_shard // (QUERY_HEADS // KEY_VALUE_HEADS)

    own_piece = lax.dynamic_index_in_dim(group_prefix_cache, key_value_head, 2, keepdims=False)
    core = expert_index % 2
    far_half = expert_index // 2
    half_rows = own_piece.shape[0] // 2
    mine = lax.dynamic_slice_in_dim(own_piece, core * half_rows, half_rows, 0)
    along_z = gather_prefix_near(mine, n_req)
    ff_shard = w_gate.shape[2]
    packed = jnp.concatenate([w_gate[0].T, w_up[0].T, w_down[0]], axis=0)
    packed_late = packed
    w_output_late = w_output
    halves_mine = gather_prefix_halves(along_z, n_req)
    halves_other = exp_flip(halves_mine, n_exp, 1)
    w_output_full = gather_exp_relay(w_output_late, 0, n_req, n_exp)
    packed_full = gather_exp_relay(packed_late.reshape(1, 3 * ff_shard, -1), 0, n_req, n_exp)
    gate_full = packed_full[:, :ff_shard].reshape(-1, packed.shape[1]).T
    up_full = packed_full[:, ff_shard : 2 * ff_shard].reshape(-1, packed.shape[1]).T
    down_full = packed_full[:, 2 * ff_shard :].reshape(-1, packed.shape[1])

    normalized_input = rms_scale(activations, attn_gain)
    query_rows = (
        jnp.dot(normalized_input, w_query, preferred_element_type=jnp.float32) * HEAD_SIZE ** (-0.5)
    ).astype(jnp.bfloat16)
    query_rows = query_rows.reshape(tok, heads_per_shard, HEAD_SIZE)
    kv_weight = lax.dynamic_slice_in_dim(key_value_weight, key_value_head * HEAD_SIZE, HEAD_SIZE, 2)
    local_key_value = jnp.einsum(
        "td,dcf->tcf", normalized_input, kv_weight, preferred_element_type=jnp.float32
    ).astype(jnp.bfloat16)

    pair = lax.dynamic_slice_in_dim(lengths, req_index * REQ_DEV, REQ_DEV, 0)
    pair_groups = lax.dynamic_slice_in_dim(groups, req_index * REQ_DEV, REQ_DEV, 0)
    per_group = n_req // GROUPS
    positions = jnp.arange(tok)
    in_first = positions < pair[0]
    my_y, my_z, my_x = req_index // 8, (req_index // 4) % 2, req_index % 4

    def prefix_of(group):
        owner = lax.dynamic_slice_in_dim(owners, group * per_group, per_group, 0)
        where = ((my_y - owner // 8) % 4) * 8 + ((my_x - owner % 4) % 4) * 2 + (my_z - (owner // 4) % 2) % 2
        part_mine = halves_mine[where]
        part_other = halves_other[where]
        rows = jnp.concatenate([part_mine, part_other], axis=1)
        return rows.reshape(per_group * 2 * half_rows, 2, HEAD_SIZE)

    prefix_a = prefix_of(pair_groups[0])
    prefix_b = prefix_of(pair_groups[1])
    zero_q = jnp.zeros_like(query_rows)
    first3 = in_first[:, None, None]
    query_ab = jnp.concatenate(
        [jnp.where(first3, query_rows, zero_q), jnp.where(first3, zero_q, query_rows)], axis=-1
    )
    keys_ab = jnp.concatenate([prefix_a[:, 0], prefix_b[:, 0]], axis=-1)
    values_ab = jnp.concatenate([prefix_a[:, 1], prefix_b[:, 1]], axis=-1)
    pre_scores = jnp.einsum("thd,pd->htp", query_ab, keys_ab, preferred_element_type=jnp.float32)
    suf_scores = jnp.einsum(
        "thd,sd->hts", query_rows, local_key_value[:, 0], preferred_element_type=jnp.float32
    )
    allowed = (positions[None, :] <= positions[:, None]) & (in_first[:, None] == in_first[None, :])
    suf_scores = jnp.where(allowed[None], suf_scores, -jnp.inf)
    top = jnp.maximum(
        jnp.max(pre_scores, axis=-1, keepdims=True), jnp.max(suf_scores, axis=-1, keepdims=True)
    )
    pre_exp = jnp.exp(pre_scores - top)
    suf_exp = jnp.exp(suf_scores - top)
    denom = jnp.sum(pre_exp, axis=-1, keepdims=True) + jnp.sum(suf_exp, axis=-1, keepdims=True)
    pre_w = (pre_exp / denom).astype(jnp.bfloat16)
    suf_w = (suf_exp / denom).astype(jnp.bfloat16)
    pre_ctx_ab = jnp.einsum("htp,pd->thd", pre_w, values_ab, preferred_element_type=jnp.float32)
    pre_ctx = jnp.where(first3, pre_ctx_ab[..., :HEAD_SIZE], pre_ctx_ab[..., HEAD_SIZE:])
    suf_ctx = jnp.einsum(
        "hts,sd->thd", suf_w, local_key_value[:, 1], preferred_element_type=jnp.float32
    )
    context = (pre_ctx + suf_ctx).astype(jnp.bfloat16)
    context = context.reshape(tok, heads_per_shard * HEAD_SIZE)
    context_full = gather_exp(context, 1, n_exp)
    attn = jnp.dot(context_full, w_output_full, preferred_element_type=jnp.float32)
    resid = (activations.astype(jnp.float32) + attn).astype(jnp.bfloat16)
    normed_moe = rms_scale(resid, moe_gain)

    n_experts = n_req
    cap = min(tok, 2 * tok * TOP // n_req)
    quarter = cap // n_exp
    expert_ids = jnp.arange(n_experts, dtype=jnp.int32)
    chose = jnp.any(picks[:, :, None] == expert_ids[None, None, :], axis=1).astype(jnp.bfloat16)
    earlier = (positions[None, :] < positions[:, None]).astype(jnp.bfloat16)
    before = jnp.dot(earlier, chose, preferred_element_type=jnp.float32).astype(jnp.int32)
    pick_hot = picks[:, :, None] == expert_ids[None, None, :]
    slot = jnp.sum(jnp.where(pick_hot, before[:, None, :], 0), axis=2)
    local = slot - expert_index * quarter
    keep = (local >= 0) & (local < quarter)
    target = jnp.where(keep, picks * quarter + local, -1)
    columns = jnp.arange(n_experts * quarter, dtype=jnp.int32)
    hits = target[:, :, None] == columns[None, None, :]
    dispatch = jnp.any(hits, axis=1).astype(jnp.bfloat16)
    send = jnp.einsum("tq,td->qd", dispatch, normed_moe, preferred_element_type=jnp.float32)
    send = send.astype(jnp.bfloat16).reshape(n_experts, quarter, width_model)
    received = lax.all_to_all(send, "req", split_axis=0, concat_axis=0, tiled=True)
    rows = received.reshape(-1, width_model)
    gate = jnp.dot(rows, gate_full, preferred_element_type=jnp.float32)
    up = jnp.dot(rows, up_full, preferred_element_type=jnp.float32)
    hidden = (jnp.maximum(gate, 0.0) * up).astype(jnp.bfloat16)
    part = jnp.dot(hidden, down_full, preferred_element_type=jnp.float32).astype(jnp.bfloat16)
    part = part.reshape(n_experts, quarter, width_model)
    back = lax.all_to_all(part, "req", split_axis=0, concat_axis=0, tiled=True)
    back = back.reshape(-1, width_model)
    combine = jnp.sum(jnp.where(hits, pick_weight[:, :, None], 0.0), axis=1)
    half_tok = tok // 2
    quarter_tok = tok // 4

    def mix_rows(first_row, count):
        weights = lax.dynamic_slice_in_dim(combine, first_row, count, 0)
        weights_hi = weights.astype(jnp.bfloat16)
        weights_lo = (weights - weights_hi.astype(jnp.float32)).astype(jnp.bfloat16)
        return jnp.dot(weights_hi, back, preferred_element_type=jnp.float32) + jnp.dot(
            weights_lo, back, preferred_element_type=jnp.float32
        )

    give_half = mix_rows((1 - core) * half_tok, half_tok)
    got_half = exp_flip(give_half, n_exp, 1)
    my_half = core * half_tok
    give_q = mix_rows(my_half + (1 - far_half) * quarter_tok, quarter_tok) + lax.dynamic_slice_in_dim(
        got_half, (1 - far_half) * quarter_tok, quarter_tok, 0
    )
    got_q = exp_flip(give_q, n_exp, 2)
    my_rows = my_half + far_half * quarter_tok
    keep_q = mix_rows(my_rows, quarter_tok) + lax.dynamic_slice_in_dim(
        got_half, far_half * quarter_tok, quarter_tok, 0
    )
    quarter_sum = keep_q + got_q
    resid_rows = lax.dynamic_slice_in_dim(resid, my_rows, quarter_tok, 0)
    out_q = (resid_rows.astype(jnp.float32) + quarter_sum).astype(jnp.bfloat16)
    other_q = exp_flip(out_q, n_exp, 2)
    out_half = jnp.zeros((half_tok, width_model), jnp.bfloat16)
    out_half = lax.dynamic_update_slice_in_dim(out_half, out_q, far_half * quarter_tok, 0)
    out_half = lax.dynamic_update_slice_in_dim(out_half, other_q, (1 - far_half) * quarter_tok, 0)
    other_half = exp_flip(out_half, n_exp, 1)
    out = jnp.zeros((tok, width_model), jnp.bfloat16)
    out = lax.dynamic_update_slice_in_dim(out, out_half, my_half, 0)
    return lax.dynamic_update_slice_in_dim(out, other_half, (1 - core) * half_tok, 0)


def solution(mesh):
    return jax.shard_map(
        body,
        mesh=mesh,
        in_specs=(
            P("req", None),
            P(),
            P(None, "exp"),
            P(),
            P("exp", None),
            P("req", None, None, None),
            P(),
            P(),
            P(),
            P(),
            P("req", None, "exp"),
            P("req", None, "exp"),
            P("req", "exp", None),
            P("req", None),
            P("req", None),
        ),
        out_specs=P("req", None),
        check_vma=False,
    )
```

```python
import jax
import jax.numpy as jnp
from jax import lax
from jax.sharding import PartitionSpec as P

QUERY_HEADS = 12
KEY_VALUE_HEADS = 2
HEAD_SIZE = 128
TOP = 4
GROUPS = 4
REQ_DEV = 2
LMIN = 64


EPS = 1e-06


def rms_scale(rows, gain):
    rows32 = rows.astype(jnp.float32)
    inverse = lax.rsqrt(jnp.mean(rows32 * rows32, axis=-1, keepdims=True) + EPS)
    return (rows32 * inverse * gain).astype(jnp.bfloat16)


def prefix_for(gathered, owners, group, per_group):
    prefix_segments = lax.dynamic_slice_in_dim(owners, group * per_group, per_group, 0)
    return gathered[prefix_segments].reshape(per_group * gathered.shape[1], 2, gathered.shape[3])


def req_shift_pairs(n_req, kind, d):
    pairs = []
    for r in range(n_req):
        if kind == "x":
            dest = (r // 4) * 4 + (r % 4 + d) % 4
        elif kind == "z":
            dest = r ^ 4
        else:
            dest = (r + 8 * d) % n_req
        pairs.append((r, dest))
    return pairs


def exp_flip(x, n_exp, bit):
    return lax.ppermute(x, "exp", [(e, e ^ bit) for e in range(n_exp)])


def gather_exp(x, axis, n_exp):
    far = exp_flip(x, n_exp, 2)
    near = exp_flip(jnp.concatenate([x, far], axis=axis), n_exp, 1)
    return jnp.concatenate([x, far, near], axis=axis)


def far_relay(x, n_req, n_exp):
    def index(r, e):
        return r * n_exp + e

    first = []
    second = []
    for r in range(n_req):
        for e in range(n_exp):
            if e % 2 == 0:
                first.append((index(r, e), index(r ^ 4, e)))
                second.append((index(r, e), index(r ^ 4, e ^ 2)))
            else:
                first.append((index(r, e), index(r ^ 4, e ^ 2)))
                second.append((index(r, e), index(r ^ 4, e)))
    hop = lax.ppermute(x, ("req", "exp"), first)
    return lax.ppermute(hop, ("req", "exp"), second)


def gather_exp_relay(x, axis, n_req, n_exp):
    far = far_relay(x, n_req, n_exp)
    near = exp_flip(jnp.concatenate([x, far], axis=axis), n_exp, 1)
    return jnp.concatenate([x, far, near], axis=axis)


def gather_prefix_near(mine, n_req):
    return jnp.stack([mine, lax.ppermute(mine, "req", req_shift_pairs(n_req, "z", 1))])


def gather_prefix_halves(along_z, n_req):
    along_x = jnp.stack(
        [along_z] + [lax.ppermute(along_z, "req", req_shift_pairs(n_req, "x", d)) for d in (1, 2, 3)]
    )
    along_y = jnp.stack(
        [along_x] + [lax.ppermute(along_x, "req", req_shift_pairs(n_req, "y", d)) for d in (1, 2, 3)]
    )
    return along_y.reshape((n_req,) + along_z.shape[1:])


def body(
    activations,
    attn_gain,
    w_query,
    key_value_weight,
    w_output,
    group_prefix_cache,
    lengths,
    groups,
    owners,
    moe_gain,
    w_gate,
    w_up,
    w_down,
    picks,
    pick_weight,
):
    req_index = lax.axis_index("req")
    expert_index = lax.axis_index("exp")
    n_req = lax.axis_size("req")
    n_exp = lax.axis_size("exp")
    tok = activations.shape[0]
    width_model = activations.shape[1]
    heads_per_shard = w_query.shape[1] // HEAD_SIZE
    key_value_head = expert_index * heads_per_shard // (QUERY_HEADS // KEY_VALUE_HEADS)

    own_piece = lax.dynamic_index_in_dim(group_prefix_cache, key_value_head, 2, keepdims=False)
    core = expert_index % 2
    far_half = expert_index // 2
    half_rows = own_piece.shape[0] // 2
    mine = lax.dynamic_slice_in_dim(own_piece, core * half_rows, half_rows, 0)
    along_z = gather_prefix_near(mine, n_req)
    ff_shard = w_gate.shape[2]
    packed = jnp.concatenate([w_gate[0].T, w_up[0].T, w_down[0]], axis=0)
    packed_late, along_z = lax.optimization_barrier((packed, along_z))
    w_output_late = w_output
    halves_mine = gather_prefix_halves(along_z, n_req)
    halves_other = exp_flip(halves_mine, n_exp, 1)
    w_output_full = gather_exp_relay(w_output_late, 0, n_req, n_exp)
    packed_full = gather_exp_relay(packed_late.reshape(1, 3 * ff_shard, -1), 0, n_req, n_exp)
    gate_full = packed_full[:, :ff_shard].reshape(-1, packed.shape[1]).T
    up_full = packed_full[:, ff_shard : 2 * ff_shard].reshape(-1, packed.shape[1]).T
    down_full = packed_full[:, 2 * ff_shard :].reshape(-1, packed.shape[1])

    normalized_input = rms_scale(activations, attn_gain)
    query_rows = (
        jnp.dot(normalized_input, w_query, preferred_element_type=jnp.float32) * HEAD_SIZE ** (-0.5)
    ).astype(jnp.bfloat16)
    query_rows = query_rows.reshape(tok, heads_per_shard, HEAD_SIZE)
    kv_weight = lax.dynamic_slice_in_dim(key_value_weight, key_value_head * HEAD_SIZE, HEAD_SIZE, 2)
    local_key_value = jnp.einsum(
        "td,dcf->tcf", normalized_input, kv_weight, preferred_element_type=jnp.float32
    ).astype(jnp.bfloat16)

    pair = lax.dynamic_slice_in_dim(lengths, req_index * REQ_DEV, REQ_DEV, 0)
    pair_groups = lax.dynamic_slice_in_dim(groups, req_index * REQ_DEV, REQ_DEV, 0)
    per_group = n_req // GROUPS
    positions = jnp.arange(tok)
    in_first = positions < pair[0]
    my_y, my_z, my_x = req_index // 8, (req_index // 4) % 2, req_index % 4

    def prefix_of(group):
        owner = lax.dynamic_slice_in_dim(owners, group * per_group, per_group, 0)
        where = ((my_y - owner // 8) % 4) * 8 + ((my_x - owner % 4) % 4) * 2 + (my_z - (owner // 4) % 2) % 2
        part_mine = halves_mine[where]
        part_other = halves_other[where]
        rows = jnp.concatenate([part_mine, part_other], axis=1)
        return rows.reshape(per_group * 2 * half_rows, 2, HEAD_SIZE)

    prefix_a = prefix_of(pair_groups[0])
    prefix_b = prefix_of(pair_groups[1])
    first3 = in_first[:, None, None]
    in_a = first3.astype(jnp.bfloat16)
    query_ab = jnp.concatenate([query_rows * in_a, query_rows * (1 - in_a)], axis=-1)
    keys_ab = jnp.concatenate([prefix_a[:, 0], prefix_b[:, 0]], axis=-1)
    values_ab = jnp.concatenate([prefix_a[:, 1], prefix_b[:, 1]], axis=-1)
    pre_scores = jnp.einsum("thd,pd->htp", query_ab, keys_ab, preferred_element_type=jnp.float32)
    suf_scores = jnp.einsum(
        "thd,sd->hts", query_rows, local_key_value[:, 0], preferred_element_type=jnp.float32
    )
    allowed = (positions[None, :] <= positions[:, None]) & (in_first[:, None] == in_first[None, :])
    suf_scores = jnp.where(allowed[None], suf_scores, -jnp.inf)
    top = jnp.maximum(
        jnp.max(pre_scores, axis=-1, keepdims=True), jnp.max(suf_scores, axis=-1, keepdims=True)
    )
    pre_exp = jnp.exp(pre_scores - top)
    suf_exp = jnp.exp(suf_scores - top)
    denom = jnp.sum(pre_exp, axis=-1, keepdims=True) + jnp.sum(suf_exp, axis=-1, keepdims=True)
    pre_w = (pre_exp / denom).astype(jnp.bfloat16)
    suf_w = (suf_exp / denom).astype(jnp.bfloat16)
    pre_ctx_ab = jnp.einsum("htp,pd->thd", pre_w, values_ab, preferred_element_type=jnp.float32)
    pre_ctx = jnp.where(first3, pre_ctx_ab[..., :HEAD_SIZE], pre_ctx_ab[..., HEAD_SIZE:])
    suf_ctx = jnp.einsum(
        "hts,sd->thd", suf_w, local_key_value[:, 1], preferred_element_type=jnp.float32
    )
    context = (pre_ctx + suf_ctx).astype(jnp.bfloat16)
    context = context.reshape(tok, heads_per_shard * HEAD_SIZE)
    context_full = gather_exp(context, 1, n_exp)
    attn = jnp.dot(context_full, w_output_full, preferred_element_type=jnp.float32)
    resid = (activations.astype(jnp.float32) + attn).astype(jnp.bfloat16)
    normed_moe = rms_scale(resid, moe_gain)

    n_experts = n_req
    cap = min(tok, 2 * tok * TOP // n_req)
    quarter = cap // n_exp
    expert_ids = jnp.arange(n_experts, dtype=jnp.int32)
    chose = jnp.any(picks[:, :, None] == expert_ids[None, None, :], axis=1).astype(jnp.bfloat16)
    earlier = (positions[None, :] < positions[:, None]).astype(jnp.bfloat16)
    before = jnp.dot(earlier, chose, preferred_element_type=jnp.float32).astype(jnp.int32)
    pick_hot = picks[:, :, None] == expert_ids[None, None, :]
    slot = jnp.sum(jnp.where(pick_hot, before[:, None, :], 0), axis=2)
    local = slot - expert_index * quarter
    keep = (local >= 0) & (local < quarter)
    target = jnp.where(keep, picks * quarter + local, -1)
    columns = jnp.arange(n_experts * quarter, dtype=jnp.int32)
    hits = target[:, :, None] == columns[None, None, :]
    dispatch = jnp.any(hits, axis=1).astype(jnp.bfloat16)
    send = jnp.einsum("tq,td->qd", dispatch, normed_moe, preferred_element_type=jnp.float32)
    send = send.astype(jnp.bfloat16).reshape(n_experts, quarter, width_model)
    received = lax.all_to_all(send, "req", split_axis=0, concat_axis=0, tiled=True)
    rows = received.reshape(-1, width_model)
    gate = jnp.dot(rows, gate_full, preferred_element_type=jnp.float32)
    up = jnp.dot(rows, up_full, preferred_element_type=jnp.float32)
    hidden = (jnp.maximum(gate, 0.0) * up).astype(jnp.bfloat16)
    part = jnp.dot(hidden, down_full, preferred_element_type=jnp.float32).astype(jnp.bfloat16)
    part = part.reshape(n_experts, quarter, width_model)
    back = lax.all_to_all(part, "req", split_axis=0, concat_axis=0, tiled=True)
    back = back.reshape(-1, width_model)
    combine = jnp.sum(jnp.where(hits, pick_weight[:, :, None], 0.0), axis=1)
    half_tok = tok // 2
    quarter_tok = tok // 4

    def mix_rows(first_row, count):
        weights = lax.dynamic_slice_in_dim(combine, first_row, count, 0)
        weights_hi = weights.astype(jnp.bfloat16)
        weights_lo = (weights - weights_hi.astype(jnp.float32)).astype(jnp.bfloat16)
        return jnp.dot(weights_hi, back, preferred_element_type=jnp.float32) + jnp.dot(
            weights_lo, back, preferred_element_type=jnp.float32
        )

    give_half = mix_rows((1 - core) * half_tok, half_tok)
    got_half = exp_flip(give_half, n_exp, 1)
    my_half = core * half_tok
    give_q = mix_rows(my_half + (1 - far_half) * quarter_tok, quarter_tok) + lax.dynamic_slice_in_dim(
        got_half, (1 - far_half) * quarter_tok, quarter_tok, 0
    )
    got_q = exp_flip(give_q, n_exp, 2)
    my_rows = my_half + far_half * quarter_tok
    keep_q = mix_rows(my_rows, quarter_tok) + lax.dynamic_slice_in_dim(
        got_half, far_half * quarter_tok, quarter_tok, 0
    )
    quarter_sum = keep_q + got_q
    resid_rows = lax.dynamic_slice_in_dim(resid, my_rows, quarter_tok, 0)
    out_q = (resid_rows.astype(jnp.float32) + quarter_sum).astype(jnp.bfloat16)
    other_q = exp_flip(out_q, n_exp, 2)
    out_half = jnp.zeros((half_tok, width_model), jnp.bfloat16)
    out_half = lax.dynamic_update_slice_in_dim(out_half, out_q, far_half * quarter_tok, 0)
    out_half = lax.dynamic_update_slice_in_dim(out_half, other_q, (1 - far_half) * quarter_tok, 0)
    other_half = exp_flip(out_half, n_exp, 1)
    out = jnp.zeros((tok, width_model), jnp.bfloat16)
    out = lax.dynamic_update_slice_in_dim(out, out_half, my_half, 0)
    return lax.dynamic_update_slice_in_dim(out, other_half, (1 - core) * half_tok, 0)


def solution(mesh):
    return jax.shard_map(
        body,
        mesh=mesh,
        in_specs=(
            P("req", None),
            P(),
            P(None, "exp"),
            P(),
            P("exp", None),
            P("req", None, None, None),
            P(),
            P(),
            P(),
            P(),
            P("req", None, "exp"),
            P("req", None, "exp"),
            P("req", "exp", None),
            P("req", None),
            P("req", None),
        ),
        out_specs=P("req", None),
        check_vma=False,
    )
```
